128 devices in a mesh: az: 16 (over z, y), rg: 8 (over x, core).
Axes of the slice: x: 4, y: 4, z: 4, core: 2. Of those that a mesh axis runs over, the one named last changes fastest.
Arguments:
- master_phasor_raster: bfloat16 [2, 2560, 10240], P(None, ('az', 'rg')), may hold values from -6 to 6
- slave_phasor_raster: bfloat16 [2, 2560, 10240], P(None, ('az', 'rg')), may hold values from -6 to 6
- segment_track_trim: int32 [16, 2], replicated, may hold values from 0 to 16
- segment_slant_trim: int32 [16, 2], replicated, may hold values from 0 to 96
Outputs:
- phase: float32 [512, 2048], P('az', 'rg')
- weight: float32 [512, 2048], P('az', 'rg')
The draws below stay inside these ranges and needn't reach their ends.
Inputs may be any that keep to these rules, and one draw needn't show every extreme that they name: segment_track_trim rows hold invalid line counts at the start and end of each burst. segment_slant_trim rows hold invalid column counts at the near and far range edge of each burst.
All inputs are finite; a program needn't handle non-finite values.
Results may differ from the reference program's by a relative error of at most 0.0003.
Values may be sent and summed in bfloat16 or wider, within the bound.
No kernel may reach another device: no remote copies, remote signals or barrier semaphores. Data moves between devices by JAX's collectives and lax.ppermute only.
A program may use at most 128 MiB of HBM per device.

```python
from functools import partial
import jax
import jax.numpy as jnp
from jax import lax

LOOK = 5
LEVELS = 6
ITERS = 3
SWEEPS = 4
SEGMENT_HEIGHT = 160
SWATH_SEGMENTS = 16
LINES = 2560
RANGE = 10240
COARSE_HEIGHT = 512
COARSE_WIDTH = 2048


def with_ends(drawn, own_key, smallest, high):
    spot = [jax.random.randint(jax.random.fold_in(own_key, axis), (), 0, length) for axis, length in enumerate(drawn.shape)]
    longest = drawn.shape.index(max(drawn.shape))
    beside = spot[:longest] + [(spot[longest] + 1) % drawn.shape[longest]] + spot[longest + 1:]
    return drawn.at[tuple(spot)].set(smallest).at[tuple(beside)].set(high)


def level_of(rng, extent, split, smallest, largest):
    level, own = 1.0, jax.random.fold_in(rng, 6)
    for dim, blocks in split:
        heights = jnp.exp(jax.random.uniform(jax.random.fold_in(own, dim), (blocks,), jnp.float32, smallest / len(split), largest / len(split)))
        level = level * jnp.repeat(heights, extent[dim] // blocks).reshape([-1 if axis == dim else 1 for axis in range(len(extent))])
    return level


def scatter_about(key, dims, spread, most, shards=(), held_as=jnp.bfloat16):
    entries = jax.random.normal(key, dims, jnp.float32) * spread
    if len(shards) > 0:
        entries = level_of(key, dims, shards, -0.22, 0.18) * entries
    return jnp.clip(entries, min=-most, max=most).astype(held_as)


def setup_inputs(seed: int = 0) -> dict:
    key_of = jax.random.split(jax.random.key(seed), 5)
    return {
        "master_phasor_raster": scatter_about(key_of[0], (2, LINES, RANGE), 1.0, 6.0, ((1, 128),)),
        "slave_phasor_raster": scatter_about(key_of[1], (2, LINES, RANGE), 1.0, 6.0, ((1, 128),)),
        "segment_track_trim": with_ends(jax.random.randint(key_of[2], (SWATH_SEGMENTS, 2), 0, 17), jax.random.fold_in(key_of[2], 1), 0, 16).astype(jnp.int32),
        "segment_slant_trim": with_ends(jax.random.randint(key_of[3], (SWATH_SEGMENTS, 2), 0, 97), jax.random.fold_in(key_of[3], 1), 0, 96).astype(jnp.int32),
    }


OMEGA = 0.6
MU = 0.01


def mean_multilook(leading_phasor_raster, trailing_phasor_raster, along_track_position, column_index, track_trim_width, slant_trim_width, slant_sample_total):
    usable_stripes = (along_track_position >= track_trim_width[0]) & (along_track_position < SEGMENT_HEIGHT - track_trim_width[1])
    cols_ok = (column_index >= slant_trim_width[0]) & (column_index < slant_sample_total - slant_trim_width[1])
    valid_mask = (usable_stripes[:, None] & cols_ok[None, :]).astype(jnp.float32)
    first_re = leading_phasor_raster[0].astype(jnp.float32) * valid_mask
    first_im = leading_phasor_raster[1].astype(jnp.float32) * valid_mask
    second_re = trailing_phasor_raster[0].astype(jnp.float32) * valid_mask
    second_im = trailing_phasor_raster[1].astype(jnp.float32) * valid_mask
    products = jnp.stack([first_re * second_re + first_im * second_im,
                          first_im * second_re - first_re * second_im,
                          first_re * first_re + first_im * first_im,
                          second_re * second_re + second_im * second_im])
    height_rows, width_cols = valid_mask.shape
    return products.reshape(4, height_rows // LOOK, LOOK, width_cols // LOOK, LOOK).sum(axis=(2, 4))


def edge_terms(left_re, left_im, left_weight, right_re, right_im, right_weight):
    edge_weight = 0.5 * (left_weight + right_weight)
    cross_im = right_im * left_re - right_re * left_im
    power_sum = left_re * left_re + left_im * left_im + right_re * right_re + right_im * right_im + 1.0
    return edge_weight, 2.0 * cross_im / power_sum


def apply_padded(vector, operators):
    east, west, south, north, diagonal = operators
    padded = jnp.pad(vector, 1)
    return (diagonal * vector - east * padded[1:-1, 2:] - west * padded[1:-1, :-2]
            - south * padded[2:, 1:-1] - north * padded[:-2, 1:-1])


def restrict_sum(vector):
    rows_now, cols_now = vector.shape
    return vector.reshape(rows_now // 2, 2, cols_now // 2, 2).sum(axis=(1, 3))


def prolong_copy(vector):
    rows_now, cols_now = vector.shape
    return jnp.broadcast_to(vector[:, None, :, None], (rows_now, 2, cols_now, 2)).reshape(rows_now * 2, cols_now * 2)


def build_levels(east, west, south, north):
    levels = []
    for level in range(LEVELS):
        diagonal = east + west + south + north + MU * 4.0 ** level
        levels.append((east, west, south, north, diagonal))
        if level + 1 < LEVELS:
            east, west, south, north = (east[0::2, 1::2] + east[1::2, 1::2],
                                        west[0::2, 0::2] + west[1::2, 0::2],
                                        south[1::2, 0::2] + south[1::2, 1::2],
                                        north[0::2, 0::2] + north[0::2, 1::2])
    return levels


def jacobi_sweeps(rhs_vec, operators, apply_fn):
    estimate = OMEGA * rhs_vec / operators[4]
    for sweep_index in range(SWEEPS - 1):
        estimate = estimate + OMEGA * (rhs_vec - apply_fn(estimate, operators)) / operators[4]
    return estimate


def vcycle(rhs_vec, level, levels, apply_fn, coarse_fn):
    diagonal = levels[level][4]
    if level == LEVELS - 1:
        return coarse_fn(rhs_vec, levels[level])
    estimate = OMEGA * rhs_vec / diagonal
    remain = rhs_vec - apply_fn(estimate, levels[level])
    correction = vcycle(restrict_sum(remain), level + 1, levels, apply_fn, coarse_fn)
    estimate = estimate + prolong_copy(correction)
    return estimate + OMEGA * (rhs_vec - apply_fn(estimate, levels[level])) / diagonal


def reference(master_phasor_raster, slave_phasor_raster, segment_track_trim, segment_slant_trim):
    slant_sample_total = master_phasor_raster.shape[2]

    def segment_pixel_totals(segment_ordinal):
        leading_phasor_raster = lax.dynamic_slice_in_dim(master_phasor_raster, segment_ordinal * SEGMENT_HEIGHT, SEGMENT_HEIGHT, 1)
        trailing_phasor_raster = lax.dynamic_slice_in_dim(slave_phasor_raster, segment_ordinal * SEGMENT_HEIGHT, SEGMENT_HEIGHT, 1)
        return mean_multilook(leading_phasor_raster, trailing_phasor_raster, jnp.arange(SEGMENT_HEIGHT, dtype=jnp.int32),
                         jnp.arange(slant_sample_total, dtype=jnp.int32), segment_track_trim[segment_ordinal],
                         segment_slant_trim[segment_ordinal], slant_sample_total)

    segment_pile = lax.map(segment_pixel_totals, jnp.arange(SWATH_SEGMENTS, dtype=jnp.int32))
    pixel_totals = jnp.transpose(segment_pile, (1, 0, 2, 3)).reshape(4, COARSE_HEIGHT, COARSE_WIDTH)
    look_re, look_im, power_one, power_two = pixel_totals[0], pixel_totals[1], pixel_totals[2], pixel_totals[3]
    weight = 0.05 + 4.0 * (look_re * look_re + look_im * look_im) / jnp.maximum(power_one * power_two, 1.0)

    edge_h, grad_h = edge_terms(look_re[:, :-1], look_im[:, :-1], weight[:, :-1],
                                look_re[:, 1:], look_im[:, 1:], weight[:, 1:])
    edge_v, grad_v = edge_terms(look_re[:-1, :], look_im[:-1, :], weight[:-1, :],
                                look_re[1:, :], look_im[1:, :], weight[1:, :])
    east = jnp.pad(edge_h, ((0, 0), (0, 1)))
    west = jnp.pad(edge_h, ((0, 0), (1, 0)))
    south = jnp.pad(edge_v, ((0, 1), (0, 0)))
    north = jnp.pad(edge_v, ((1, 0), (0, 0)))
    flux_h = edge_h * grad_h
    flux_v = edge_v * grad_v
    rhs = -(jnp.pad(flux_h, ((0, 0), (0, 1))) - jnp.pad(flux_h, ((0, 0), (1, 0)))
            + jnp.pad(flux_v, ((0, 1), (0, 0))) - jnp.pad(flux_v, ((1, 0), (0, 0))))

    levels = build_levels(east, west, south, north)
    coarse_fn = partial(jacobi_sweeps, apply_fn=apply_padded)

    def precondition(vector):
        return vcycle(vector, 0, levels, apply_padded, coarse_fn)

    solution = jnp.zeros_like(rhs)
    residual = rhs
    precond = precondition(residual)
    direction = precond
    norm_now = jnp.sum(residual * precond)
    for step_index in range(ITERS):
        image_vec = apply_padded(direction, levels[0])
        step_length = norm_now / jnp.sum(direction * image_vec)
        solution = solution + step_length * direction
        residual = residual - step_length * image_vec
        if step_index + 1 < ITERS:
            precond = precondition(residual)
            norm_next = jnp.sum(residual * precond)
            direction = precond + (norm_next / norm_now) * direction
            norm_now = norm_next
    return solution, weight
```

```python
import jax
import jax.numpy as jnp
from jax import lax
from jax.sharding import PartitionSpec as P

LOOK = 5
LEVELS = 6
ITERS = 3
SWEEPS = 4
SEGMENT_HEIGHT = 160
GATHER_LEVEL = 2


OMEGA = 0.6
MU = 0.01


def neighbours(v):
    n_az = lax.axis_size("az")
    n_rg = lax.axis_size("rg")
    above = lax.ppermute(v[..., -1:, :], "az", [(i, i + 1) for i in range(n_az - 1)])
    below = lax.ppermute(v[..., :1, :], "az", [(i + 1, i) for i in range(n_az - 1)])
    left = lax.ppermute(v[..., :, -1:], "rg", [(i, i + 1) for i in range(n_rg - 1)])
    right = lax.ppermute(v[..., :, :1], "rg", [(i + 1, i) for i in range(n_rg - 1)])
    north = jnp.concatenate([above, v[..., :-1, :]], axis=-2)
    south = jnp.concatenate([v[..., 1:, :], below], axis=-2)
    west = jnp.concatenate([left, v[..., :, :-1]], axis=-1)
    east = jnp.concatenate([v[..., :, 1:], right], axis=-1)
    return north, south, west, east


def apply_halo(vector, operators):
    east, west, south, north, diagonal = operators
    v_n, v_s, v_w, v_e = neighbours(vector)
    return diagonal * vector - east * v_e - west * v_w - south * v_s - north * v_n


def apply_padded(vector, operators):
    east, west, south, north, diagonal = operators
    padded = jnp.pad(vector, 1)
    return (diagonal * vector - east * padded[1:-1, 2:] - west * padded[1:-1, :-2]
            - south * padded[2:, 1:-1] - north * padded[:-2, 1:-1])


def mean_multilook(leading, trailing, row_ok, col_ok):
    valid_mask = (row_ok[:, None] & col_ok[None, :]).astype(jnp.float32)
    first_re = leading[0].astype(jnp.float32) * valid_mask
    first_im = leading[1].astype(jnp.float32) * valid_mask
    second_re = trailing[0].astype(jnp.float32) * valid_mask
    second_im = trailing[1].astype(jnp.float32) * valid_mask
    products = jnp.stack(
        [
            first_re * second_re + first_im * second_im,
            first_im * second_re - first_re * second_im,
            first_re * first_re + first_im * first_im,
            second_re * second_re + second_im * second_im,
        ]
    )
    height_rows, width_cols = valid_mask.shape
    rows = products.reshape(4, height_rows // LOOK, LOOK, width_cols).sum(axis=2)
    return rows.reshape(4, height_rows // LOOK, width_cols // LOOK, LOOK).sum(axis=3)


def edge_terms(left_re, left_im, left_weight, right_re, right_im, right_weight):
    edge_weight = 0.5 * (left_weight + right_weight)
    cross_im = right_im * left_re - right_re * left_im
    power_sum = (
        left_re * left_re + left_im * left_im + right_re * right_re + right_im * right_im + 1.0
    )
    return (edge_weight, 2.0 * cross_im / power_sum)


def restrict_sum(vector):
    rows_now, cols_now = vector.shape
    return vector.reshape(rows_now // 2, 2, cols_now // 2, 2).sum(axis=(1, 3))


def prolong_copy(vector):
    rows_now, cols_now = vector.shape
    return jnp.broadcast_to(vector[:, None, :, None], (rows_now, 2, cols_now, 2)).reshape(
        rows_now * 2, cols_now * 2
    )


def coarsen(east, west, south, north):
    return (
        east[0::2, 1::2] + east[1::2, 1::2],
        west[0::2, 0::2] + west[1::2, 0::2],
        south[1::2, 0::2] + south[1::2, 1::2],
        north[0::2, 0::2] + north[0::2, 1::2],
    )


def build_levels(east, west, south, north, first_level, last_level):
    levels = {}
    for level in range(first_level, last_level):
        diagonal = east + west + south + north + MU * 4.0**level
        levels[level] = (east, west, south, north, diagonal)
        if level + 1 < LEVELS:
            east, west, south, north = coarsen(east, west, south, north)
    return levels, (east, west, south, north)


def jacobi_sweeps(rhs_vec, operators, apply_fn):
    estimate = OMEGA * rhs_vec / operators[4]
    for sweep_index in range(SWEEPS - 1):
        estimate = estimate + OMEGA * (rhs_vec - apply_fn(estimate, operators)) / operators[4]
    return estimate


def vcycle(rhs_vec, level, levels, apply_fn, stop_fn):
    if level == LEVELS - 1:
        return jacobi_sweeps(rhs_vec, levels[level], apply_fn)
    if stop_fn is not None and level == GATHER_LEVEL:
        return stop_fn(rhs_vec)
    diagonal = levels[level][4]
    estimate = OMEGA * rhs_vec / diagonal
    remain = rhs_vec - apply_fn(estimate, levels[level])
    correction = vcycle(restrict_sum(remain), level + 1, levels, apply_fn, stop_fn)
    estimate = estimate + prolong_copy(correction)
    return estimate + OMEGA * (rhs_vec - apply_fn(estimate, levels[level])) / diagonal


def everyone():
    return lax.axis_size("az") * lax.axis_size("rg")


def gather_grid(blocks):
    n_az = lax.axis_size("az")
    n_rg = lax.axis_size("rg")
    count, h, w = blocks.shape
    sent = jnp.broadcast_to(blocks[None], (n_az * n_rg, count, h, w))
    got = lax.all_to_all(sent, ("az", "rg"), 0, 0, tiled=True)
    got = got.reshape(n_az, n_rg, count, h, w).transpose(2, 0, 3, 1, 4)
    return got.reshape(count, n_az * h, n_rg * w)


def total(values):
    n = everyone()
    sent = jnp.broadcast_to(values[None], (n, values.shape[0]))
    got = lax.all_to_all(sent, ("az", "rg"), 0, 0, tiled=True)
    return jnp.sum(got, axis=0)


def local(master_phasor_raster, slave_phasor_raster, segment_track_trim, segment_slant_trim):
    n_az = lax.axis_size("az")
    n_range = lax.axis_size("rg")
    segment_ordinal = lax.axis_index("az")
    range_index = lax.axis_index("rg")
    track_trim_width = lax.dynamic_index_in_dim(
        segment_track_trim, segment_ordinal, 0, keepdims=False
    )
    slant_trim_width = lax.dynamic_index_in_dim(
        segment_slant_trim, segment_ordinal, 0, keepdims=False
    )
    lines_here = master_phasor_raster.shape[1]
    slant_sample_total = master_phasor_raster.shape[2]
    along_track_position = range_index * lines_here + jnp.arange(lines_here, dtype=jnp.int32)
    column_index = jnp.arange(slant_sample_total, dtype=jnp.int32)
    row_ok = (along_track_position >= track_trim_width[0]) & (
        along_track_position < SEGMENT_HEIGHT - track_trim_width[1]
    )
    col_ok = (column_index >= slant_trim_width[0]) & (
        column_index < slant_sample_total - slant_trim_width[1]
    )
    pixel_totals = mean_multilook(master_phasor_raster, slave_phasor_raster, row_ok, col_ok)
    look_re, look_im, power_one, power_two = (
        pixel_totals[0],
        pixel_totals[1],
        pixel_totals[2],
        pixel_totals[3],
    )
    weight = 0.05 + 4.0 * (look_re * look_re + look_im * look_im) / jnp.maximum(
        power_one * power_two, 1.0
    )
    fields = jnp.stack([look_re, look_im, weight])
    n_fields, rows_here, cols_all = fields.shape
    cols_here = cols_all // n_range
    fields = fields.reshape(n_fields, rows_here, n_range, cols_here).transpose(2, 0, 1, 3)
    fields = lax.all_to_all(fields, "rg", 0, 0, tiled=True)
    fields = fields.transpose(1, 0, 2, 3).reshape(n_fields, n_range * rows_here, cols_here)
    weight = fields[2]
    shard_height_total = n_range * rows_here

    f_n, f_s, f_w, f_e = neighbours(fields)
    edge_h, grad_h = edge_terms(fields[0], fields[1], fields[2], f_e[0], f_e[1], f_e[2])
    col_global = range_index * cols_here + jnp.arange(cols_here, dtype=jnp.int32)
    keep_h = (col_global <= cols_here * n_range - 2).astype(jnp.float32)
    edge_h = edge_h * keep_h[None, :]
    edge_v, grad_v = edge_terms(fields[0], fields[1], fields[2], f_s[0], f_s[1], f_s[2])
    row_global = segment_ordinal * shard_height_total + jnp.arange(shard_height_total, dtype=jnp.int32)
    keep_v = (row_global <= shard_height_total * n_az - 2).astype(jnp.float32)
    edge_v = edge_v * keep_v[:, None]
    flux_h = edge_h * grad_h
    flux_v = edge_v * grad_v
    e_n, _, e_w, _ = neighbours(jnp.stack([edge_h, flux_h, edge_v, flux_v]))
    west_edge, flux_w, north_edge, flux_n = e_w[0], e_w[1], e_n[2], e_n[3]
    rhs = -(flux_h - flux_w + flux_v - flux_n)

    levels, coarse_edges = build_levels(edge_h, west_edge, south=edge_v, north=north_edge,
                                        first_level=0, last_level=GATHER_LEVEL)
    whole_edges = gather_grid(jnp.stack(coarse_edges))
    whole_levels, _ = build_levels(whole_edges[0], whole_edges[1], whole_edges[2], whole_edges[3],
                                   GATHER_LEVEL, LEVELS)
    block_h, block_w = coarse_edges[0].shape

    def coarse_solve(rhs_vec):
        whole_rhs = gather_grid(rhs_vec[None])[0]
        whole_x = vcycle(whole_rhs, GATHER_LEVEL, whole_levels, apply_padded, None)
        return lax.dynamic_slice(whole_x, (segment_ordinal * block_h, range_index * block_w),
                                 (block_h, block_w))

    def precondition(vector):
        return vcycle(vector, 0, levels, apply_halo, coarse_solve)

    solution = jnp.zeros_like(rhs)
    residual = rhs
    precond = precondition(residual)
    direction = precond
    image_vec = apply_halo(direction, levels[0])
    sums = total(jnp.stack([jnp.sum(residual * precond), jnp.sum(direction * image_vec)]))
    norm_now = sums[0]
    curvature = sums[1]
    for step_index in range(ITERS):
        if step_index > 0:
            image_vec = apply_halo(direction, levels[0])
            curvature = total(jnp.sum(direction * image_vec)[None])[0]
        step_length = norm_now / curvature
        solution = solution + step_length * direction
        residual = residual - step_length * image_vec
        if step_index + 1 < ITERS:
            precond = precondition(residual)
            norm_next = total(jnp.sum(residual * precond)[None])[0]
            direction = precond + norm_next / norm_now * direction
            norm_now = norm_next
    return (solution, weight)


def solution(mesh):
    return jax.shard_map(
        local,
        mesh=mesh,
        in_specs=(P(None, ("az", "rg"), None), P(None, ("az", "rg"), None), P(), P()),
        out_specs=(P("az", "rg"), P("az", "rg")),
        check_vma=False,
    )
```

```python
import jax
import jax.numpy as jnp
from jax import lax
from jax.sharding import PartitionSpec as P

LOOK = 5
LEVELS = 6
ITERS = 3
SWEEPS = 4
SEGMENT_HEIGHT = 160
GATHER_LEVEL = 1


OMEGA = 0.6
MU = 0.01


def neighbours(v):
    n_az = lax.axis_size("az")
    n_rg = lax.axis_size("rg")
    above = lax.ppermute(v[..., -1:, :], "az", [(i, i + 1) for i in range(n_az - 1)])
    below = lax.ppermute(v[..., :1, :], "az", [(i + 1, i) for i in range(n_az - 1)])
    left = lax.ppermute(v[..., :, -1:], "rg", [(i, i + 1) for i in range(n_rg - 1)])
    right = lax.ppermute(v[..., :, :1], "rg", [(i + 1, i) for i in range(n_rg - 1)])
    north = jnp.concatenate([above, v[..., :-1, :]], axis=-2)
    south = jnp.concatenate([v[..., 1:, :], below], axis=-2)
    west = jnp.concatenate([left, v[..., :, :-1]], axis=-1)
    east = jnp.concatenate([v[..., :, 1:], right], axis=-1)
    return north, south, west, east


def apply_halo(vector, operators):
    east, west, south, north, diagonal = operators
    v_n, v_s, v_w, v_e = neighbours(vector)
    return diagonal * vector - east * v_e - west * v_w - south * v_s - north * v_n


def apply_padded(vector, operators):
    east, west, south, north, diagonal = operators
    padded = jnp.pad(vector, 1)
    return (diagonal * vector - east * padded[1:-1, 2:] - west * padded[1:-1, :-2]
            - south * padded[2:, 1:-1] - north * padded[:-2, 1:-1])


def mean_multilook(leading, trailing, row_ok, col_ok):
    valid_mask = (row_ok[:, None] & col_ok[None, :]).astype(jnp.float32)
    first_re = leading[0].astype(jnp.float32) * valid_mask
    first_im = leading[1].astype(jnp.float32) * valid_mask
    second_re = trailing[0].astype(jnp.float32) * valid_mask
    second_im = trailing[1].astype(jnp.float32) * valid_mask
    products = jnp.stack(
        [
            first_re * second_re + first_im * second_im,
            first_im * second_re - first_re * second_im,
            first_re * first_re + first_im * first_im,
            second_re * second_re + second_im * second_im,
        ]
    )
    height_rows, width_cols = valid_mask.shape
    span = LOOK * 128
    grouped = products.reshape(4, height_rows, width_cols // span, span)
    cols = jnp.einsum("pikc,cd->pikd", grouped, group_sum(span, LOOK).T, precision=HIGHEST)
    cols = cols.reshape(4, height_rows, width_cols // LOOK)
    return jnp.einsum("ri,pic->prc", group_sum(height_rows, LOOK), cols, precision=HIGHEST)


def edge_terms(left_re, left_im, left_weight, right_re, right_im, right_weight):
    edge_weight = 0.5 * (left_weight + right_weight)
    cross_im = right_im * left_re - right_re * left_im
    power_sum = (
        left_re * left_re + left_im * left_im + right_re * right_re + right_im * right_im + 1.0
    )
    return (edge_weight, 2.0 * cross_im / power_sum)


HIGHEST = lax.Precision.HIGHEST


def group_sum(n, size):
    group = lax.broadcasted_iota(jnp.int32, (n // size, n), 0)
    cell = lax.broadcasted_iota(jnp.int32, (n // size, n), 1)
    return (cell // size == group).astype(jnp.float32)


def pick(n, offset):
    group = lax.broadcasted_iota(jnp.int32, (n // 2, n), 0)
    cell = lax.broadcasted_iota(jnp.int32, (n // 2, n), 1)
    return (cell == 2 * group + offset).astype(jnp.float32)


def sandwich(left, vector, right):
    inner = jnp.dot(left, vector, precision=HIGHEST)
    return jnp.dot(inner, right, precision=HIGHEST)


def restrict_sum(vector):
    rows_now, cols_now = vector.shape
    return sandwich(group_sum(rows_now, 2), vector, group_sum(cols_now, 2).T)


def prolong_copy(vector):
    rows_now, cols_now = vector.shape
    return sandwich(group_sum(2 * rows_now, 2).T, vector, group_sum(2 * cols_now, 2))


def coarsen(east, west, south, north):
    rows_now, cols_now = east.shape
    row_sum = group_sum(rows_now, 2)
    col_sum = group_sum(cols_now, 2).T
    return (
        sandwich(row_sum, east, pick(cols_now, 1).T),
        sandwich(row_sum, west, pick(cols_now, 0).T),
        sandwich(pick(rows_now, 1), south, col_sum),
        sandwich(pick(rows_now, 0), north, col_sum),
    )


def build_levels(east, west, south, north, first_level, last_level):
    levels = {}
    for level in range(first_level, last_level):
        diagonal = east + west + south + north + MU * 4.0**level
        levels[level] = (east, west, south, north, diagonal)
        if level + 1 < LEVELS:
            east, west, south, north = coarsen(east, west, south, north)
    return levels, (east, west, south, north)


def jacobi_sweeps(rhs_vec, operators, apply_fn):
    estimate = OMEGA * rhs_vec / operators[4]
    for sweep_index in range(SWEEPS - 1):
        estimate = estimate + OMEGA * (rhs_vec - apply_fn(estimate, operators)) / operators[4]
    return estimate


def vcycle(rhs_vec, level, levels, apply_fn, stop_fn):
    if level == LEVELS - 1:
        return jacobi_sweeps(rhs_vec, levels[level], apply_fn)
    if stop_fn is not None and level == GATHER_LEVEL:
        return stop_fn(rhs_vec)
    diagonal = levels[level][4]
    estimate = OMEGA * rhs_vec / diagonal
    remain = rhs_vec - apply_fn(estimate, levels[level])
    correction = vcycle(restrict_sum(remain), level + 1, levels, apply_fn, stop_fn)
    estimate = estimate + prolong_copy(correction)
    return estimate + OMEGA * (rhs_vec - apply_fn(estimate, levels[level])) / diagonal


def everyone():
    return lax.axis_size("az") * lax.axis_size("rg")


def gather_grid(blocks):
    n_az = lax.axis_size("az")
    n_rg = lax.axis_size("rg")
    count, h, w = blocks.shape
    sent = jnp.broadcast_to(blocks[None], (n_az * n_rg, count, h, w))
    got = lax.all_to_all(sent, ("az", "rg"), 0, 0, tiled=True)
    got = got.reshape(n_az, n_rg, count, h, w).transpose(2, 0, 3, 1, 4)
    return got.reshape(count, n_az * h, n_rg * w)


def total(values):
    n = everyone()
    sent = jnp.broadcast_to(values[None], (n, values.shape[0]))
    got = lax.all_to_all(sent, ("az", "rg"), 0, 0, tiled=True)
    return jnp.sum(got, axis=0)


def local(master_phasor_raster, slave_phasor_raster, segment_track_trim, segment_slant_trim):
    n_az = lax.axis_size("az")
    n_range = lax.axis_size("rg")
    segment_ordinal = lax.axis_index("az")
    range_index = lax.axis_index("rg")
    track_trim_width = lax.dynamic_index_in_dim(
        segment_track_trim, segment_ordinal, 0, keepdims=False
    )
    slant_trim_width = lax.dynamic_index_in_dim(
        segment_slant_trim, segment_ordinal, 0, keepdims=False
    )
    lines_here = master_phasor_raster.shape[1]
    slant_sample_total = master_phasor_raster.shape[2]
    along_track_position = range_index * lines_here + jnp.arange(lines_here, dtype=jnp.int32)
    column_index = jnp.arange(slant_sample_total, dtype=jnp.int32)
    row_ok = (along_track_position >= track_trim_width[0]) & (
        along_track_position < SEGMENT_HEIGHT - track_trim_width[1]
    )
    col_ok = (column_index >= slant_trim_width[0]) & (
        column_index < slant_sample_total - slant_trim_width[1]
    )
    pixel_totals = mean_multilook(master_phasor_raster, slave_phasor_raster, row_ok, col_ok)
    look_re, look_im, power_one, power_two = (
        pixel_totals[0],
        pixel_totals[1],
        pixel_totals[2],
        pixel_totals[3],
    )
    weight = 0.05 + 4.0 * (look_re * look_re + look_im * look_im) / jnp.maximum(
        power_one * power_two, 1.0
    )
    fields = jnp.stack([look_re, look_im, weight])
    n_fields, rows_here, cols_all = fields.shape
    cols_here = cols_all // n_range
    fields = fields.reshape(n_fields, rows_here, n_range, cols_here).transpose(2, 0, 1, 3)
    fields = lax.all_to_all(fields, "rg", 0, 0, tiled=True)
    fields = fields.transpose(1, 0, 2, 3).reshape(n_fields, n_range * rows_here, cols_here)
    weight = fields[2]
    shard_height_total = n_range * rows_here

    f_n, f_s, f_w, f_e = neighbours(fields)
    edge_h, grad_h = edge_terms(fields[0], fields[1], fields[2], f_e[0], f_e[1], f_e[2])
    col_global = range_index * cols_here + jnp.arange(cols_here, dtype=jnp.int32)
    keep_h = (col_global <= cols_here * n_range - 2).astype(jnp.float32)
    edge_h = edge_h * keep_h[None, :]
    edge_v, grad_v = edge_terms(fields[0], fields[1], fields[2], f_s[0], f_s[1], f_s[2])
    row_global = segment_ordinal * shard_height_total + jnp.arange(shard_height_total, dtype=jnp.int32)
    keep_v = (row_global <= shard_height_total * n_az - 2).astype(jnp.float32)
    edge_v = edge_v * keep_v[:, None]
    flux_h = edge_h * grad_h
    flux_v = edge_v * grad_v
    e_n, _, e_w, _ = neighbours(jnp.stack([edge_h, flux_h, edge_v, flux_v]))
    west_edge, flux_w, north_edge, flux_n = e_w[0], e_w[1], e_n[2], e_n[3]
    rhs = -(flux_h - flux_w + flux_v - flux_n)

    levels, coarse_edges = build_levels(edge_h, west_edge, south=edge_v, north=north_edge,
                                        first_level=0, last_level=GATHER_LEVEL)
    whole_edges = gather_grid(jnp.stack(coarse_edges))
    whole_levels, _ = build_levels(whole_edges[0], whole_edges[1], whole_edges[2], whole_edges[3],
                                   GATHER_LEVEL, LEVELS)
    block_h, block_w = coarse_edges[0].shape

    def coarse_solve(rhs_vec):
        whole_rhs = gather_grid(rhs_vec[None])[0]
        whole_x = vcycle(whole_rhs, GATHER_LEVEL, whole_levels, apply_padded, None)
        return lax.dynamic_slice(whole_x, (segment_ordinal * block_h, range_index * block_w),
                                 (block_h, block_w))

    def precondition(vector):
        return vcycle(vector, 0, levels, apply_halo, coarse_solve)

    solution = jnp.zeros_like(rhs)
    residual = rhs
    precond = precondition(residual)
    direction = precond
    image_vec = apply_halo(direction, levels[0])
    sums = total(jnp.stack([jnp.sum(residual * precond), jnp.sum(direction * image_vec)]))
    norm_now = sums[0]
    curvature = sums[1]
    for step_index in range(ITERS):
        if step_index > 0:
            image_vec = apply_halo(direction, levels[0])
            curvature = total(jnp.sum(direction * image_vec)[None])[0]
        step_length = norm_now / curvature
        solution = solution + step_length * direction
        residual = residual - step_length * image_vec
        if step_index + 1 < ITERS:
            precond = precondition(residual)
            norm_next = total(jnp.sum(residual * precond)[None])[0]
            direction = precond + norm_next / norm_now * direction
            norm_now = norm_next
    return (solution, weight)


def solution(mesh):
    return jax.shard_map(
        local,
        mesh=mesh,
        in_specs=(P(None, ("az", "rg"), None), P(None, ("az", "rg"), None), P(), P()),
        out_specs=(P("az", "rg"), P("az", "rg")),
        check_vma=False,
    )
```

```python
import jax
import jax.numpy as jnp
from jax import lax
from jax.sharding import PartitionSpec as P

LOOK = 5
LEVELS = 6
ITERS = 3
SWEEPS = 4
SEGMENT_HEIGHT = 160
GATHER_LEVEL = 1


OMEGA = 0.6
MU = 0.01


def neighbours(v):
    n_az = lax.axis_size("az")
    n_rg = lax.axis_size("rg")
    above = lax.ppermute(v[..., -1:, :], "az", [(i, i + 1) for i in range(n_az - 1)])
    below = lax.ppermute(v[..., :1, :], "az", [(i + 1, i) for i in range(n_az - 1)])
    left = lax.ppermute(v[..., :, -1:], "rg", [(i, i + 1) for i in range(n_rg - 1)])
    right = lax.ppermute(v[..., :, :1], "rg", [(i + 1, i) for i in range(n_rg - 1)])
    north = jnp.concatenate([above, v[..., :-1, :]], axis=-2)
    south = jnp.concatenate([v[..., 1:, :], below], axis=-2)
    west = jnp.concatenate([left, v[..., :, :-1]], axis=-1)
    east = jnp.concatenate([v[..., :, 1:], right], axis=-1)
    return north, south, west, east


def apply_halo(vector, operators):
    east, west, south, north, diagonal = operators
    v_n, v_s, v_w, v_e = neighbours(vector)
    return diagonal * vector - east * v_e - west * v_w - south * v_s - north * v_n


def apply_padded(vector, operators):
    east, west, south, north, diagonal = operators
    padded = jnp.pad(vector, 1)
    return (diagonal * vector - east * padded[1:-1, 2:] - west * padded[1:-1, :-2]
            - south * padded[2:, 1:-1] - north * padded[:-2, 1:-1])


def mean_multilook(leading, trailing, row_ok, col_ok):
    valid_mask = (row_ok[:, None] & col_ok[None, :]).astype(jnp.float32)
    first_re = leading[0].astype(jnp.float32) * valid_mask
    first_im = leading[1].astype(jnp.float32) * valid_mask
    second_re = trailing[0].astype(jnp.float32) * valid_mask
    second_im = trailing[1].astype(jnp.float32) * valid_mask
    products = jnp.stack(
        [
            first_re * second_re + first_im * second_im,
            first_im * second_re - first_re * second_im,
            first_re * first_re + first_im * first_im,
            second_re * second_re + second_im * second_im,
        ]
    )
    height_rows, width_cols = valid_mask.shape
    span = LOOK * 128
    grouped = products.reshape(4, height_rows, width_cols // span, span)
    cols = jnp.einsum("pikc,cd->pikd", grouped, group_sum(span, LOOK).T, precision=HIGHEST)
    cols = cols.reshape(4, height_rows, width_cols // LOOK)
    return jnp.einsum("ri,pic->prc", group_sum(height_rows, LOOK), cols, precision=HIGHEST)


def edge_terms(left_re, left_im, left_weight, right_re, right_im, right_weight):
    edge_weight = 0.5 * (left_weight + right_weight)
    cross_im = right_im * left_re - right_re * left_im
    power_sum = (
        left_re * left_re + left_im * left_im + right_re * right_re + right_im * right_im + 1.0
    )
    return (edge_weight, 2.0 * cross_im / power_sum)


HIGHEST = lax.Precision.HIGHEST


def group_sum(n, size):
    group = lax.broadcasted_iota(jnp.int32, (n // size, n), 0)
    cell = lax.broadcasted_iota(jnp.int32, (n // size, n), 1)
    return (cell // size == group).astype(jnp.float32)


def pick(n, offset):
    group = lax.broadcasted_iota(jnp.int32, (n // 2, n), 0)
    cell = lax.broadcasted_iota(jnp.int32, (n // 2, n), 1)
    return (cell == 2 * group + offset).astype(jnp.float32)


def sandwich(left, vector, right):
    inner = jnp.dot(left, vector, precision=HIGHEST)
    return jnp.dot(inner, right, precision=HIGHEST)


def restrict_sum(vector):
    rows_now, cols_now = vector.shape
    return sandwich(group_sum(rows_now, 2), vector, group_sum(cols_now, 2).T)


def prolong_copy(vector):
    rows_now, cols_now = vector.shape
    return sandwich(group_sum(2 * rows_now, 2).T, vector, group_sum(2 * cols_now, 2))


def coarsen(east, west, south, north):
    rows_now, cols_now = east.shape
    row_sum = group_sum(rows_now, 2)
    col_sum = group_sum(cols_now, 2).T
    return (
        sandwich(row_sum, east, pick(cols_now, 1).T),
        sandwich(row_sum, west, pick(cols_now, 0).T),
        sandwich(pick(rows_now, 1), south, col_sum),
        sandwich(pick(rows_now, 0), north, col_sum),
    )


def build_levels(east, west, south, north, first_level, last_level):
    levels = {}
    for level in range(first_level, last_level):
        diagonal = east + west + south + north + MU * 4.0**level
        levels[level] = (east, west, south, north, diagonal)
        if level + 1 < LEVELS:
            east, west, south, north = coarsen(east, west, south, north)
    return levels, (east, west, south, north)


def jacobi_sweeps(rhs_vec, operators, apply_fn):
    estimate = OMEGA * rhs_vec / operators[4]
    for sweep_index in range(SWEEPS - 1):
        estimate = estimate + OMEGA * (rhs_vec - apply_fn(estimate, operators)) / operators[4]
    return estimate


def vcycle(rhs_vec, level, levels, apply_fn, stop_fn):
    if level == LEVELS - 1:
        return jacobi_sweeps(rhs_vec, levels[level], apply_fn)
    if stop_fn is not None and level == GATHER_LEVEL:
        return stop_fn(rhs_vec)
    diagonal = levels[level][4]
    estimate = OMEGA * rhs_vec / diagonal
    remain = rhs_vec - apply_fn(estimate, levels[level])
    correction = vcycle(restrict_sum(remain), level + 1, levels, apply_fn, stop_fn)
    estimate = estimate + prolong_copy(correction)
    return estimate + OMEGA * (rhs_vec - apply_fn(estimate, levels[level])) / diagonal


def everyone():
    return lax.axis_size("az") * lax.axis_size("rg")


def gather_grid(blocks):
    n_az = lax.axis_size("az")
    n_rg = lax.axis_size("rg")
    count, h, w = blocks.shape
    sent = jnp.broadcast_to(blocks[None], (n_az * n_rg, count, h, w))
    got = lax.all_to_all(sent, ("az", "rg"), 0, 0, tiled=True)
    got = got.reshape(n_az, n_rg, count, h, w).transpose(2, 0, 3, 1, 4)
    return got.reshape(count, n_az * h, n_rg * w)


def total(values):
    n = everyone()
    sent = jnp.broadcast_to(values[None], (n, values.shape[0]))
    got = lax.all_to_all(sent, ("az", "rg"), 0, 0, tiled=True)
    return jnp.sum(got, axis=0)


def local(master_phasor_raster, slave_phasor_raster, segment_track_trim, segment_slant_trim):
    n_az = lax.axis_size("az")
    n_range = lax.axis_size("rg")
    segment_ordinal = lax.axis_index("az")
    range_index = lax.axis_index("rg")
    track_trim_width = lax.dynamic_index_in_dim(
        segment_track_trim, segment_ordinal, 0, keepdims=False
    )
    slant_trim_width = lax.dynamic_index_in_dim(
        segment_slant_trim, segment_ordinal, 0, keepdims=False
    )
    lines_here = master_phasor_raster.shape[1]
    slant_sample_total = master_phasor_raster.shape[2]
    along_track_position = range_index * lines_here + jnp.arange(lines_here, dtype=jnp.int32)
    column_index = jnp.arange(slant_sample_total, dtype=jnp.int32)
    row_ok = (along_track_position >= track_trim_width[0]) & (
        along_track_position < SEGMENT_HEIGHT - track_trim_width[1]
    )
    col_ok = (column_index >= slant_trim_width[0]) & (
        column_index < slant_sample_total - slant_trim_width[1]
    )
    pixel_totals = mean_multilook(master_phasor_raster, slave_phasor_raster, row_ok, col_ok)
    look_re, look_im, power_one, power_two = (
        pixel_totals[0],
        pixel_totals[1],
        pixel_totals[2],
        pixel_totals[3],
    )
    weight = 0.05 + 4.0 * (look_re * look_re + look_im * look_im) / jnp.maximum(
        power_one * power_two, 1.0
    )
    fields = jnp.stack([look_re, look_im, weight])
    n_fields, rows_here, cols_all = fields.shape
    cols_here = cols_all // n_range
    fields = fields.reshape(n_fields, rows_here, n_range, cols_here).transpose(2, 0, 1, 3)
    fields = lax.all_to_all(fields, "rg", 0, 0, tiled=True)
    fields = fields.transpose(1, 0, 2, 3).reshape(n_fields, n_range * rows_here, cols_here)
    weight = fields[2]
    shard_height_total = n_range * rows_here

    f_n, f_s, f_w, f_e = neighbours(fields)
    edge_h, grad_h = edge_terms(fields[0], fields[1], fields[2], f_e[0], f_e[1], f_e[2])
    col_global = range_index * cols_here + jnp.arange(cols_here, dtype=jnp.int32)
    keep_h = (col_global <= cols_here * n_range - 2).astype(jnp.float32)
    edge_h = edge_h * keep_h[None, :]
    edge_v, grad_v = edge_terms(fields[0], fields[1], fields[2], f_s[0], f_s[1], f_s[2])
    row_global = segment_ordinal * shard_height_total + jnp.arange(shard_height_total, dtype=jnp.int32)
    keep_v = (row_global <= shard_height_total * n_az - 2).astype(jnp.float32)
    edge_v = edge_v * keep_v[:, None]
    flux_h = edge_h * grad_h
    flux_v = edge_v * grad_v
    e_n, _, e_w, _ = neighbours(jnp.stack([edge_h, flux_h, edge_v, flux_v]))
    west_edge, flux_w, north_edge, flux_n = e_w[0], e_w[1], e_n[2], e_n[3]
    rhs = -(flux_h - flux_w + flux_v - flux_n)

    levels, coarse_edges = build_levels(edge_h, west_edge, south=edge_v, north=north_edge,
                                        first_level=0, last_level=GATHER_LEVEL)
    block_h, block_w = coarse_edges[0].shape
    whole = {}

    def coarse_solve(rhs_vec):
        if not whole:
            got = gather_grid(jnp.concatenate([jnp.stack(coarse_edges), rhs_vec[None]]))
            whole["levels"] = build_levels(got[0], got[1], got[2], got[3], GATHER_LEVEL, LEVELS)[0]
            whole_rhs = got[4]
        else:
            whole_rhs = gather_grid(rhs_vec[None])[0]
        whole_x = vcycle(whole_rhs, GATHER_LEVEL, whole["levels"], apply_padded, None)
        return lax.dynamic_slice(whole_x, (segment_ordinal * block_h, range_index * block_w),
                                 (block_h, block_w))

    def precondition(vector):
        return vcycle(vector, 0, levels, apply_halo, coarse_solve)

    solution = jnp.zeros_like(rhs)
    residual = rhs
    precond = precondition(residual)
    direction = precond
    image_vec = apply_halo(direction, levels[0])
    sums = total(jnp.stack([jnp.sum(residual * precond), jnp.sum(direction * image_vec)]))
    norm_now = sums[0]
    curvature = sums[1]
    for step_index in range(ITERS):
        step_length = norm_now / curvature
        solution = solution + step_length * direction
        if step_index + 1 < ITERS:
            residual = residual - step_length * image_vec
            precond = precondition(residual)
            image_z = apply_halo(precond, levels[0])
            sums = total(jnp.stack([jnp.sum(residual * precond), jnp.sum(precond * image_z),
                                    jnp.sum(precond * image_vec)]))
            norm_next = sums[0]
            ratio = norm_next / norm_now
            direction = precond + ratio * direction
            image_vec = image_z + ratio * image_vec
            curvature = sums[1] + 2.0 * ratio * sums[2] + ratio * ratio * curvature
            norm_now = norm_next
    return (solution, weight)


def solution(mesh):
    return jax.shard_map(
        local,
        mesh=mesh,
        in_specs=(P(None, ("az", "rg"), None), P(None, ("az", "rg"), None), P(), P()),
        out_specs=(P("az", "rg"), P("az", "rg")),
        check_vma=False,
    )
```

```python
import jax
import jax.numpy as jnp
from jax import lax
from jax.sharding import PartitionSpec as P

LOOK = 5
LEVELS = 6
ITERS = 3
SWEEPS = 4
SEGMENT_HEIGHT = 160
GATHER_LEVEL = 1


OMEGA = 0.6
MU = 0.01


def neighbours(v):
    n_az = lax.axis_size("az")
    n_rg = lax.axis_size("rg")
    above = lax.ppermute(v[..., -1:, :], "az", [(i, i + 1) for i in range(n_az - 1)])
    below = lax.ppermute(v[..., :1, :], "az", [(i + 1, i) for i in range(n_az - 1)])
    left = lax.ppermute(v[..., :, -1:], "rg", [(i, i + 1) for i in range(n_rg - 1)])
    right = lax.ppermute(v[..., :, :1], "rg", [(i + 1, i) for i in range(n_rg - 1)])
    north = jnp.concatenate([above, v[..., :-1, :]], axis=-2)
    south = jnp.concatenate([v[..., 1:, :], below], axis=-2)
    west = jnp.concatenate([left, v[..., :, :-1]], axis=-1)
    east = jnp.concatenate([v[..., :, 1:], right], axis=-1)
    return north, south, west, east


def apply_halo(vector, operators):
    east, west, south, north, diagonal = operators
    v_n, v_s, v_w, v_e = neighbours(vector)
    return diagonal * vector - east * v_e - west * v_w - south * v_s - north * v_n


def apply_padded(vector, operators):
    east, west, south, north, diagonal = operators
    padded = jnp.pad(vector, 1)
    return (diagonal * vector - east * padded[1:-1, 2:] - west * padded[1:-1, :-2]
            - south * padded[2:, 1:-1] - north * padded[:-2, 1:-1])


def mean_multilook(leading, trailing, row_ok, col_ok):
    valid_mask = (row_ok[:, None] & col_ok[None, :]).astype(jnp.float32)
    first_re = leading[0].astype(jnp.float32) * valid_mask
    first_im = leading[1].astype(jnp.float32) * valid_mask
    second_re = trailing[0].astype(jnp.float32) * valid_mask
    second_im = trailing[1].astype(jnp.float32) * valid_mask
    products = jnp.stack(
        [
            first_re * second_re + first_im * second_im,
            first_im * second_re - first_re * second_im,
            first_re * first_re + first_im * first_im,
            second_re * second_re + second_im * second_im,
        ]
    )
    height_rows, width_cols = valid_mask.shape
    span = LOOK * 128
    grouped = products.reshape(4, height_rows, width_cols // span, span)
    cols = jnp.einsum("pikc,cd->pikd", grouped, group_sum(span, LOOK).T, precision=HIGHEST)
    cols = cols.reshape(4, height_rows, width_cols // LOOK)
    return jnp.einsum("ri,pic->prc", group_sum(height_rows, LOOK), cols, precision=HIGHEST)


def edge_terms(left_re, left_im, left_weight, right_re, right_im, right_weight):
    edge_weight = 0.5 * (left_weight + right_weight)
    cross_im = right_im * left_re - right_re * left_im
    power_sum = (
        left_re * left_re + left_im * left_im + right_re * right_re + right_im * right_im + 1.0
    )
    return (edge_weight, 2.0 * cross_im / power_sum)


HIGHEST = lax.Precision.HIGHEST


def group_sum(n, size):
    group = lax.broadcasted_iota(jnp.int32, (n // size, n), 0)
    cell = lax.broadcasted_iota(jnp.int32, (n // size, n), 1)
    return (cell // size == group).astype(jnp.float32)


def pick(n, offset):
    group = lax.broadcasted_iota(jnp.int32, (n // 2, n), 0)
    cell = lax.broadcasted_iota(jnp.int32, (n // 2, n), 1)
    return (cell == 2 * group + offset).astype(jnp.float32)


def sandwich(left, vector, right):
    inner = jnp.dot(left, vector, precision=HIGHEST)
    return jnp.dot(inner, right, precision=HIGHEST)


def restrict_sum(vector):
    rows_now, cols_now = vector.shape
    return sandwich(group_sum(rows_now, 2), vector, group_sum(cols_now, 2).T)


def prolong_copy(vector):
    rows_now, cols_now = vector.shape
    return sandwich(group_sum(2 * rows_now, 2).T, vector, group_sum(2 * cols_now, 2))


def coarsen(east, west, south, north):
    rows_now, cols_now = east.shape
    row_sum = group_sum(rows_now, 2)
    col_sum = group_sum(cols_now, 2).T
    return (
        sandwich(row_sum, east, pick(cols_now, 1).T),
        sandwich(row_sum, west, pick(cols_now, 0).T),
        sandwich(pick(rows_now, 1), south, col_sum),
        sandwich(pick(rows_now, 0), north, col_sum),
    )


def build_levels(east, west, south, north, first_level, last_level):
    levels = {}
    for level in range(first_level, last_level):
        diagonal = east + west + south + north + MU * 4.0**level
        levels[level] = (east, west, south, north, diagonal)
        if level + 1 < LEVELS:
            east, west, south, north = coarsen(east, west, south, north)
    return levels, (east, west, south, north)


def jacobi_sweeps(rhs_vec, operators, apply_fn):
    estimate = OMEGA * rhs_vec / operators[4]
    for sweep_index in range(SWEEPS - 1):
        estimate = estimate + OMEGA * (rhs_vec - apply_fn(estimate, operators)) / operators[4]
    return estimate


def vcycle(rhs_vec, level, levels, apply_fn, stop_fn):
    if level == LEVELS - 1:
        return jacobi_sweeps(rhs_vec, levels[level], apply_fn)
    if stop_fn is not None and level == GATHER_LEVEL:
        return stop_fn(rhs_vec)
    diagonal = levels[level][4]
    estimate = OMEGA * rhs_vec / diagonal
    remain = rhs_vec - apply_fn(estimate, levels[level])
    correction = vcycle(restrict_sum(remain), level + 1, levels, apply_fn, stop_fn)
    estimate = estimate + prolong_copy(correction)
    return estimate + OMEGA * (rhs_vec - apply_fn(estimate, levels[level])) / diagonal


def everyone():
    return lax.axis_size("az") * lax.axis_size("rg")


def gather_strip(blocks):
    n_az = lax.axis_size("az")
    n_rg = lax.axis_size("rg")
    count, h, w = blocks.shape
    sent = jnp.broadcast_to(blocks[None], (n_az, count, h, w))
    got = lax.all_to_all(sent, "az", 0, 0, tiled=True)
    column = got.transpose(1, 0, 2, 3).reshape(count, n_az * h, w)
    left = lax.ppermute(column, "rg", [(i, i + 1) for i in range(n_rg - 1)])
    right = lax.ppermute(column, "rg", [(i + 1, i) for i in range(n_rg - 1)])
    return jnp.concatenate([left, column, right], axis=-1)


def shifted(values, axis):
    pad = [(0, 0)] * values.ndim
    pad[axis] = (1, 0)
    return lax.slice_in_dim(jnp.pad(values, pad), 0, values.shape[axis], axis=axis)


def total(values):
    n = everyone()
    sent = jnp.broadcast_to(values[None], (n, values.shape[0]))
    got = lax.all_to_all(sent, ("az", "rg"), 0, 0, tiled=True)
    return jnp.sum(got, axis=0)


def local(master_phasor_raster, slave_phasor_raster, segment_track_trim, segment_slant_trim):
    n_az = lax.axis_size("az")
    n_range = lax.axis_size("rg")
    segment_ordinal = lax.axis_index("az")
    range_index = lax.axis_index("rg")
    track_trim_width = lax.dynamic_index_in_dim(
        segment_track_trim, segment_ordinal, 0, keepdims=False
    )
    slant_trim_width = lax.dynamic_index_in_dim(
        segment_slant_trim, segment_ordinal, 0, keepdims=False
    )
    lines_here = master_phasor_raster.shape[1]
    slant_sample_total = master_phasor_raster.shape[2]
    along_track_position = range_index * lines_here + jnp.arange(lines_here, dtype=jnp.int32)
    column_index = jnp.arange(slant_sample_total, dtype=jnp.int32)
    row_ok = (along_track_position >= track_trim_width[0]) & (
        along_track_position < SEGMENT_HEIGHT - track_trim_width[1]
    )
    col_ok = (column_index >= slant_trim_width[0]) & (
        column_index < slant_sample_total - slant_trim_width[1]
    )
    pixel_totals = mean_multilook(master_phasor_raster, slave_phasor_raster, row_ok, col_ok)
    look_re, look_im, power_one, power_two = (
        pixel_totals[0],
        pixel_totals[1],
        pixel_totals[2],
        pixel_totals[3],
    )
    weight = 0.05 + 4.0 * (look_re * look_re + look_im * look_im) / jnp.maximum(
        power_one * power_two, 1.0
    )
    fields = jnp.stack([look_re, look_im, weight])
    n_fields, rows_here, cols_all = fields.shape
    cols_here = cols_all // n_range
    fields = fields.reshape(n_fields, rows_here, n_range, cols_here).transpose(2, 0, 1, 3)
    fields = lax.all_to_all(fields, "rg", 0, 0, tiled=True)
    fields = fields.transpose(1, 0, 2, 3).reshape(n_fields, n_range * rows_here, cols_here)
    weight = fields[2]
    shard_height_total = n_range * rows_here

    f_n, f_s, f_w, f_e = neighbours(fields)
    edge_h, grad_h = edge_terms(fields[0], fields[1], fields[2], f_e[0], f_e[1], f_e[2])
    col_global = range_index * cols_here + jnp.arange(cols_here, dtype=jnp.int32)
    keep_h = (col_global <= cols_here * n_range - 2).astype(jnp.float32)
    edge_h = edge_h * keep_h[None, :]
    edge_v, grad_v = edge_terms(fields[0], fields[1], fields[2], f_s[0], f_s[1], f_s[2])
    row_global = segment_ordinal * shard_height_total + jnp.arange(shard_height_total, dtype=jnp.int32)
    keep_v = (row_global <= shard_height_total * n_az - 2).astype(jnp.float32)
    edge_v = edge_v * keep_v[:, None]
    flux_h = edge_h * grad_h
    flux_v = edge_v * grad_v
    e_n, _, e_w, _ = neighbours(jnp.stack([edge_h, flux_h, edge_v, flux_v]))
    west_edge, flux_w, north_edge, flux_n = e_w[0], e_w[1], e_n[2], e_n[3]
    rhs = -(flux_h - flux_w + flux_v - flux_n)

    levels, coarse_edges = build_levels(edge_h, west_edge, south=edge_v, north=north_edge,
                                        first_level=0, last_level=GATHER_LEVEL)
    block_h, block_w = coarse_edges[0].shape
    whole = {}

    def coarse_solve(rhs_vec):
        if not whole:
            got = gather_strip(jnp.stack([coarse_edges[0], coarse_edges[2], rhs_vec]))
            east_s, south_s = got[0], got[1]
            whole["levels"] = build_levels(east_s, shifted(east_s, 1), south_s, shifted(south_s, 0),
                                           GATHER_LEVEL, LEVELS)[0]
            strip_rhs = got[2]
        else:
            strip_rhs = gather_strip(rhs_vec[None])[0]
        strip_x = vcycle(strip_rhs, GATHER_LEVEL, whole["levels"], apply_padded, None)
        return lax.dynamic_slice(strip_x, (segment_ordinal * block_h, block_w), (block_h, block_w))

    def precondition(vector):
        return vcycle(vector, 0, levels, apply_halo, coarse_solve)

    solution = jnp.zeros_like(rhs)
    residual = rhs
    precond = precondition(residual)
    direction = precond
    image_vec = apply_halo(direction, levels[0])
    sums = total(jnp.stack([jnp.sum(residual * precond), jnp.sum(direction * image_vec)]))
    norm_now = sums[0]
    curvature = sums[1]
    for step_index in range(ITERS):
        step_length = norm_now / curvature
        solution = solution + step_length * direction
        if step_index + 1 < ITERS:
            residual = residual - step_length * image_vec
            precond = precondition(residual)
            image_z = apply_halo(precond, levels[0])
            sums = total(jnp.stack([jnp.sum(residual * precond), jnp.sum(precond * image_z),
                                    jnp.sum(precond * image_vec)]))
            norm_next = sums[0]
            ratio = norm_next / norm_now
            direction = precond + ratio * direction
            image_vec = image_z + ratio * image_vec
            curvature = sums[1] + 2.0 * ratio * sums[2] + ratio * ratio * curvature
            norm_now = norm_next
    return (solution, weight)


def solution(mesh):
    return jax.shard_map(
        local,
        mesh=mesh,
        in_specs=(P(None, ("az", "rg"), None), P(None, ("az", "rg"), None), P(), P()),
        out_specs=(P("az", "rg"), P("az", "rg")),
        check_vma=False,
    )
```

```python
import jax
import jax.numpy as jnp
from jax import lax
from jax.sharding import PartitionSpec as P

LOOK = 5
LEVELS = 6
ITERS = 3
SWEEPS = 4
SEGMENT_HEIGHT = 160
GATHER_LEVEL = 1


OMEGA = 0.6
MU = 0.01


def neighbours(v):
    n_az = lax.axis_size("az")
    n_rg = lax.axis_size("rg")
    above = lax.ppermute(v[..., -1:, :], "az", [(i, i + 1) for i in range(n_az - 1)])
    below = lax.ppermute(v[..., :1, :], "az", [(i + 1, i) for i in range(n_az - 1)])
    left = lax.ppermute(v[..., :, -1:], "rg", [(i, i + 1) for i in range(n_rg - 1)])
    right = lax.ppermute(v[..., :, :1], "rg", [(i + 1, i) for i in range(n_rg - 1)])
    north = jnp.concatenate([above, v[..., :-1, :]], axis=-2)
    south = jnp.concatenate([v[..., 1:, :], below], axis=-2)
    west = jnp.concatenate([left, v[..., :, :-1]], axis=-1)
    east = jnp.concatenate([v[..., :, 1:], right], axis=-1)
    return north, south, west, east


def apply_halo(vector, operators):
    east, west, south, north, diagonal = operators
    v_n, v_s, v_w, v_e = neighbours(vector)
    return diagonal * vector - east * v_e - west * v_w - south * v_s - north * v_n


def extended(v, width):
    n_az = lax.axis_size("az")
    n_rg = lax.axis_size("rg")
    above = lax.ppermute(v[..., -width:, :], "az", [(i, i + 1) for i in range(n_az - 1)])
    below = lax.ppermute(v[..., :width, :], "az", [(i + 1, i) for i in range(n_az - 1)])
    v = jnp.concatenate([above, v, below], axis=-2)
    left = lax.ppermute(v[..., :, -width:], "rg", [(i, i + 1) for i in range(n_rg - 1)])
    right = lax.ppermute(v[..., :, :width], "rg", [(i + 1, i) for i in range(n_rg - 1)])
    return jnp.concatenate([left, v, right], axis=-1)


def apply_inner(padded, operators):
    east, west, south, north, diagonal = operators
    return (diagonal * padded[1:-1, 1:-1] - east * padded[1:-1, 2:] - west * padded[1:-1, :-2]
            - south * padded[2:, 1:-1] - north * padded[:-2, 1:-1])


def apply_padded(vector, operators):
    east, west, south, north, diagonal = operators
    padded = jnp.pad(vector, 1)
    return (diagonal * vector - east * padded[1:-1, 2:] - west * padded[1:-1, :-2]
            - south * padded[2:, 1:-1] - north * padded[:-2, 1:-1])


def mean_multilook(leading, trailing, row_ok, col_ok):
    valid_mask = (row_ok[:, None] & col_ok[None, :]).astype(jnp.float32)
    first_re = leading[0].astype(jnp.float32) * valid_mask
    first_im = leading[1].astype(jnp.float32) * valid_mask
    second_re = trailing[0].astype(jnp.float32) * valid_mask
    second_im = trailing[1].astype(jnp.float32) * valid_mask
    products = jnp.stack(
        [
            first_re * second_re + first_im * second_im,
            first_im * second_re - first_re * second_im,
            first_re * first_re + first_im * first_im,
            second_re * second_re + second_im * second_im,
        ]
    )
    height_rows, width_cols = valid_mask.shape
    span = LOOK * 128
    grouped = products.reshape(4, height_rows, width_cols // span, span)
    cols = jnp.einsum("pikc,cd->pikd", grouped, group_sum(span, LOOK).T, precision=HIGHEST)
    cols = cols.reshape(4, height_rows, width_cols // LOOK)
    return jnp.einsum("ri,pic->prc", group_sum(height_rows, LOOK), cols, precision=HIGHEST)


def edge_terms(left_re, left_im, left_weight, right_re, right_im, right_weight):
    edge_weight = 0.5 * (left_weight + right_weight)
    cross_im = right_im * left_re - right_re * left_im
    power_sum = (
        left_re * left_re + left_im * left_im + right_re * right_re + right_im * right_im + 1.0
    )
    return (edge_weight, 2.0 * cross_im / power_sum)


HIGHEST = lax.Precision.HIGHEST


def group_sum(n, size):
    group = lax.broadcasted_iota(jnp.int32, (n // size, n), 0)
    cell = lax.broadcasted_iota(jnp.int32, (n // size, n), 1)
    return (cell // size == group).astype(jnp.float32)


def pick(n, offset):
    group = lax.broadcasted_iota(jnp.int32, (n // 2, n), 0)
    cell = lax.broadcasted_iota(jnp.int32, (n // 2, n), 1)
    return (cell == 2 * group + offset).astype(jnp.float32)


def sandwich(left, vector, right):
    inner = jnp.dot(left, vector, precision=HIGHEST)
    return jnp.dot(inner, right, precision=HIGHEST)


def restrict_sum(vector):
    rows_now, cols_now = vector.shape
    return sandwich(group_sum(rows_now, 2), vector, group_sum(cols_now, 2).T)


def prolong_copy(vector):
    rows_now, cols_now = vector.shape
    return sandwich(group_sum(2 * rows_now, 2).T, vector, group_sum(2 * cols_now, 2))


def coarsen(east, west, south, north):
    rows_now, cols_now = east.shape
    row_sum = group_sum(rows_now, 2)
    col_sum = group_sum(cols_now, 2).T
    return (
        sandwich(row_sum, east, pick(cols_now, 1).T),
        sandwich(row_sum, west, pick(cols_now, 0).T),
        sandwich(pick(rows_now, 1), south, col_sum),
        sandwich(pick(rows_now, 0), north, col_sum),
    )


def build_levels(east, west, south, north, first_level, last_level):
    levels = {}
    for level in range(first_level, last_level):
        diagonal = east + west + south + north + MU * 4.0**level
        levels[level] = (east, west, south, north, diagonal)
        if level + 1 < LEVELS:
            east, west, south, north = coarsen(east, west, south, north)
    return levels, (east, west, south, north)


def jacobi_sweeps(rhs_vec, operators, apply_fn):
    estimate = OMEGA * rhs_vec / operators[4]
    for sweep_index in range(SWEEPS - 1):
        estimate = estimate + OMEGA * (rhs_vec - apply_fn(estimate, operators)) / operators[4]
    return estimate


def vcycle(rhs_vec, level, levels, apply_fn, stop_fn):
    if level == LEVELS - 1:
        return jacobi_sweeps(rhs_vec, levels[level], apply_fn)
    if stop_fn is not None and level == GATHER_LEVEL:
        return stop_fn(rhs_vec)
    diagonal = levels[level][4]
    estimate = OMEGA * rhs_vec / diagonal
    remain = rhs_vec - apply_fn(estimate, levels[level])
    correction = vcycle(restrict_sum(remain), level + 1, levels, apply_fn, stop_fn)
    estimate = estimate + prolong_copy(correction)
    return estimate + OMEGA * (rhs_vec - apply_fn(estimate, levels[level])) / diagonal


def everyone():
    return lax.axis_size("az") * lax.axis_size("rg")


def gather_strip(blocks):
    n_az = lax.axis_size("az")
    n_rg = lax.axis_size("rg")
    count, h, w = blocks.shape
    sent = jnp.broadcast_to(blocks[None], (n_az, count, h, w))
    got = lax.all_to_all(sent, "az", 0, 0, tiled=True)
    column = got.transpose(1, 0, 2, 3).reshape(count, n_az * h, w)
    left = lax.ppermute(column, "rg", [(i, i + 1) for i in range(n_rg - 1)])
    right = lax.ppermute(column, "rg", [(i + 1, i) for i in range(n_rg - 1)])
    return jnp.concatenate([left, column, right], axis=-1)


def shifted(values, axis):
    pad = [(0, 0)] * values.ndim
    pad[axis] = (1, 0)
    return lax.slice_in_dim(jnp.pad(values, pad), 0, values.shape[axis], axis=axis)


def total(values):
    n = everyone()
    sent = jnp.broadcast_to(values[None], (n, values.shape[0]))
    got = lax.all_to_all(sent, ("az", "rg"), 0, 0, tiled=True)
    return jnp.sum(got, axis=0)


def local(master_phasor_raster, slave_phasor_raster, segment_track_trim, segment_slant_trim):
    n_az = lax.axis_size("az")
    n_range = lax.axis_size("rg")
    segment_ordinal = lax.axis_index("az")
    range_index = lax.axis_index("rg")
    track_trim_width = lax.dynamic_index_in_dim(
        segment_track_trim, segment_ordinal, 0, keepdims=False
    )
    slant_trim_width = lax.dynamic_index_in_dim(
        segment_slant_trim, segment_ordinal, 0, keepdims=False
    )
    lines_here = master_phasor_raster.shape[1]
    slant_sample_total = master_phasor_raster.shape[2]
    along_track_position = range_index * lines_here + jnp.arange(lines_here, dtype=jnp.int32)
    column_index = jnp.arange(slant_sample_total, dtype=jnp.int32)
    row_ok = (along_track_position >= track_trim_width[0]) & (
        along_track_position < SEGMENT_HEIGHT - track_trim_width[1]
    )
    col_ok = (column_index >= slant_trim_width[0]) & (
        column_index < slant_sample_total - slant_trim_width[1]
    )
    pixel_totals = mean_multilook(master_phasor_raster, slave_phasor_raster, row_ok, col_ok)
    look_re, look_im, power_one, power_two = (
        pixel_totals[0],
        pixel_totals[1],
        pixel_totals[2],
        pixel_totals[3],
    )
    weight = 0.05 + 4.0 * (look_re * look_re + look_im * look_im) / jnp.maximum(
        power_one * power_two, 1.0
    )
    fields = jnp.stack([look_re, look_im, weight])
    n_fields, rows_here, cols_all = fields.shape
    cols_here = cols_all // n_range
    fields = fields.reshape(n_fields, rows_here, n_range, cols_here).transpose(2, 0, 1, 3)
    fields = lax.all_to_all(fields, "rg", 0, 0, tiled=True)
    fields = fields.transpose(1, 0, 2, 3).reshape(n_fields, n_range * rows_here, cols_here)
    weight = fields[2]
    shard_height_total = n_range * rows_here

    f_n, f_s, f_w, f_e = neighbours(fields)
    edge_h, grad_h = edge_terms(fields[0], fields[1], fields[2], f_e[0], f_e[1], f_e[2])
    col_global = range_index * cols_here + jnp.arange(cols_here, dtype=jnp.int32)
    keep_h = (col_global <= cols_here * n_range - 2).astype(jnp.float32)
    edge_h = edge_h * keep_h[None, :]
    edge_v, grad_v = edge_terms(fields[0], fields[1], fields[2], f_s[0], f_s[1], f_s[2])
    row_global = segment_ordinal * shard_height_total + jnp.arange(shard_height_total, dtype=jnp.int32)
    keep_v = (row_global <= shard_height_total * n_az - 2).astype(jnp.float32)
    edge_v = edge_v * keep_v[:, None]
    flux_h = edge_h * grad_h
    flux_v = edge_v * grad_v
    e_n, _, e_w, _ = neighbours(jnp.stack([edge_h, flux_h, edge_v, flux_v]))
    west_edge, flux_w, north_edge, flux_n = e_w[0], e_w[1], e_n[2], e_n[3]
    rhs = -(flux_h - flux_w + flux_v - flux_n)

    levels, coarse_edges = build_levels(edge_h, west_edge, south=edge_v, north=north_edge,
                                        first_level=0, last_level=GATHER_LEVEL)
    block_h, block_w = coarse_edges[0].shape
    whole = {}

    ops_wide = extended(jnp.stack(levels[0]), 2)
    diag_wide = jnp.where(ops_wide[4] > 0, ops_wide[4], 1.0)
    ring_ops = tuple(ops_wide[k, 1:-1, 1:-1] for k in range(4)) + (diag_wide[1:-1, 1:-1],)

    def coarse_solve(rhs_vec):
        if not whole:
            got = gather_strip(jnp.stack([coarse_edges[0], coarse_edges[2], rhs_vec]))
            east_s, south_s = got[0], got[1]
            whole["levels"] = build_levels(east_s, shifted(east_s, 1), south_s, shifted(south_s, 0),
                                           GATHER_LEVEL, LEVELS)[0]
            strip_rhs = got[2]
        else:
            strip_rhs = gather_strip(rhs_vec[None])[0]
        strip_x = vcycle(strip_rhs, GATHER_LEVEL, whole["levels"], apply_padded, None)
        strip_x = jnp.pad(strip_x, ((1, 1), (0, 0)))
        return lax.dynamic_slice(strip_x, (segment_ordinal * block_h, block_w - 1),
                                 (block_h + 2, block_w + 2))

    def precondition(rhs_vec):
        rhs_wide = extended(rhs_vec, 2)
        estimate = OMEGA * rhs_wide / diag_wide
        remain = rhs_vec - apply_inner(estimate[1:-1, 1:-1], levels[0])
        estimate = estimate + prolong_copy(coarse_solve(restrict_sum(remain)))
        ring = estimate[1:-1, 1:-1] + OMEGA * (rhs_wide[1:-1, 1:-1] - apply_inner(estimate, ring_ops)) / ring_ops[4]
        return ring[1:-1, 1:-1], apply_inner(ring, levels[0])

    solution = jnp.zeros_like(rhs)
    residual = rhs
    precond, image_vec = precondition(residual)
    direction = precond
    sums = total(jnp.stack([jnp.sum(residual * precond), jnp.sum(direction * image_vec)]))
    norm_now = sums[0]
    curvature = sums[1]
    for step_index in range(ITERS):
        step_length = norm_now / curvature
        solution = solution + step_length * direction
        if step_index + 1 < ITERS:
            residual = residual - step_length * image_vec
            precond, image_z = precondition(residual)
            sums = total(jnp.stack([jnp.sum(residual * precond), jnp.sum(precond * image_z),
                                    jnp.sum(precond * image_vec)]))
            norm_next = sums[0]
            ratio = norm_next / norm_now
            direction = precond + ratio * direction
            image_vec = image_z + ratio * image_vec
            curvature = sums[1] + 2.0 * ratio * sums[2] + ratio * ratio * curvature
            norm_now = norm_next
    return (solution, weight)


def solution(mesh):
    return jax.shard_map(
        local,
        mesh=mesh,
        in_specs=(P(None, ("az", "rg"), None), P(None, ("az", "rg"), None), P(), P()),
        out_specs=(P("az", "rg"), P("az", "rg")),
        check_vma=False,
    )
```

```python
import jax
import jax.numpy as jnp
from jax import lax
from jax.sharding import PartitionSpec as P

LOOK = 5
LEVELS = 6
ITERS = 3
SWEEPS = 4
SEGMENT_HEIGHT = 160
GATHER_LEVEL = 1


OMEGA = 0.6
MU = 0.01


def neighbours(v):
    n_az = lax.axis_size("az")
    n_rg = lax.axis_size("rg")
    above = lax.ppermute(v[..., -1:, :], "az", [(i, i + 1) for i in range(n_az - 1)])
    below = lax.ppermute(v[..., :1, :], "az", [(i + 1, i) for i in range(n_az - 1)])
    left = lax.ppermute(v[..., :, -1:], "rg", [(i, i + 1) for i in range(n_rg - 1)])
    right = lax.ppermute(v[..., :, :1], "rg", [(i + 1, i) for i in range(n_rg - 1)])
    north = jnp.concatenate([above, v[..., :-1, :]], axis=-2)
    south = jnp.concatenate([v[..., 1:, :], below], axis=-2)
    west = jnp.concatenate([left, v[..., :, :-1]], axis=-1)
    east = jnp.concatenate([v[..., :, 1:], right], axis=-1)
    return north, south, west, east


def apply_halo(vector, operators):
    east, west, south, north, diagonal = operators
    v_n, v_s, v_w, v_e = neighbours(vector)
    return diagonal * vector - east * v_e - west * v_w - south * v_s - north * v_n


def extended(v, width):
    n_az = lax.axis_size("az")
    n_rg = lax.axis_size("rg")
    above = lax.ppermute(v[..., -width:, :], "az", [(i, i + 1) for i in range(n_az - 1)])
    below = lax.ppermute(v[..., :width, :], "az", [(i + 1, i) for i in range(n_az - 1)])
    v = jnp.concatenate([above, v, below], axis=-2)
    left = lax.ppermute(v[..., :, -width:], "rg", [(i, i + 1) for i in range(n_rg - 1)])
    right = lax.ppermute(v[..., :, :width], "rg", [(i + 1, i) for i in range(n_rg - 1)])
    return jnp.concatenate([left, v, right], axis=-1)


def apply_inner(padded, operators):
    east, west, south, north, diagonal = operators
    return (diagonal * padded[1:-1, 1:-1] - east * padded[1:-1, 2:] - west * padded[1:-1, :-2]
            - south * padded[2:, 1:-1] - north * padded[:-2, 1:-1])


def apply_padded(vector, operators):
    east, west, south, north, diagonal = operators
    padded = jnp.pad(vector, 1)
    return (diagonal * vector - east * padded[1:-1, 2:] - west * padded[1:-1, :-2]
            - south * padded[2:, 1:-1] - north * padded[:-2, 1:-1])


def mean_multilook(leading, trailing, row_ok, col_ok):
    valid_mask = (row_ok[:, None] & col_ok[None, :]).astype(jnp.float32)
    first_re = leading[0].astype(jnp.float32) * valid_mask
    first_im = leading[1].astype(jnp.float32) * valid_mask
    second_re = trailing[0].astype(jnp.float32) * valid_mask
    second_im = trailing[1].astype(jnp.float32) * valid_mask
    products = jnp.stack(
        [
            first_re * second_re + first_im * second_im,
            first_im * second_re - first_re * second_im,
            first_re * first_re + first_im * first_im,
            second_re * second_re + second_im * second_im,
        ]
    )
    height_rows, width_cols = valid_mask.shape
    span = LOOK * 128
    grouped = products.reshape(4, height_rows, width_cols // span, span)
    cols = jnp.einsum("pikc,cd->pikd", grouped, group_sum(span, LOOK).T, precision=HIGHEST)
    cols = cols.reshape(4, height_rows, width_cols // LOOK)
    return jnp.einsum("ri,pic->prc", group_sum(height_rows, LOOK), cols, precision=HIGHEST)


def edge_terms(left_re, left_im, left_weight, right_re, right_im, right_weight):
    edge_weight = 0.5 * (left_weight + right_weight)
    cross_im = right_im * left_re - right_re * left_im
    power_sum = (
        left_re * left_re + left_im * left_im + right_re * right_re + right_im * right_im + 1.0
    )
    return (edge_weight, 2.0 * cross_im / power_sum)


HIGHEST = lax.Precision.HIGHEST


def group_sum(n, size):
    group = lax.broadcasted_iota(jnp.int32, (n // size, n), 0)
    cell = lax.broadcasted_iota(jnp.int32, (n // size, n), 1)
    return (cell // size == group).astype(jnp.float32)


def pick(n, offset):
    group = lax.broadcasted_iota(jnp.int32, (n // 2, n), 0)
    cell = lax.broadcasted_iota(jnp.int32, (n // 2, n), 1)
    return (cell == 2 * group + offset).astype(jnp.float32)


def sandwich(left, vector, right):
    inner = jnp.dot(left, vector, precision=HIGHEST)
    return jnp.dot(inner, right, precision=HIGHEST)


def restrict_sum(vector):
    rows_now, cols_now = vector.shape
    return sandwich(group_sum(rows_now, 2), vector, group_sum(cols_now, 2).T)


def prolong_copy(vector):
    rows_now, cols_now = vector.shape
    return sandwich(group_sum(2 * rows_now, 2).T, vector, group_sum(2 * cols_now, 2))


def coarsen(east, west, south, north):
    rows_now, cols_now = east.shape
    row_sum = group_sum(rows_now, 2)
    col_sum = group_sum(cols_now, 2).T
    return (
        sandwich(row_sum, east, pick(cols_now, 1).T),
        sandwich(row_sum, west, pick(cols_now, 0).T),
        sandwich(pick(rows_now, 1), south, col_sum),
        sandwich(pick(rows_now, 0), north, col_sum),
    )


def build_levels(east, west, south, north, first_level, last_level):
    levels = {}
    for level in range(first_level, last_level):
        diagonal = east + west + south + north + MU * 4.0**level
        levels[level] = (east, west, south, north, diagonal)
        if level + 1 < LEVELS:
            east, west, south, north = coarsen(east, west, south, north)
    return levels, (east, west, south, north)


def jacobi_sweeps(rhs_vec, operators, apply_fn):
    estimate = OMEGA * rhs_vec / operators[4]
    for sweep_index in range(SWEEPS - 1):
        estimate = estimate + OMEGA * (rhs_vec - apply_fn(estimate, operators)) / operators[4]
    return estimate


def vcycle(rhs_vec, level, levels, apply_fn, stop_fn):
    if level == LEVELS - 1:
        return jacobi_sweeps(rhs_vec, levels[level], apply_fn)
    if stop_fn is not None and level == GATHER_LEVEL:
        return stop_fn(rhs_vec)
    diagonal = levels[level][4]
    estimate = OMEGA * rhs_vec / diagonal
    remain = rhs_vec - apply_fn(estimate, levels[level])
    correction = vcycle(restrict_sum(remain), level + 1, levels, apply_fn, stop_fn)
    estimate = estimate + prolong_copy(correction)
    return estimate + OMEGA * (rhs_vec - apply_fn(estimate, levels[level])) / diagonal


def everyone():
    return lax.axis_size("az") * lax.axis_size("rg")


def gather_strip(blocks):
    n_az = lax.axis_size("az")
    n_rg = lax.axis_size("rg")
    count, h, w = blocks.shape
    sent = jnp.broadcast_to(blocks[None], (n_az, count, h, w))
    got = lax.all_to_all(sent, "az", 0, 0, tiled=True)
    column = got.transpose(1, 0, 2, 3).reshape(count, n_az * h, w)
    left = lax.ppermute(column, "rg", [(i, i + 1) for i in range(n_rg - 1)])
    right = lax.ppermute(column, "rg", [(i + 1, i) for i in range(n_rg - 1)])
    return jnp.concatenate([left, column, right], axis=-1)


def shifted(values, axis):
    pad = [(0, 0)] * values.ndim
    pad[axis] = (1, 0)
    return lax.slice_in_dim(jnp.pad(values, pad), 0, values.shape[axis], axis=axis)


def total(values):
    n = everyone()
    sent = jnp.broadcast_to(values[None], (n, values.shape[0]))
    got = lax.all_to_all(sent, ("az", "rg"), 0, 0, tiled=True)
    return jnp.sum(got, axis=0)


def local(master_phasor_raster, slave_phasor_raster, segment_track_trim, segment_slant_trim):
    n_az = lax.axis_size("az")
    n_range = lax.axis_size("rg")
    segment_ordinal = lax.axis_index("az")
    range_index = lax.axis_index("rg")
    track_trim_width = lax.dynamic_index_in_dim(
        segment_track_trim, segment_ordinal, 0, keepdims=False
    )
    slant_trim_width = lax.dynamic_index_in_dim(
        segment_slant_trim, segment_ordinal, 0, keepdims=False
    )
    lines_here = master_phasor_raster.shape[1]
    slant_sample_total = master_phasor_raster.shape[2]
    along_track_position = range_index * lines_here + jnp.arange(lines_here, dtype=jnp.int32)
    column_index = jnp.arange(slant_sample_total, dtype=jnp.int32)
    row_ok = (along_track_position >= track_trim_width[0]) & (
        along_track_position < SEGMENT_HEIGHT - track_trim_width[1]
    )
    col_ok = (column_index >= slant_trim_width[0]) & (
        column_index < slant_sample_total - slant_trim_width[1]
    )
    pixel_totals = mean_multilook(master_phasor_raster, slave_phasor_raster, row_ok, col_ok)
    look_re, look_im, power_one, power_two = (
        pixel_totals[0],
        pixel_totals[1],
        pixel_totals[2],
        pixel_totals[3],
    )
    weight = 0.05 + 4.0 * (look_re * look_re + look_im * look_im) / jnp.maximum(
        power_one * power_two, 1.0
    )
    border = 3
    fields = jnp.stack([look_re, look_im, weight])
    n_fields, rows_here, cols_all = fields.shape
    cols_here = cols_all // n_range
    fields = jnp.pad(fields, ((0, 0), (0, 0), (border, border)))
    fields = jnp.stack([fields[:, :, c * cols_here:(c + 1) * cols_here + 2 * border] for c in range(n_range)])
    fields = lax.all_to_all(fields, "rg", 0, 0, tiled=True)
    fields = fields.transpose(1, 0, 2, 3).reshape(n_fields, n_range * rows_here, cols_here + 2 * border)
    shard_height_total = n_range * rows_here
    above = lax.ppermute(fields[:, -border:, :], "az", [(i, i + 1) for i in range(n_az - 1)])
    below = lax.ppermute(fields[:, :border, :], "az", [(i + 1, i) for i in range(n_az - 1)])
    fields = jnp.concatenate([above, fields, below], axis=1)
    weight = fields[2, border:-border, border:-border]

    row_global = segment_ordinal * shard_height_total - border + jnp.arange(
        shard_height_total + 2 * border, dtype=jnp.int32)
    col_global = range_index * cols_here - border + jnp.arange(cols_here + 2 * border, dtype=jnp.int32)
    edge_h, grad_h = edge_terms(fields[0, :, :-1], fields[1, :, :-1], fields[2, :, :-1],
                                fields[0, :, 1:], fields[1, :, 1:], fields[2, :, 1:])
    keep_h = ((col_global[:-1] >= 0) & (col_global[:-1] <= cols_here * n_range - 2)).astype(jnp.float32)
    edge_h = edge_h * keep_h[None, :]
    edge_v, grad_v = edge_terms(fields[0, :-1], fields[1, :-1], fields[2, :-1],
                                fields[0, 1:], fields[1, 1:], fields[2, 1:])
    keep_v = ((row_global[:-1] >= 0) & (row_global[:-1] <= shard_height_total * n_az - 2)).astype(jnp.float32)
    edge_v = edge_v * keep_v[:, None]
    flux_h = edge_h * grad_h
    flux_v = edge_v * grad_v
    east_w = edge_h[1:-1, 1:]
    west_w = edge_h[1:-1, :-1]
    south_w = edge_v[1:, 1:-1]
    north_w = edge_v[:-1, 1:-1]
    diag_wide = east_w + west_w + south_w + north_w + MU * 4.0**0
    rhs_wide = -(flux_h[1:-1, 1:] - flux_h[1:-1, :-1] + flux_v[1:, 1:-1] - flux_v[:-1, 1:-1])
    rhs = rhs_wide[2:-2, 2:-2]
    own = (slice(2, -2), slice(2, -2))
    levels, coarse_edges = build_levels(east_w[own], west_w[own], south_w[own], north_w[own],
                                        first_level=0, last_level=GATHER_LEVEL)
    block_h, block_w = coarse_edges[0].shape
    whole = {}

    ring_ops = tuple(x[1:-1, 1:-1] for x in (east_w, west_w, south_w, north_w, diag_wide))

    def coarse_solve(rhs_vec):
        if not whole:
            got = gather_strip(jnp.stack([coarse_edges[0], coarse_edges[2], rhs_vec]))
            east_s, south_s = got[0], got[1]
            whole["levels"] = build_levels(east_s, shifted(east_s, 1), south_s, shifted(south_s, 0),
                                           GATHER_LEVEL, LEVELS)[0]
            strip_rhs = got[2]
        else:
            strip_rhs = gather_strip(rhs_vec[None])[0]
        strip_x = vcycle(strip_rhs, GATHER_LEVEL, whole["levels"], apply_padded, None)
        strip_x = jnp.pad(strip_x, ((1, 1), (0, 0)))
        return lax.dynamic_slice(strip_x, (segment_ordinal * block_h, block_w - 1),
                                 (block_h + 2, block_w + 2))

    def precondition(rhs_vec, rhs_wide=None):
        if rhs_wide is None:
            rhs_wide = extended(rhs_vec, 2)
        estimate = OMEGA * rhs_wide / diag_wide
        remain = rhs_vec - apply_inner(estimate[1:-1, 1:-1], levels[0])
        estimate = estimate + prolong_copy(coarse_solve(restrict_sum(remain)))
        ring = estimate[1:-1, 1:-1] + OMEGA * (rhs_wide[1:-1, 1:-1] - apply_inner(estimate, ring_ops)) / ring_ops[4]
        return ring[1:-1, 1:-1], apply_inner(ring, levels[0])

    solution = jnp.zeros_like(rhs)
    residual = rhs
    precond, image_vec = precondition(residual, rhs_wide)
    direction = precond
    sums = total(jnp.stack([jnp.sum(residual * precond), jnp.sum(direction * image_vec)]))
    norm_now = sums[0]
    curvature = sums[1]
    for step_index in range(ITERS):
        step_length = norm_now / curvature
        solution = solution + step_length * direction
        if step_index + 1 < ITERS:
            residual = residual - step_length * image_vec
            precond, image_z = precondition(residual)
            sums = total(jnp.stack([jnp.sum(residual * precond), jnp.sum(precond * image_z),
                                    jnp.sum(precond * image_vec)]))
            norm_next = sums[0]
            ratio = norm_next / norm_now
            direction = precond + ratio * direction
            image_vec = image_z + ratio * image_vec
            curvature = sums[1] + 2.0 * ratio * sums[2] + ratio * ratio * curvature
            norm_now = norm_next
    return (solution, weight)


def solution(mesh):
    return jax.shard_map(
        local,
        mesh=mesh,
        in_specs=(P(None, ("az", "rg"), None), P(None, ("az", "rg"), None), P(), P()),
        out_specs=(P("az", "rg"), P("az", "rg")),
        check_vma=False,
    )
```

```python
import jax
import jax.numpy as jnp
from jax import lax
from jax.sharding import PartitionSpec as P

LOOK = 5
LEVELS = 6
ITERS = 3
SWEEPS = 4
SEGMENT_HEIGHT = 160
GATHER_LEVEL = 1


OMEGA = 0.6
MU = 0.01


def neighbours(v):
    n_az = lax.axis_size("az")
    n_rg = lax.axis_size("rg")
    above = lax.ppermute(v[..., -1:, :], "az", [(i, i + 1) for i in range(n_az - 1)])
    below = lax.ppermute(v[..., :1, :], "az", [(i + 1, i) for i in range(n_az - 1)])
    left = lax.ppermute(v[..., :, -1:], "rg", [(i, i + 1) for i in range(n_rg - 1)])
    right = lax.ppermute(v[..., :, :1], "rg", [(i + 1, i) for i in range(n_rg - 1)])
    north = jnp.concatenate([above, v[..., :-1, :]], axis=-2)
    south = jnp.concatenate([v[..., 1:, :], below], axis=-2)
    west = jnp.concatenate([left, v[..., :, :-1]], axis=-1)
    east = jnp.concatenate([v[..., :, 1:], right], axis=-1)
    return north, south, west, east


def apply_halo(vector, operators):
    east, west, south, north, diagonal = operators
    v_n, v_s, v_w, v_e = neighbours(vector)
    return diagonal * vector - east * v_e - west * v_w - south * v_s - north * v_n


def extended(v, width):
    n_az = lax.axis_size("az")
    n_rg = lax.axis_size("rg")
    above = lax.ppermute(v[..., -width:, :], "az", [(i, i + 1) for i in range(n_az - 1)])
    below = lax.ppermute(v[..., :width, :], "az", [(i + 1, i) for i in range(n_az - 1)])
    v = jnp.concatenate([above, v, below], axis=-2)
    left = lax.ppermute(v[..., :, -width:], "rg", [(i, i + 1) for i in range(n_rg - 1)])
    right = lax.ppermute(v[..., :, :width], "rg", [(i + 1, i) for i in range(n_rg - 1)])
    return jnp.concatenate([left, v, right], axis=-1)


def apply_inner(padded, operators):
    east, west, south, north, diagonal = operators
    return (diagonal * padded[1:-1, 1:-1] - east * padded[1:-1, 2:] - west * padded[1:-1, :-2]
            - south * padded[2:, 1:-1] - north * padded[:-2, 1:-1])


def apply_padded(vector, operators):
    east, west, south, north, diagonal = operators
    padded = jnp.pad(vector, 1)
    return (diagonal * vector - east * padded[1:-1, 2:] - west * padded[1:-1, :-2]
            - south * padded[2:, 1:-1] - north * padded[:-2, 1:-1])


def mean_multilook(leading, trailing, row_ok, col_ok):
    valid_mask = (row_ok[:, None] & col_ok[None, :]).astype(jnp.float32)
    first_re = leading[0].astype(jnp.float32) * valid_mask
    first_im = leading[1].astype(jnp.float32) * valid_mask
    second_re = trailing[0].astype(jnp.float32) * valid_mask
    second_im = trailing[1].astype(jnp.float32) * valid_mask
    products = jnp.stack(
        [
            first_re * second_re + first_im * second_im,
            first_im * second_re - first_re * second_im,
            first_re * first_re + first_im * first_im,
            second_re * second_re + second_im * second_im,
        ]
    )
    height_rows, width_cols = valid_mask.shape
    span = LOOK * 128
    grouped = products.reshape(4, height_rows, width_cols // span, span)
    cols = jnp.einsum("pikc,cd->pikd", grouped, group_sum(span, LOOK).T, precision=HIGHEST)
    cols = cols.reshape(4, height_rows, width_cols // LOOK)
    return jnp.einsum("ri,pic->prc", group_sum(height_rows, LOOK), cols, precision=HIGHEST)


def edge_terms(left_re, left_im, left_weight, right_re, right_im, right_weight):
    edge_weight = 0.5 * (left_weight + right_weight)
    cross_im = right_im * left_re - right_re * left_im
    power_sum = (
        left_re * left_re + left_im * left_im + right_re * right_re + right_im * right_im + 1.0
    )
    return (edge_weight, 2.0 * cross_im / power_sum)


HIGHEST = lax.Precision.HIGHEST


def group_sum(n, size):
    group = lax.broadcasted_iota(jnp.int32, (n // size, n), 0)
    cell = lax.broadcasted_iota(jnp.int32, (n // size, n), 1)
    return (cell // size == group).astype(jnp.float32)


def pick(n, offset):
    group = lax.broadcasted_iota(jnp.int32, (n // 2, n), 0)
    cell = lax.broadcasted_iota(jnp.int32, (n // 2, n), 1)
    return (cell == 2 * group + offset).astype(jnp.float32)


def sandwich(left, vector, right):
    inner = jnp.dot(left, vector, precision=HIGHEST)
    return jnp.dot(inner, right, precision=HIGHEST)


def restrict_sum(vector):
    rows_now, cols_now = vector.shape
    return sandwich(group_sum(rows_now, 2), vector, group_sum(cols_now, 2).T)


def prolong_copy(vector):
    rows_now, cols_now = vector.shape
    return sandwich(group_sum(2 * rows_now, 2).T, vector, group_sum(2 * cols_now, 2))


def coarsen(east, west, south, north):
    rows_now, cols_now = east.shape
    row_sum = group_sum(rows_now, 2)
    col_sum = group_sum(cols_now, 2).T
    return (
        sandwich(row_sum, east, pick(cols_now, 1).T),
        sandwich(row_sum, west, pick(cols_now, 0).T),
        sandwich(pick(rows_now, 1), south, col_sum),
        sandwich(pick(rows_now, 0), north, col_sum),
    )


def build_levels(east, west, south, north, first_level, last_level):
    levels = {}
    for level in range(first_level, last_level):
        diagonal = east + west + south + north + MU * 4.0**level
        levels[level] = (east, west, south, north, diagonal)
        if level + 1 < LEVELS:
            east, west, south, north = coarsen(east, west, south, north)
    return levels, (east, west, south, north)


def jacobi_sweeps(rhs_vec, operators, apply_fn):
    estimate = OMEGA * rhs_vec / operators[4]
    for sweep_index in range(SWEEPS - 1):
        estimate = estimate + OMEGA * (rhs_vec - apply_fn(estimate, operators)) / operators[4]
    return estimate


def vcycle(rhs_vec, level, levels, apply_fn, stop_fn):
    if level == LEVELS - 1:
        return jacobi_sweeps(rhs_vec, levels[level], apply_fn)
    if stop_fn is not None and level == GATHER_LEVEL:
        return stop_fn(rhs_vec)
    diagonal = levels[level][4]
    estimate = OMEGA * rhs_vec / diagonal
    remain = rhs_vec - apply_fn(estimate, levels[level])
    correction = vcycle(restrict_sum(remain), level + 1, levels, apply_fn, stop_fn)
    estimate = estimate + prolong_copy(correction)
    return estimate + OMEGA * (rhs_vec - apply_fn(estimate, levels[level])) / diagonal


def everyone():
    return lax.axis_size("az") * lax.axis_size("rg")


def gather_strip(blocks):
    n_az = lax.axis_size("az")
    n_rg = lax.axis_size("rg")
    count, h, w = blocks.shape
    sent = jnp.broadcast_to(blocks[None], (n_az, count, h, w))
    got = lax.all_to_all(sent, "az", 0, 0, tiled=True)
    column = got.transpose(1, 0, 2, 3).reshape(count, n_az * h, w)
    left = lax.ppermute(column, "rg", [(i, i + 1) for i in range(n_rg - 1)])
    right = lax.ppermute(column, "rg", [(i + 1, i) for i in range(n_rg - 1)])
    return jnp.concatenate([left, column, right], axis=-1)


def shifted(values, axis):
    pad = [(0, 0)] * values.ndim
    pad[axis] = (1, 0)
    return lax.slice_in_dim(jnp.pad(values, pad), 0, values.shape[axis], axis=axis)


def total(values):
    n = everyone()
    sent = jnp.broadcast_to(values[None], (n, values.shape[0]))
    got = lax.all_to_all(sent, ("az", "rg"), 0, 0, tiled=True)
    return jnp.sum(got, axis=0)


def local(master_phasor_raster, slave_phasor_raster, segment_track_trim, segment_slant_trim):
    n_az = lax.axis_size("az")
    n_range = lax.axis_size("rg")
    segment_ordinal = lax.axis_index("az")
    range_index = lax.axis_index("rg")
    track_trim_width = lax.dynamic_index_in_dim(
        segment_track_trim, segment_ordinal, 0, keepdims=False
    )
    slant_trim_width = lax.dynamic_index_in_dim(
        segment_slant_trim, segment_ordinal, 0, keepdims=False
    )
    lines_here = master_phasor_raster.shape[1]
    slant_sample_total = master_phasor_raster.shape[2]
    along_track_position = range_index * lines_here + jnp.arange(lines_here, dtype=jnp.int32)
    column_index = jnp.arange(slant_sample_total, dtype=jnp.int32)
    row_ok = (along_track_position >= track_trim_width[0]) & (
        along_track_position < SEGMENT_HEIGHT - track_trim_width[1]
    )
    col_ok = (column_index >= slant_trim_width[0]) & (
        column_index < slant_sample_total - slant_trim_width[1]
    )
    pixel_totals = mean_multilook(master_phasor_raster, slave_phasor_raster, row_ok, col_ok)
    look_re, look_im, power_one, power_two = (
        pixel_totals[0],
        pixel_totals[1],
        pixel_totals[2],
        pixel_totals[3],
    )
    weight = 0.05 + 4.0 * (look_re * look_re + look_im * look_im) / jnp.maximum(
        power_one * power_two, 1.0
    )
    border = 3
    fields = jnp.stack([look_re, look_im, weight])
    n_fields, rows_here, cols_all = fields.shape
    cols_here = cols_all // n_range
    fields = jnp.pad(fields, ((0, 0), (0, 0), (border, border)))
    fields = jnp.stack([fields[:, :, c * cols_here:(c + 1) * cols_here + 2 * border] for c in range(n_range)])
    fields = lax.all_to_all(fields, "rg", 0, 0, tiled=True)
    fields = fields.transpose(1, 0, 2, 3).reshape(n_fields, n_range * rows_here, cols_here + 2 * border)
    shard_height_total = n_range * rows_here
    above = lax.ppermute(fields[:, -border:, :], "az", [(i, i + 1) for i in range(n_az - 1)])
    below = lax.ppermute(fields[:, :border, :], "az", [(i + 1, i) for i in range(n_az - 1)])
    fields = jnp.concatenate([above, fields, below], axis=1)
    weight = fields[2, border:-border, border:-border]

    row_global = segment_ordinal * shard_height_total - border + jnp.arange(
        shard_height_total + 2 * border, dtype=jnp.int32)
    col_global = range_index * cols_here - border + jnp.arange(cols_here + 2 * border, dtype=jnp.int32)
    edge_h, grad_h = edge_terms(fields[0, :, :-1], fields[1, :, :-1], fields[2, :, :-1],
                                fields[0, :, 1:], fields[1, :, 1:], fields[2, :, 1:])
    keep_h = ((col_global[:-1] >= 0) & (col_global[:-1] <= cols_here * n_range - 2)).astype(jnp.float32)
    edge_h = edge_h * keep_h[None, :]
    edge_v, grad_v = edge_terms(fields[0, :-1], fields[1, :-1], fields[2, :-1],
                                fields[0, 1:], fields[1, 1:], fields[2, 1:])
    keep_v = ((row_global[:-1] >= 0) & (row_global[:-1] <= shard_height_total * n_az - 2)).astype(jnp.float32)
    edge_v = edge_v * keep_v[:, None]
    flux_h = edge_h * grad_h
    flux_v = edge_v * grad_v
    east_w = edge_h[1:-1, 1:]
    west_w = edge_h[1:-1, :-1]
    south_w = edge_v[1:, 1:-1]
    north_w = edge_v[:-1, 1:-1]
    diag_wide = east_w + west_w + south_w + north_w + MU * 4.0**0
    rhs_wide = -(flux_h[1:-1, 1:] - flux_h[1:-1, :-1] + flux_v[1:, 1:-1] - flux_v[:-1, 1:-1])
    rhs = rhs_wide[2:-2, 2:-2]
    own = (slice(2, -2), slice(2, -2))
    levels, coarse_edges = build_levels(east_w[own], west_w[own], south_w[own], north_w[own],
                                        first_level=0, last_level=GATHER_LEVEL)
    block_h, block_w = coarse_edges[0].shape
    whole = {}

    ring_ops = tuple(x[1:-1, 1:-1] for x in (east_w, west_w, south_w, north_w, diag_wide))

    def coarse_solve(rhs_vec):
        if not whole:
            got = gather_strip(jnp.stack([coarse_edges[0], coarse_edges[2], rhs_vec]))
            east_s, south_s = got[0], got[1]
            whole["levels"] = build_levels(east_s, shifted(east_s, 1), south_s, shifted(south_s, 0),
                                           GATHER_LEVEL, LEVELS)[0]
            strip_rhs = got[2]
        else:
            strip_rhs = gather_strip(rhs_vec[None])[0]
        strip_x = vcycle(strip_rhs, GATHER_LEVEL, whole["levels"], apply_padded, None)
        strip_x = jnp.pad(strip_x, ((1, 1), (0, 0)))
        return lax.dynamic_slice(strip_x, (segment_ordinal * block_h, block_w - 1),
                                 (block_h + 2, block_w + 2))

    def precondition(rhs_vec, rhs_wide=None):
        if rhs_wide is None:
            rhs_wide = extended(rhs_vec, 2)
        estimate = OMEGA * rhs_wide / diag_wide
        remain = rhs_vec - apply_inner(estimate[1:-1, 1:-1], levels[0])
        estimate = estimate + prolong_copy(coarse_solve(restrict_sum(remain)))
        ring = estimate[1:-1, 1:-1] + OMEGA * (rhs_wide[1:-1, 1:-1] - apply_inner(estimate, ring_ops)) / ring_ops[4]
        return ring[1:-1, 1:-1], apply_inner(ring, levels[0])

    solution = jnp.zeros_like(rhs)
    residual = rhs
    residual_wide = rhs_wide
    precond, image_vec = precondition(residual, residual_wide)
    image_wide = extended(image_vec, 2) if ITERS > 1 else None
    direction = precond
    sums = total(jnp.stack([jnp.sum(residual * precond), jnp.sum(direction * image_vec)]))
    norm_now = sums[0]
    curvature = sums[1]
    for step_index in range(ITERS):
        step_length = norm_now / curvature
        solution = solution + step_length * direction
        if step_index + 1 < ITERS:
            residual_wide = residual_wide - step_length * image_wide
            residual = residual_wide[2:-2, 2:-2]
            precond, image_z = precondition(residual, residual_wide)
            image_z_wide = extended(image_z, 2) if step_index + 2 < ITERS else None
            sums = total(jnp.stack([jnp.sum(residual * precond), jnp.sum(precond * image_z),
                                    jnp.sum(precond * image_vec)]))
            norm_next = sums[0]
            ratio = norm_next / norm_now
            direction = precond + ratio * direction
            image_vec = image_z + ratio * image_vec
            if image_z_wide is not None:
                image_wide = image_z_wide + ratio * image_wide
            curvature = sums[1] + 2.0 * ratio * sums[2] + ratio * ratio * curvature
            norm_now = norm_next
    return (solution, weight)


def solution(mesh):
    return jax.shard_map(
        local,
        mesh=mesh,
        in_specs=(P(None, ("az", "rg"), None), P(None, ("az", "rg"), None), P(), P()),
        out_specs=(P("az", "rg"), P("az", "rg")),
        check_vma=False,
    )
```

```python
import jax
import jax.numpy as jnp
from jax import lax
from jax.sharding import PartitionSpec as P

LOOK = 5
LEVELS = 6
ITERS = 3
SWEEPS = 4
SEGMENT_HEIGHT = 160
GATHER_LEVEL = 1


OMEGA = 0.6
MU = 0.01


def neighbours(v):
    n_az = lax.axis_size("az")
    n_rg = lax.axis_size("rg")
    above = lax.ppermute(v[..., -1:, :], "az", [(i, i + 1) for i in range(n_az - 1)])
    below = lax.ppermute(v[..., :1, :], "az", [(i + 1, i) for i in range(n_az - 1)])
    left = lax.ppermute(v[..., :, -1:], "rg", [(i, i + 1) for i in range(n_rg - 1)])
    right = lax.ppermute(v[..., :, :1], "rg", [(i + 1, i) for i in range(n_rg - 1)])
    north = jnp.concatenate([above, v[..., :-1, :]], axis=-2)
    south = jnp.concatenate([v[..., 1:, :], below], axis=-2)
    west = jnp.concatenate([left, v[..., :, :-1]], axis=-1)
    east = jnp.concatenate([v[..., :, 1:], right], axis=-1)
    return north, south, west, east


def apply_halo(vector, operators):
    east, west, south, north, diagonal = operators
    v_n, v_s, v_w, v_e = neighbours(vector)
    return diagonal * vector - east * v_e - west * v_w - south * v_s - north * v_n


def extended(v, width):
    n_az = lax.axis_size("az")
    n_rg = lax.axis_size("rg")
    above = lax.ppermute(v[..., -width:, :], "az", [(i, i + 1) for i in range(n_az - 1)])
    below = lax.ppermute(v[..., :width, :], "az", [(i + 1, i) for i in range(n_az - 1)])
    v = jnp.concatenate([above, v, below], axis=-2)
    left = lax.ppermute(v[..., :, -width:], "rg", [(i, i + 1) for i in range(n_rg - 1)])
    right = lax.ppermute(v[..., :, :width], "rg", [(i + 1, i) for i in range(n_rg - 1)])
    return jnp.concatenate([left, v, right], axis=-1)


def apply_inner(padded, operators):
    east, west, south, north, diagonal = operators
    return (diagonal * padded[1:-1, 1:-1] - east * padded[1:-1, 2:] - west * padded[1:-1, :-2]
            - south * padded[2:, 1:-1] - north * padded[:-2, 1:-1])


def apply_padded(vector, operators):
    east, west, south, north, diagonal = operators
    padded = jnp.pad(vector, 1)
    return (diagonal * vector - east * padded[1:-1, 2:] - west * padded[1:-1, :-2]
            - south * padded[2:, 1:-1] - north * padded[:-2, 1:-1])


def mean_multilook(leading, trailing, row_ok, col_ok):
    valid_mask = (row_ok[:, None] & col_ok[None, :]).astype(jnp.float32)
    first_re = leading[0].astype(jnp.float32) * valid_mask
    first_im = leading[1].astype(jnp.float32) * valid_mask
    second_re = trailing[0].astype(jnp.float32) * valid_mask
    second_im = trailing[1].astype(jnp.float32) * valid_mask
    products = jnp.stack(
        [
            first_re * second_re + first_im * second_im,
            first_im * second_re - first_re * second_im,
            first_re * first_re + first_im * first_im,
            second_re * second_re + second_im * second_im,
        ]
    )
    height_rows, width_cols = valid_mask.shape
    span = LOOK * 128
    grouped = products.reshape(4, height_rows, width_cols // span, span)
    cols = jnp.einsum("pikc,cd->pikd", grouped, group_sum(span, LOOK).T, precision=HIGHEST)
    cols = cols.reshape(4, height_rows, width_cols // LOOK)
    return jnp.einsum("ri,pic->prc", group_sum(height_rows, LOOK), cols, precision=HIGHEST)


def edge_terms(left_re, left_im, left_weight, right_re, right_im, right_weight):
    edge_weight = 0.5 * (left_weight + right_weight)
    cross_im = right_im * left_re - right_re * left_im
    power_sum = (
        left_re * left_re + left_im * left_im + right_re * right_re + right_im * right_im + 1.0
    )
    return (edge_weight, 2.0 * cross_im / power_sum)


HIGHEST = lax.Precision.HIGHEST


def group_sum(n, size):
    group = lax.broadcasted_iota(jnp.int32, (n // size, n), 0)
    cell = lax.broadcasted_iota(jnp.int32, (n // size, n), 1)
    return (cell // size == group).astype(jnp.float32)


def pick(n, offset):
    group = lax.broadcasted_iota(jnp.int32, (n // 2, n), 0)
    cell = lax.broadcasted_iota(jnp.int32, (n // 2, n), 1)
    return (cell == 2 * group + offset).astype(jnp.float32)


def sandwich(left, vector, right):
    inner = jnp.dot(left, vector, precision=HIGHEST)
    return jnp.dot(inner, right, precision=HIGHEST)


def restrict_sum(vector):
    rows_now, cols_now = vector.shape
    return sandwich(group_sum(rows_now, 2), vector, group_sum(cols_now, 2).T)


def prolong_copy(vector):
    rows_now, cols_now = vector.shape
    return sandwich(group_sum(2 * rows_now, 2).T, vector, group_sum(2 * cols_now, 2))


def coarsen(east, west, south, north):
    rows_now, cols_now = east.shape
    row_sum = group_sum(rows_now, 2)
    col_sum = group_sum(cols_now, 2).T
    return (
        sandwich(row_sum, east, pick(cols_now, 1).T),
        sandwich(row_sum, west, pick(cols_now, 0).T),
        sandwich(pick(rows_now, 1), south, col_sum),
        sandwich(pick(rows_now, 0), north, col_sum),
    )


def build_levels(east, west, south, north, first_level, last_level):
    levels = {}
    for level in range(first_level, last_level):
        diagonal = east + west + south + north + MU * 4.0**level
        levels[level] = (east, west, south, north, diagonal)
        if level + 1 < LEVELS:
            east, west, south, north = coarsen(east, west, south, north)
    return levels, (east, west, south, north)


def jacobi_sweeps(rhs_vec, operators, apply_fn):
    estimate = OMEGA * rhs_vec / operators[4]
    for sweep_index in range(SWEEPS - 1):
        estimate = estimate + OMEGA * (rhs_vec - apply_fn(estimate, operators)) / operators[4]
    return estimate


def vcycle(rhs_vec, level, levels, apply_fn, stop_fn):
    if level == LEVELS - 1:
        return jacobi_sweeps(rhs_vec, levels[level], apply_fn)
    if stop_fn is not None and level == GATHER_LEVEL:
        return stop_fn(rhs_vec)
    diagonal = levels[level][4]
    estimate = OMEGA * rhs_vec / diagonal
    remain = rhs_vec - apply_fn(estimate, levels[level])
    correction = vcycle(restrict_sum(remain), level + 1, levels, apply_fn, stop_fn)
    estimate = estimate + prolong_copy(correction)
    return estimate + OMEGA * (rhs_vec - apply_fn(estimate, levels[level])) / diagonal


def everyone():
    return lax.axis_size("az") * lax.axis_size("rg")


def gather_strip(blocks):
    n_az = lax.axis_size("az")
    n_rg = lax.axis_size("rg")
    count, h, w = blocks.shape
    sent = jnp.broadcast_to(blocks[None], (n_az, count, h, w))
    got = lax.all_to_all(sent, "az", 0, 0, tiled=True)
    column = got.transpose(1, 0, 2, 3).reshape(count, n_az * h, w)
    left = lax.ppermute(column, "rg", [(i, i + 1) for i in range(n_rg - 1)])
    right = lax.ppermute(column, "rg", [(i + 1, i) for i in range(n_rg - 1)])
    return jnp.concatenate([left, column, right], axis=-1)


def shifted(values, axis):
    pad = [(0, 0)] * values.ndim
    pad[axis] = (1, 0)
    return lax.slice_in_dim(jnp.pad(values, pad), 0, values.shape[axis], axis=axis)


def total(values):
    n = everyone()
    sent = jnp.broadcast_to(values[None], (n, values.shape[0]))
    got = lax.all_to_all(sent, ("az", "rg"), 0, 0, tiled=True)
    return jnp.sum(got, axis=0)


def local(master_phasor_raster, slave_phasor_raster, segment_track_trim, segment_slant_trim):
    n_az = lax.axis_size("az")
    n_range = lax.axis_size("rg")
    segment_ordinal = lax.axis_index("az")
    range_index = lax.axis_index("rg")
    track_trim_width = lax.dynamic_index_in_dim(
        segment_track_trim, segment_ordinal, 0, keepdims=False
    )
    slant_trim_width = lax.dynamic_index_in_dim(
        segment_slant_trim, segment_ordinal, 0, keepdims=False
    )
    lines_here = master_phasor_raster.shape[1]
    slant_sample_total = master_phasor_raster.shape[2]
    along_track_position = range_index * lines_here + jnp.arange(lines_here, dtype=jnp.int32)
    column_index = jnp.arange(slant_sample_total, dtype=jnp.int32)
    row_ok = (along_track_position >= track_trim_width[0]) & (
        along_track_position < SEGMENT_HEIGHT - track_trim_width[1]
    )
    col_ok = (column_index >= slant_trim_width[0]) & (
        column_index < slant_sample_total - slant_trim_width[1]
    )
    pixel_totals = mean_multilook(master_phasor_raster, slave_phasor_raster, row_ok, col_ok)
    look_re, look_im, power_one, power_two = (
        pixel_totals[0],
        pixel_totals[1],
        pixel_totals[2],
        pixel_totals[3],
    )
    weight = 0.05 + 4.0 * (look_re * look_re + look_im * look_im) / jnp.maximum(
        power_one * power_two, 1.0
    )
    widest = 2 * ITERS
    border = widest + 1
    fields = jnp.stack([look_re, look_im, weight])
    n_fields, rows_here, cols_all = fields.shape
    cols_here = cols_all // n_range
    fields = jnp.pad(fields, ((0, 0), (0, 0), (border, border)))
    fields = jnp.stack([fields[:, :, c * cols_here:(c + 1) * cols_here + 2 * border] for c in range(n_range)])
    fields = lax.all_to_all(fields, "rg", 0, 0, tiled=True)
    fields = fields.transpose(1, 0, 2, 3).reshape(n_fields, n_range * rows_here, cols_here + 2 * border)
    shard_height_total = n_range * rows_here
    above = lax.ppermute(fields[:, -border:, :], "az", [(i, i + 1) for i in range(n_az - 1)])
    below = lax.ppermute(fields[:, :border, :], "az", [(i + 1, i) for i in range(n_az - 1)])
    fields = jnp.concatenate([above, fields, below], axis=1)
    weight = fields[2, border:-border, border:-border]

    row_global = segment_ordinal * shard_height_total - border + jnp.arange(
        shard_height_total + 2 * border, dtype=jnp.int32)
    col_global = range_index * cols_here - border + jnp.arange(cols_here + 2 * border, dtype=jnp.int32)
    edge_h, grad_h = edge_terms(fields[0, :, :-1], fields[1, :, :-1], fields[2, :, :-1],
                                fields[0, :, 1:], fields[1, :, 1:], fields[2, :, 1:])
    keep_h = ((col_global[:-1] >= 0) & (col_global[:-1] <= cols_here * n_range - 2)).astype(jnp.float32)
    edge_h = edge_h * keep_h[None, :]
    edge_v, grad_v = edge_terms(fields[0, :-1], fields[1, :-1], fields[2, :-1],
                                fields[0, 1:], fields[1, 1:], fields[2, 1:])
    keep_v = ((row_global[:-1] >= 0) & (row_global[:-1] <= shard_height_total * n_az - 2)).astype(jnp.float32)
    edge_v = edge_v * keep_v[:, None]
    flux_h = edge_h * grad_h
    flux_v = edge_v * grad_v
    east_w = edge_h[1:-1, 1:]
    west_w = edge_h[1:-1, :-1]
    south_w = edge_v[1:, 1:-1]
    north_w = edge_v[:-1, 1:-1]
    diag_w = east_w + west_w + south_w + north_w + MU * 4.0**0
    ops_w = (east_w, west_w, south_w, north_w, diag_w)
    rhs_wide = -(flux_h[1:-1, 1:] - flux_h[1:-1, :-1] + flux_v[1:, 1:-1] - flux_v[:-1, 1:-1])

    def crop(values, ring):
        cut = (values.shape[-2] - shard_height_total) // 2 - ring
        if cut == 0:
            return values
        return values[..., cut:-cut, cut:-cut]

    def ops_at(ring):
        return tuple(crop(x, ring) for x in ops_w)

    levels, coarse_edges = build_levels(*ops_at(0)[:4], first_level=0, last_level=GATHER_LEVEL)
    block_h, block_w = coarse_edges[0].shape
    whole = {}

    def coarse_solve(rhs_vec, ring):
        if not whole:
            got = gather_strip(jnp.stack([coarse_edges[0], coarse_edges[2], rhs_vec]))
            east_s, south_s = got[0], got[1]
            whole["levels"] = build_levels(east_s, shifted(east_s, 1), south_s, shifted(south_s, 0),
                                           GATHER_LEVEL, LEVELS)[0]
            strip_rhs = got[2]
        else:
            strip_rhs = gather_strip(rhs_vec[None])[0]
        strip_x = vcycle(strip_rhs, GATHER_LEVEL, whole["levels"], apply_padded, None)
        coarse_ring = ring // 2
        strip_x = jnp.pad(strip_x, ((coarse_ring, coarse_ring), (0, 0)))
        return lax.dynamic_slice(strip_x, (segment_ordinal * block_h, block_w - coarse_ring),
                                 (block_h + 2 * coarse_ring, block_w + 2 * coarse_ring))

    def precondition(rhs_wide):
        ring = (rhs_wide.shape[0] - shard_height_total) // 2
        diag_here = ops_at(ring)[4]
        estimate = OMEGA * rhs_wide / diag_here
        remain = crop(rhs_wide, 0) - apply_inner(crop(estimate, 1), levels[0])
        estimate = estimate + prolong_copy(coarse_solve(restrict_sum(remain), ring))
        inner = ops_at(ring - 1)
        smoothed = crop(estimate, ring - 1) + OMEGA * (crop(rhs_wide, ring - 1) - apply_inner(estimate, inner)) / inner[4]
        return smoothed, apply_inner(smoothed, ops_at(ring - 2))

    residual_wide = rhs_wide
    precond, image_vec = precondition(residual_wide)
    direction = precond
    sums = total(jnp.stack([jnp.sum(crop(residual_wide, 0) * crop(precond, 0)),
                            jnp.sum(crop(direction, 0) * crop(image_vec, 0))]))
    norm_now = sums[0]
    curvature = sums[1]
    solution = jnp.zeros_like(crop(rhs_wide, 0))
    for step_index in range(ITERS):
        step_length = norm_now / curvature
        solution = solution + step_length * crop(direction, 0)
        if step_index + 1 < ITERS:
            ring = (image_vec.shape[0] - shard_height_total) // 2
            residual_wide = crop(residual_wide, ring) - step_length * image_vec
            precond, image_z = precondition(residual_wide)
            sums = total(jnp.stack([jnp.sum(crop(residual_wide, 0) * crop(precond, 0)),
                                    jnp.sum(crop(precond, 0) * crop(image_z, 0)),
                                    jnp.sum(crop(precond, 0) * crop(image_vec, 0))]))
            norm_next = sums[0]
            ratio = norm_next / norm_now
            direction = precond + ratio * crop(direction, ring - 1)
            image_vec = image_z + ratio * crop(image_vec, ring - 2)
            curvature = sums[1] + 2.0 * ratio * sums[2] + ratio * ratio * curvature
            norm_now = norm_next
    return (solution, weight)


def solution(mesh):
    return jax.shard_map(
        local,
        mesh=mesh,
        in_specs=(P(None, ("az", "rg"), None), P(None, ("az", "rg"), None), P(), P()),
        out_specs=(P("az", "rg"), P("az", "rg")),
        check_vma=False,
    )
```

```python
import jax
import jax.numpy as jnp
from jax import lax
from jax.sharding import PartitionSpec as P

LOOK = 5
LEVELS = 6
ITERS = 3
SWEEPS = 4
SEGMENT_HEIGHT = 160
GATHER_LEVEL = 1


OMEGA = 0.6
MU = 0.01


def neighbours(v):
    n_az = lax.axis_size("az")
    n_rg = lax.axis_size("rg")
    above = lax.ppermute(v[..., -1:, :], "az", [(i, i + 1) for i in range(n_az - 1)])
    below = lax.ppermute(v[..., :1, :], "az", [(i + 1, i) for i in range(n_az - 1)])
    left = lax.ppermute(v[..., :, -1:], "rg", [(i, i + 1) for i in range(n_rg - 1)])
    right = lax.ppermute(v[..., :, :1], "rg", [(i + 1, i) for i in range(n_rg - 1)])
    north = jnp.concatenate([above, v[..., :-1, :]], axis=-2)
    south = jnp.concatenate([v[..., 1:, :], below], axis=-2)
    west = jnp.concatenate([left, v[..., :, :-1]], axis=-1)
    east = jnp.concatenate([v[..., :, 1:], right], axis=-1)
    return north, south, west, east


def apply_halo(vector, operators):
    east, west, south, north, diagonal = operators
    v_n, v_s, v_w, v_e = neighbours(vector)
    return diagonal * vector - east * v_e - west * v_w - south * v_s - north * v_n


def extended(v, width):
    n_az = lax.axis_size("az")
    n_rg = lax.axis_size("rg")
    above = lax.ppermute(v[..., -width:, :], "az", [(i, i + 1) for i in range(n_az - 1)])
    below = lax.ppermute(v[..., :width, :], "az", [(i + 1, i) for i in range(n_az - 1)])
    v = jnp.concatenate([above, v, below], axis=-2)
    left = lax.ppermute(v[..., :, -width:], "rg", [(i, i + 1) for i in range(n_rg - 1)])
    right = lax.ppermute(v[..., :, :width], "rg", [(i + 1, i) for i in range(n_rg - 1)])
    return jnp.concatenate([left, v, right], axis=-1)


def apply_inner(padded, operators):
    east, west, south, north, diagonal = operators
    return (diagonal * padded[1:-1, 1:-1] - east * padded[1:-1, 2:] - west * padded[1:-1, :-2]
            - south * padded[2:, 1:-1] - north * padded[:-2, 1:-1])


def apply_padded(vector, operators):
    east, west, south, north, diagonal = operators
    padded = jnp.pad(vector, 1)
    return (diagonal * vector - east * padded[1:-1, 2:] - west * padded[1:-1, :-2]
            - south * padded[2:, 1:-1] - north * padded[:-2, 1:-1])


def mean_multilook(leading, trailing, row_ok, col_ok):
    valid_mask = (row_ok[:, None] & col_ok[None, :]).astype(jnp.float32)
    first_re = leading[0].astype(jnp.float32) * valid_mask
    first_im = leading[1].astype(jnp.float32) * valid_mask
    second_re = trailing[0].astype(jnp.float32) * valid_mask
    second_im = trailing[1].astype(jnp.float32) * valid_mask
    products = jnp.stack(
        [
            first_re * second_re + first_im * second_im,
            first_im * second_re - first_re * second_im,
            first_re * first_re + first_im * first_im,
            second_re * second_re + second_im * second_im,
        ]
    )
    height_rows, width_cols = valid_mask.shape
    span = LOOK * 128
    grouped = products.reshape(4, height_rows, width_cols // span, span)
    cols = jnp.einsum("pikc,cd->pikd", grouped, group_sum(span, LOOK).T, precision=HIGHEST)
    cols = cols.reshape(4, height_rows, width_cols // LOOK)
    return jnp.einsum("ri,pic->prc", group_sum(height_rows, LOOK), cols, precision=HIGHEST)


def edge_terms(left_re, left_im, left_weight, right_re, right_im, right_weight):
    edge_weight = 0.5 * (left_weight + right_weight)
    cross_im = right_im * left_re - right_re * left_im
    power_sum = (
        left_re * left_re + left_im * left_im + right_re * right_re + right_im * right_im + 1.0
    )
    return (edge_weight, 2.0 * cross_im / power_sum)


HIGHEST = lax.Precision.HIGHEST


def group_sum(n, size):
    group = lax.broadcasted_iota(jnp.int32, (n // size, n), 0)
    cell = lax.broadcasted_iota(jnp.int32, (n // size, n), 1)
    return (cell // size == group).astype(jnp.float32)


def pick(n, offset):
    group = lax.broadcasted_iota(jnp.int32, (n // 2, n), 0)
    cell = lax.broadcasted_iota(jnp.int32, (n // 2, n), 1)
    return (cell == 2 * group + offset).astype(jnp.float32)


def sandwich(left, vector, right):
    inner = jnp.dot(left, vector, precision=HIGHEST)
    return jnp.dot(inner, right, precision=HIGHEST)


def restrict_sum(vector):
    rows_now, cols_now = vector.shape
    return sandwich(group_sum(rows_now, 2), vector, group_sum(cols_now, 2).T)


def prolong_copy(vector):
    rows_now, cols_now = vector.shape
    return sandwich(group_sum(2 * rows_now, 2).T, vector, group_sum(2 * cols_now, 2))


def coarsen(east, west, south, north):
    rows_now, cols_now = east.shape
    row_sum = group_sum(rows_now, 2)
    col_sum = group_sum(cols_now, 2).T
    return (
        sandwich(row_sum, east, pick(cols_now, 1).T),
        sandwich(row_sum, west, pick(cols_now, 0).T),
        sandwich(pick(rows_now, 1), south, col_sum),
        sandwich(pick(rows_now, 0), north, col_sum),
    )


def build_levels(east, west, south, north, first_level, last_level):
    levels = {}
    for level in range(first_level, last_level):
        diagonal = east + west + south + north + MU * 4.0**level
        levels[level] = (east, west, south, north, diagonal)
        if level + 1 < LEVELS:
            east, west, south, north = coarsen(east, west, south, north)
    return levels, (east, west, south, north)


def jacobi_sweeps(rhs_vec, operators, apply_fn):
    estimate = OMEGA * rhs_vec / operators[4]
    for sweep_index in range(SWEEPS - 1):
        estimate = estimate + OMEGA * (rhs_vec - apply_fn(estimate, operators)) / operators[4]
    return estimate


def vcycle(rhs_vec, level, levels, apply_fn, stop_fn):
    if level == LEVELS - 1:
        return jacobi_sweeps(rhs_vec, levels[level], apply_fn)
    if stop_fn is not None and level == GATHER_LEVEL:
        return stop_fn(rhs_vec)
    diagonal = levels[level][4]
    estimate = OMEGA * rhs_vec / diagonal
    remain = rhs_vec - apply_fn(estimate, levels[level])
    correction = vcycle(restrict_sum(remain), level + 1, levels, apply_fn, stop_fn)
    estimate = estimate + prolong_copy(correction)
    return estimate + OMEGA * (rhs_vec - apply_fn(estimate, levels[level])) / diagonal


def everyone():
    return lax.axis_size("az") * lax.axis_size("rg")


def gather_strip(blocks, sums=None):
    n_az = lax.axis_size("az")
    n_rg = lax.axis_size("rg")
    count, h, w = blocks.shape
    if sums is not None:
        extra = jnp.zeros((1, h, w), jnp.float32).at[0, 0, :sums.shape[0]].set(sums)
        blocks = jnp.concatenate([blocks, extra])
    sent = jnp.broadcast_to(blocks[None], (n_az,) + blocks.shape)
    got = lax.all_to_all(sent, "az", 0, 0, tiled=True)
    summed = None
    if sums is not None:
        column_sums = jnp.sum(got[:, count, 0, :sums.shape[0]], axis=0)
        rows = lax.all_to_all(jnp.broadcast_to(column_sums[None], (n_rg, sums.shape[0])), "rg", 0, 0, tiled=True)
        summed = jnp.sum(rows, axis=0)
        got = got[:, :count]
    column = got.transpose(1, 0, 2, 3).reshape(count, n_az * h, w)
    left = lax.ppermute(column, "rg", [(i, i + 1) for i in range(n_rg - 1)])
    right = lax.ppermute(column, "rg", [(i + 1, i) for i in range(n_rg - 1)])
    return jnp.concatenate([left, column, right], axis=-1), summed


def shifted(values, axis):
    pad = [(0, 0)] * values.ndim
    pad[axis] = (1, 0)
    return lax.slice_in_dim(jnp.pad(values, pad), 0, values.shape[axis], axis=axis)


def total(values):
    n = everyone()
    sent = jnp.broadcast_to(values[None], (n, values.shape[0]))
    got = lax.all_to_all(sent, ("az", "rg"), 0, 0, tiled=True)
    return jnp.sum(got, axis=0)


def local(master_phasor_raster, slave_phasor_raster, segment_track_trim, segment_slant_trim):
    n_az = lax.axis_size("az")
    n_range = lax.axis_size("rg")
    segment_ordinal = lax.axis_index("az")
    range_index = lax.axis_index("rg")
    track_trim_width = lax.dynamic_index_in_dim(
        segment_track_trim, segment_ordinal, 0, keepdims=False
    )
    slant_trim_width = lax.dynamic_index_in_dim(
        segment_slant_trim, segment_ordinal, 0, keepdims=False
    )
    lines_here = master_phasor_raster.shape[1]
    slant_sample_total = master_phasor_raster.shape[2]
    along_track_position = range_index * lines_here + jnp.arange(lines_here, dtype=jnp.int32)
    column_index = jnp.arange(slant_sample_total, dtype=jnp.int32)
    row_ok = (along_track_position >= track_trim_width[0]) & (
        along_track_position < SEGMENT_HEIGHT - track_trim_width[1]
    )
    col_ok = (column_index >= slant_trim_width[0]) & (
        column_index < slant_sample_total - slant_trim_width[1]
    )
    pixel_totals = mean_multilook(master_phasor_raster, slave_phasor_raster, row_ok, col_ok)
    look_re, look_im, power_one, power_two = (
        pixel_totals[0],
        pixel_totals[1],
        pixel_totals[2],
        pixel_totals[3],
    )
    weight = 0.05 + 4.0 * (look_re * look_re + look_im * look_im) / jnp.maximum(
        power_one * power_two, 1.0
    )
    widest = 2 * ITERS
    border = widest + 1
    fields = jnp.stack([look_re, look_im, weight])
    n_fields, rows_here, cols_all = fields.shape
    cols_here = cols_all // n_range
    fields = jnp.pad(fields, ((0, 0), (0, 0), (border, border)))
    fields = jnp.stack([fields[:, :, c * cols_here:(c + 1) * cols_here + 2 * border] for c in range(n_range)])
    fields = lax.all_to_all(fields, "rg", 0, 0, tiled=True)
    fields = fields.transpose(1, 0, 2, 3).reshape(n_fields, n_range * rows_here, cols_here + 2 * border)
    shard_height_total = n_range * rows_here
    above = lax.ppermute(fields[:, -border:, :], "az", [(i, i + 1) for i in range(n_az - 1)])
    below = lax.ppermute(fields[:, :border, :], "az", [(i + 1, i) for i in range(n_az - 1)])
    fields = jnp.concatenate([above, fields, below], axis=1)
    weight = fields[2, border:-border, border:-border]

    row_global = segment_ordinal * shard_height_total - border + jnp.arange(
        shard_height_total + 2 * border, dtype=jnp.int32)
    col_global = range_index * cols_here - border + jnp.arange(cols_here + 2 * border, dtype=jnp.int32)
    edge_h, grad_h = edge_terms(fields[0, :, :-1], fields[1, :, :-1], fields[2, :, :-1],
                                fields[0, :, 1:], fields[1, :, 1:], fields[2, :, 1:])
    keep_h = ((col_global[:-1] >= 0) & (col_global[:-1] <= cols_here * n_range - 2)).astype(jnp.float32)
    edge_h = edge_h * keep_h[None, :]
    edge_v, grad_v = edge_terms(fields[0, :-1], fields[1, :-1], fields[2, :-1],
                                fields[0, 1:], fields[1, 1:], fields[2, 1:])
    keep_v = ((row_global[:-1] >= 0) & (row_global[:-1] <= shard_height_total * n_az - 2)).astype(jnp.float32)
    edge_v = edge_v * keep_v[:, None]
    flux_h = edge_h * grad_h
    flux_v = edge_v * grad_v
    east_w = edge_h[1:-1, 1:]
    west_w = edge_h[1:-1, :-1]
    south_w = edge_v[1:, 1:-1]
    north_w = edge_v[:-1, 1:-1]
    diag_w = east_w + west_w + south_w + north_w + MU * 4.0**0
    ops_w = (east_w, west_w, south_w, north_w, diag_w)
    rhs_wide = -(flux_h[1:-1, 1:] - flux_h[1:-1, :-1] + flux_v[1:, 1:-1] - flux_v[:-1, 1:-1])

    def crop(values, ring):
        cut = (values.shape[-2] - shard_height_total) // 2 - ring
        if cut == 0:
            return values
        return values[..., cut:-cut, cut:-cut]

    def ops_at(ring):
        return tuple(crop(x, ring) for x in ops_w)

    levels, coarse_edges = build_levels(*ops_at(0)[:4], first_level=0, last_level=GATHER_LEVEL)
    block_h, block_w = coarse_edges[0].shape
    whole = {}

    def coarse_solve(rhs_vec, ring, sums):
        if not whole:
            got, summed = gather_strip(jnp.stack([coarse_edges[0], coarse_edges[2], rhs_vec]), sums)
            east_s, south_s = got[0], got[1]
            whole["levels"] = build_levels(east_s, shifted(east_s, 1), south_s, shifted(south_s, 0),
                                           GATHER_LEVEL, LEVELS)[0]
            strip_rhs = got[2]
        else:
            got, summed = gather_strip(rhs_vec[None], sums)
            strip_rhs = got[0]
        strip_x = vcycle(strip_rhs, GATHER_LEVEL, whole["levels"], apply_padded, None)
        coarse_ring = ring // 2
        strip_x = jnp.pad(strip_x, ((coarse_ring, coarse_ring), (0, 0)))
        return lax.dynamic_slice(strip_x, (segment_ordinal * block_h, block_w - coarse_ring),
                                 (block_h + 2 * coarse_ring, block_w + 2 * coarse_ring)), summed

    def precondition(rhs_wide, sums=None):
        ring = (rhs_wide.shape[0] - shard_height_total) // 2
        diag_here = ops_at(ring)[4]
        estimate = OMEGA * rhs_wide / diag_here
        remain = crop(rhs_wide, 0) - apply_inner(crop(estimate, 1), levels[0])
        patch, summed = coarse_solve(restrict_sum(remain), ring, sums)
        estimate = estimate + prolong_copy(patch)
        inner = ops_at(ring - 1)
        smoothed = crop(estimate, ring - 1) + OMEGA * (crop(rhs_wide, ring - 1) - apply_inner(estimate, inner)) / inner[4]
        return smoothed, apply_inner(smoothed, ops_at(ring - 2)), summed

    def ring_of(values):
        return (values.shape[-2] - shard_height_total) // 2

    def own_sums(*pairs):
        return jnp.stack([jnp.sum(crop(a, 0) * crop(b, 0)) for a, b in pairs])

    residual_wide = rhs_wide
    precond, image_u, _ = precondition(residual_wide)
    sums = own_sums((residual_wide, precond), (image_u, precond))
    if ITERS > 1:
        pre_image, image_pre, sums = precondition(image_u, sums)
    else:
        sums = total(sums)
    norm_now = sums[0]
    curvature = sums[1]
    step_length = norm_now / curvature
    direction, image_vec = precond, image_u
    if ITERS > 1:
        pre_dir, image_pre_dir = pre_image, image_pre
    solution = step_length * crop(direction, 0)
    for step_index in range(1, ITERS):
        residual_wide = crop(residual_wide, ring_of(image_vec)) - step_length * image_vec
        precond = crop(precond, ring_of(pre_dir)) - step_length * pre_dir
        image_u = crop(image_u, ring_of(image_pre_dir)) - step_length * image_pre_dir
        sums = own_sums((residual_wide, precond), (image_u, precond), (precond, image_vec))
        if step_index + 1 < ITERS:
            pre_image, image_pre, sums = precondition(image_u, sums)
        else:
            sums = total(sums)
        norm_next = sums[0]
        ratio = norm_next / norm_now
        curvature = sums[1] + 2.0 * ratio * sums[2] + ratio * ratio * curvature
        step_length = norm_next / curvature
        direction = precond + ratio * crop(direction, ring_of(precond))
        image_vec = image_u + ratio * crop(image_vec, ring_of(image_u))
        if step_index + 1 < ITERS:
            pre_dir = pre_image + ratio * crop(pre_dir, ring_of(pre_image))
            image_pre_dir = image_pre + ratio * crop(image_pre_dir, ring_of(image_pre))
        solution = solution + step_length * crop(direction, 0)
        norm_now = norm_next
    return (solution, weight)


def solution(mesh):
    return jax.shard_map(
        local,
        mesh=mesh,
        in_specs=(P(None, ("az", "rg"), None), P(None, ("az", "rg"), None), P(), P()),
        out_specs=(P("az", "rg"), P("az", "rg")),
        check_vma=False,
    )
```

```python
import jax
import jax.numpy as jnp
from jax import lax
from jax.sharding import PartitionSpec as P

LOOK = 5
LEVELS = 6
ITERS = 3
SWEEPS = 4
SEGMENT_HEIGHT = 160
GATHER_LEVEL = 1


OMEGA = 0.6
MU = 0.01


def neighbours(v):
    n_az = lax.axis_size("az")
    n_rg = lax.axis_size("rg")
    above = lax.ppermute(v[..., -1:, :], "az", [(i, i + 1) for i in range(n_az - 1)])
    below = lax.ppermute(v[..., :1, :], "az", [(i + 1, i) for i in range(n_az - 1)])
    left = lax.ppermute(v[..., :, -1:], "rg", [(i, i + 1) for i in range(n_rg - 1)])
    right = lax.ppermute(v[..., :, :1], "rg", [(i + 1, i) for i in range(n_rg - 1)])
    north = jnp.concatenate([above, v[..., :-1, :]], axis=-2)
    south = jnp.concatenate([v[..., 1:, :], below], axis=-2)
    west = jnp.concatenate([left, v[..., :, :-1]], axis=-1)
    east = jnp.concatenate([v[..., :, 1:], right], axis=-1)
    return north, south, west, east


def apply_halo(vector, operators):
    east, west, south, north, diagonal = operators
    v_n, v_s, v_w, v_e = neighbours(vector)
    return diagonal * vector - east * v_e - west * v_w - south * v_s - north * v_n


def extended(v, width):
    n_az = lax.axis_size("az")
    n_rg = lax.axis_size("rg")
    above = lax.ppermute(v[..., -width:, :], "az", [(i, i + 1) for i in range(n_az - 1)])
    below = lax.ppermute(v[..., :width, :], "az", [(i + 1, i) for i in range(n_az - 1)])
    v = jnp.concatenate([above, v, below], axis=-2)
    left = lax.ppermute(v[..., :, -width:], "rg", [(i, i + 1) for i in range(n_rg - 1)])
    right = lax.ppermute(v[..., :, :width], "rg", [(i + 1, i) for i in range(n_rg - 1)])
    return jnp.concatenate([left, v, right], axis=-1)


def apply_inner(padded, operators):
    east, west, south, north, diagonal = operators
    return (diagonal * padded[1:-1, 1:-1] - east * padded[1:-1, 2:] - west * padded[1:-1, :-2]
            - south * padded[2:, 1:-1] - north * padded[:-2, 1:-1])


def apply_padded(vector, operators):
    east, west, south, north, diagonal = operators
    padded = jnp.pad(vector, 1)
    return (diagonal * vector - east * padded[1:-1, 2:] - west * padded[1:-1, :-2]
            - south * padded[2:, 1:-1] - north * padded[:-2, 1:-1])


def mean_multilook(leading, trailing, row_ok, col_ok):
    valid_mask = (row_ok[:, None] & col_ok[None, :]).astype(jnp.float32)
    leading = jnp.transpose(leading, (1, 0, 2)).astype(jnp.float32)
    trailing = jnp.transpose(trailing, (1, 0, 2)).astype(jnp.float32)
    first_re = leading[:, 0, :] * valid_mask
    first_im = leading[:, 1, :] * valid_mask
    second_re = trailing[:, 0, :] * valid_mask
    second_im = trailing[:, 1, :] * valid_mask
    products = jnp.stack(
        [
            first_re * second_re + first_im * second_im,
            first_im * second_re - first_re * second_im,
            first_re * first_re + first_im * first_im,
            second_re * second_re + second_im * second_im,
        ]
    )
    height_rows, width_cols = valid_mask.shape
    span = LOOK * 128
    grouped = products.reshape(4, height_rows, width_cols // span, span)
    cols = jnp.einsum("pikc,cd->pikd", grouped, group_sum(span, LOOK).T, precision=HIGHEST)
    cols = cols.reshape(4, height_rows, width_cols // LOOK)
    return jnp.einsum("ri,pic->prc", group_sum(height_rows, LOOK), cols, precision=HIGHEST)


def edge_terms(left_re, left_im, left_weight, right_re, right_im, right_weight):
    edge_weight = 0.5 * (left_weight + right_weight)
    cross_im = right_im * left_re - right_re * left_im
    power_sum = (
        left_re * left_re + left_im * left_im + right_re * right_re + right_im * right_im + 1.0
    )
    return (edge_weight, 2.0 * cross_im / power_sum)


HIGHEST = lax.Precision.HIGHEST


def group_sum(n, size):
    group = lax.broadcasted_iota(jnp.int32, (n // size, n), 0)
    cell = lax.broadcasted_iota(jnp.int32, (n // size, n), 1)
    return (cell // size == group).astype(jnp.float32)


def pick(n, offset):
    group = lax.broadcasted_iota(jnp.int32, (n // 2, n), 0)
    cell = lax.broadcasted_iota(jnp.int32, (n // 2, n), 1)
    return (cell == 2 * group + offset).astype(jnp.float32)


def sandwich(left, vector, right):
    inner = jnp.dot(left, vector, precision=HIGHEST)
    return jnp.dot(inner, right, precision=HIGHEST)


def restrict_sum(vector):
    rows_now, cols_now = vector.shape
    return sandwich(group_sum(rows_now, 2), vector, group_sum(cols_now, 2).T)


def prolong_copy(vector):
    rows_now, cols_now = vector.shape
    return sandwich(group_sum(2 * rows_now, 2).T, vector, group_sum(2 * cols_now, 2))


def coarsen(east, west, south, north):
    rows_now, cols_now = east.shape
    row_sum = group_sum(rows_now, 2)
    col_sum = group_sum(cols_now, 2).T
    return (
        sandwich(row_sum, east, pick(cols_now, 1).T),
        sandwich(row_sum, west, pick(cols_now, 0).T),
        sandwich(pick(rows_now, 1), south, col_sum),
        sandwich(pick(rows_now, 0), north, col_sum),
    )


def build_levels(east, west, south, north, first_level, last_level):
    levels = {}
    for level in range(first_level, last_level):
        diagonal = east + west + south + north + MU * 4.0**level
        levels[level] = (east, west, south, north, diagonal)
        if level + 1 < LEVELS:
            east, west, south, north = coarsen(east, west, south, north)
    return levels, (east, west, south, north)


def jacobi_sweeps(rhs_vec, operators, apply_fn):
    estimate = OMEGA * rhs_vec / operators[4]
    for sweep_index in range(SWEEPS - 1):
        estimate = estimate + OMEGA * (rhs_vec - apply_fn(estimate, operators)) / operators[4]
    return estimate


def vcycle(rhs_vec, level, levels, apply_fn, stop_fn):
    if level == LEVELS - 1:
        return jacobi_sweeps(rhs_vec, levels[level], apply_fn)
    if stop_fn is not None and level == GATHER_LEVEL:
        return stop_fn(rhs_vec)
    diagonal = levels[level][4]
    estimate = OMEGA * rhs_vec / diagonal
    remain = rhs_vec - apply_fn(estimate, levels[level])
    correction = vcycle(restrict_sum(remain), level + 1, levels, apply_fn, stop_fn)
    estimate = estimate + prolong_copy(correction)
    return estimate + OMEGA * (rhs_vec - apply_fn(estimate, levels[level])) / diagonal


def everyone():
    return lax.axis_size("az") * lax.axis_size("rg")


def gather_strip(blocks, sums=None):
    n_az = lax.axis_size("az")
    n_rg = lax.axis_size("rg")
    count, h, w = blocks.shape
    if sums is not None:
        extra = jnp.zeros((1, h, w), jnp.float32).at[0, 0, :sums.shape[0]].set(sums)
        blocks = jnp.concatenate([blocks, extra])
    sent = jnp.broadcast_to(blocks[None], (n_az,) + blocks.shape)
    got = lax.all_to_all(sent, "az", 0, 0, tiled=True)
    summed = None
    if sums is not None:
        column_sums = jnp.sum(got[:, count, 0, :sums.shape[0]], axis=0)
        rows = lax.all_to_all(jnp.broadcast_to(column_sums[None], (n_rg, sums.shape[0])), "rg", 0, 0, tiled=True)
        summed = jnp.sum(rows, axis=0)
        got = got[:, :count]
    column = got.transpose(1, 0, 2, 3).reshape(count, n_az * h, w)
    left = lax.ppermute(column, "rg", [(i, i + 1) for i in range(n_rg - 1)])
    right = lax.ppermute(column, "rg", [(i + 1, i) for i in range(n_rg - 1)])
    return jnp.concatenate([left, column, right], axis=-1), summed


def shifted(values, axis):
    pad = [(0, 0)] * values.ndim
    pad[axis] = (1, 0)
    return lax.slice_in_dim(jnp.pad(values, pad), 0, values.shape[axis], axis=axis)


def total(values):
    n = everyone()
    sent = jnp.broadcast_to(values[None], (n, values.shape[0]))
    got = lax.all_to_all(sent, ("az", "rg"), 0, 0, tiled=True)
    return jnp.sum(got, axis=0)


def local(master_phasor_raster, slave_phasor_raster, segment_track_trim, segment_slant_trim):
    n_az = lax.axis_size("az")
    n_range = lax.axis_size("rg")
    segment_ordinal = lax.axis_index("az")
    range_index = lax.axis_index("rg")
    track_trim_width = lax.dynamic_index_in_dim(
        segment_track_trim, segment_ordinal, 0, keepdims=False
    )
    slant_trim_width = lax.dynamic_index_in_dim(
        segment_slant_trim, segment_ordinal, 0, keepdims=False
    )
    lines_here = master_phasor_raster.shape[1]
    slant_sample_total = master_phasor_raster.shape[2]
    along_track_position = range_index * lines_here + jnp.arange(lines_here, dtype=jnp.int32)
    column_index = jnp.arange(slant_sample_total, dtype=jnp.int32)
    row_ok = (along_track_position >= track_trim_width[0]) & (
        along_track_position < SEGMENT_HEIGHT - track_trim_width[1]
    )
    col_ok = (column_index >= slant_trim_width[0]) & (
        column_index < slant_sample_total - slant_trim_width[1]
    )
    pixel_totals = mean_multilook(master_phasor_raster, slave_phasor_raster, row_ok, col_ok)
    look_re, look_im, power_one, power_two = (
        pixel_totals[0],
        pixel_totals[1],
        pixel_totals[2],
        pixel_totals[3],
    )
    weight = 0.05 + 4.0 * (look_re * look_re + look_im * look_im) / jnp.maximum(
        power_one * power_two, 1.0
    )
    widest = 2 * ITERS
    border = widest + 1
    fields = jnp.stack([look_re, look_im, weight])
    n_fields, rows_here, cols_all = fields.shape
    cols_here = cols_all // n_range
    fields = jnp.pad(fields, ((0, 0), (0, 0), (border, border)))
    fields = jnp.stack([fields[:, :, c * cols_here:(c + 1) * cols_here + 2 * border] for c in range(n_range)])
    fields = lax.all_to_all(fields, "rg", 0, 0, tiled=True)
    fields = fields.transpose(1, 0, 2, 3).reshape(n_fields, n_range * rows_here, cols_here + 2 * border)
    shard_height_total = n_range * rows_here
    above = lax.ppermute(fields[:, -border:, :], "az", [(i, i + 1) for i in range(n_az - 1)])
    below = lax.ppermute(fields[:, :border, :], "az", [(i + 1, i) for i in range(n_az - 1)])
    fields = jnp.concatenate([above, fields, below], axis=1)
    weight = fields[2, border:-border, border:-border]

    row_global = segment_ordinal * shard_height_total - border + jnp.arange(
        shard_height_total + 2 * border, dtype=jnp.int32)
    col_global = range_index * cols_here - border + jnp.arange(cols_here + 2 * border, dtype=jnp.int32)
    edge_h, grad_h = edge_terms(fields[0, :, :-1], fields[1, :, :-1], fields[2, :, :-1],
                                fields[0, :, 1:], fields[1, :, 1:], fields[2, :, 1:])
    keep_h = ((col_global[:-1] >= 0) & (col_global[:-1] <= cols_here * n_range - 2)).astype(jnp.float32)
    edge_h = edge_h * keep_h[None, :]
    edge_v, grad_v = edge_terms(fields[0, :-1], fields[1, :-1], fields[2, :-1],
                                fields[0, 1:], fields[1, 1:], fields[2, 1:])
    keep_v = ((row_global[:-1] >= 0) & (row_global[:-1] <= shard_height_total * n_az - 2)).astype(jnp.float32)
    edge_v = edge_v * keep_v[:, None]
    flux_h = edge_h * grad_h
    flux_v = edge_v * grad_v
    east_w = edge_h[1:-1, 1:]
    west_w = edge_h[1:-1, :-1]
    south_w = edge_v[1:, 1:-1]
    north_w = edge_v[:-1, 1:-1]
    diag_w = east_w + west_w + south_w + north_w + MU * 4.0**0
    ops_w = (east_w, west_w, south_w, north_w, diag_w)
    rhs_wide = -(flux_h[1:-1, 1:] - flux_h[1:-1, :-1] + flux_v[1:, 1:-1] - flux_v[:-1, 1:-1])

    def crop(values, ring):
        cut = (values.shape[-2] - shard_height_total) // 2 - ring
        if cut == 0:
            return values
        return values[..., cut:-cut, cut:-cut]

    def ops_at(ring):
        return tuple(crop(x, ring) for x in ops_w)

    levels, coarse_edges = build_levels(*ops_at(0)[:4], first_level=0, last_level=GATHER_LEVEL)
    block_h, block_w = coarse_edges[0].shape
    whole = {}

    def coarse_solve(rhs_vec, ring, sums):
        if not whole:
            got, summed = gather_strip(jnp.stack([coarse_edges[0], coarse_edges[2], rhs_vec]), sums)
            east_s, south_s = got[0], got[1]
            whole["levels"] = build_levels(east_s, shifted(east_s, 1), south_s, shifted(south_s, 0),
                                           GATHER_LEVEL, LEVELS)[0]
            strip_rhs = got[2]
        else:
            got, summed = gather_strip(rhs_vec[None], sums)
            strip_rhs = got[0]
        strip_x = vcycle(strip_rhs, GATHER_LEVEL, whole["levels"], apply_padded, None)
        coarse_ring = ring // 2
        strip_x = jnp.pad(strip_x, ((coarse_ring, coarse_ring), (0, 0)))
        return lax.dynamic_slice(strip_x, (segment_ordinal * block_h, block_w - coarse_ring),
                                 (block_h + 2 * coarse_ring, block_w + 2 * coarse_ring)), summed

    def precondition(rhs_wide, sums=None):
        ring = (rhs_wide.shape[0] - shard_height_total) // 2
        diag_here = ops_at(ring)[4]
        estimate = OMEGA * rhs_wide / diag_here
        remain = crop(rhs_wide, 0) - apply_inner(crop(estimate, 1), levels[0])
        patch, summed = coarse_solve(restrict_sum(remain), ring, sums)
        estimate = estimate + prolong_copy(patch)
        inner = ops_at(ring - 1)
        smoothed = crop(estimate, ring - 1) + OMEGA * (crop(rhs_wide, ring - 1) - apply_inner(estimate, inner)) / inner[4]
        return smoothed, apply_inner(smoothed, ops_at(ring - 2)), summed

    def ring_of(values):
        return (values.shape[-2] - shard_height_total) // 2

    def own_sums(*pairs):
        return jnp.stack([jnp.sum(crop(a, 0) * crop(b, 0)) for a, b in pairs])

    residual_wide = rhs_wide
    precond, image_u, _ = precondition(residual_wide)
    sums = own_sums((residual_wide, precond), (image_u, precond))
    if ITERS > 1:
        pre_image, image_pre, sums = precondition(image_u, sums)
    else:
        sums = total(sums)
    norm_now = sums[0]
    curvature = sums[1]
    step_length = norm_now / curvature
    direction, image_vec = precond, image_u
    if ITERS > 1:
        pre_dir, image_pre_dir = pre_image, image_pre
    solution = step_length * crop(direction, 0)
    for step_index in range(1, ITERS):
        residual_wide = crop(residual_wide, ring_of(image_vec)) - step_length * image_vec
        precond = crop(precond, ring_of(pre_dir)) - step_length * pre_dir
        image_u = crop(image_u, ring_of(image_pre_dir)) - step_length * image_pre_dir
        sums = own_sums((residual_wide, precond), (image_u, precond), (precond, image_vec))
        if step_index + 1 < ITERS:
            pre_image, image_pre, sums = precondition(image_u, sums)
        else:
            sums = total(sums)
        norm_next = sums[0]
        ratio = norm_next / norm_now
        curvature = sums[1] + 2.0 * ratio * sums[2] + ratio * ratio * curvature
        step_length = norm_next / curvature
        direction = precond + ratio * crop(direction, ring_of(precond))
        image_vec = image_u + ratio * crop(image_vec, ring_of(image_u))
        if step_index + 1 < ITERS:
            pre_dir = pre_image + ratio * crop(pre_dir, ring_of(pre_image))
            image_pre_dir = image_pre + ratio * crop(image_pre_dir, ring_of(image_pre))
        solution = solution + step_length * crop(direction, 0)
        norm_now = norm_next
    return (solution, weight)


def solution(mesh):
    return jax.shard_map(
        local,
        mesh=mesh,
        in_specs=(P(None, ("az", "rg"), None), P(None, ("az", "rg"), None), P(), P()),
        out_specs=(P("az", "rg"), P("az", "rg")),
        check_vma=False,
    )
```

```python
import jax
import jax.numpy as jnp
from jax import lax
from jax.sharding import PartitionSpec as P
from jax.experimental import pallas as pl

LOOK = 5
LEVELS = 6
ITERS = 3
SWEEPS = 4
SEGMENT_HEIGHT = 160
GATHER_LEVEL = 1


OMEGA = 0.6
MU = 0.01


def neighbours(v):
    n_az = lax.axis_size("az")
    n_rg = lax.axis_size("rg")
    above = lax.ppermute(v[..., -1:, :], "az", [(i, i + 1) for i in range(n_az - 1)])
    below = lax.ppermute(v[..., :1, :], "az", [(i + 1, i) for i in range(n_az - 1)])
    left = lax.ppermute(v[..., :, -1:], "rg", [(i, i + 1) for i in range(n_rg - 1)])
    right = lax.ppermute(v[..., :, :1], "rg", [(i + 1, i) for i in range(n_rg - 1)])
    north = jnp.concatenate([above, v[..., :-1, :]], axis=-2)
    south = jnp.concatenate([v[..., 1:, :], below], axis=-2)
    west = jnp.concatenate([left, v[..., :, :-1]], axis=-1)
    east = jnp.concatenate([v[..., :, 1:], right], axis=-1)
    return north, south, west, east


def apply_halo(vector, operators):
    east, west, south, north, diagonal = operators
    v_n, v_s, v_w, v_e = neighbours(vector)
    return diagonal * vector - east * v_e - west * v_w - south * v_s - north * v_n


def extended(v, width):
    n_az = lax.axis_size("az")
    n_rg = lax.axis_size("rg")
    above = lax.ppermute(v[..., -width:, :], "az", [(i, i + 1) for i in range(n_az - 1)])
    below = lax.ppermute(v[..., :width, :], "az", [(i + 1, i) for i in range(n_az - 1)])
    v = jnp.concatenate([above, v, below], axis=-2)
    left = lax.ppermute(v[..., :, -width:], "rg", [(i, i + 1) for i in range(n_rg - 1)])
    right = lax.ppermute(v[..., :, :width], "rg", [(i + 1, i) for i in range(n_rg - 1)])
    return jnp.concatenate([left, v, right], axis=-1)


def apply_inner(padded, operators):
    east, west, south, north, diagonal = operators
    return (diagonal * padded[1:-1, 1:-1] - east * padded[1:-1, 2:] - west * padded[1:-1, :-2]
            - south * padded[2:, 1:-1] - north * padded[:-2, 1:-1])


def apply_padded(vector, operators):
    east, west, south, north, diagonal = operators
    padded = jnp.pad(vector, 1)
    return (diagonal * vector - east * padded[1:-1, 2:] - west * padded[1:-1, :-2]
            - south * padded[2:, 1:-1] - north * padded[:-2, 1:-1])


def multilook_kernel(lead_ref, trail_ref, row_ref, col_ref, out_ref):
    mask = row_ref[:, 0:1] * col_ref[...]
    first_re = lead_ref[0].astype(jnp.float32) * mask
    first_im = lead_ref[1].astype(jnp.float32) * mask
    second_re = trail_ref[0].astype(jnp.float32) * mask
    second_im = trail_ref[1].astype(jnp.float32) * mask
    products = (
        first_re * second_re + first_im * second_im,
        first_im * second_re - first_re * second_im,
        first_re * first_re + first_im * first_im,
        second_re * second_re + second_im * second_im,
    )
    for part, values in enumerate(products):
        for group in range(out_ref.shape[1]):
            acc = values[group * LOOK:group * LOOK + 1, :]
            for offset in range(1, LOOK):
                acc = acc + values[group * LOOK + offset:group * LOOK + offset + 1, :]
            out_ref[part, group:group + 1, :] = acc


def mean_multilook(leading, trailing, row_ok, col_ok):
    _, height_rows, width_cols = leading.shape
    block = 1024
    rows = pl.pallas_call(
        multilook_kernel,
        grid=(width_cols // block,),
        in_specs=[
            pl.BlockSpec((2, height_rows, block), lambda j: (0, 0, j)),
            pl.BlockSpec((2, height_rows, block), lambda j: (0, 0, j)),
            pl.BlockSpec((height_rows, 128), lambda j: (0, 0)),
            pl.BlockSpec((1, block), lambda j: (0, j)),
        ],
        out_specs=pl.BlockSpec((4, height_rows // LOOK, block), lambda j: (0, 0, j)),
        out_shape=jax.ShapeDtypeStruct((4, height_rows // LOOK, width_cols), jnp.float32),
    )(leading, trailing, jnp.broadcast_to(row_ok.astype(jnp.float32)[:, None], (height_rows, 128)),
      col_ok.astype(jnp.float32)[None, :])
    span = LOOK * 128
    grouped = rows.reshape(4, height_rows // LOOK, width_cols // span, span)
    cols = jnp.einsum("pikc,cd->pikd", grouped, group_sum(span, LOOK).T, precision=HIGHEST)
    return cols.reshape(4, height_rows // LOOK, width_cols // LOOK)


def edge_terms(left_re, left_im, left_weight, right_re, right_im, right_weight):
    edge_weight = 0.5 * (left_weight + right_weight)
    cross_im = right_im * left_re - right_re * left_im
    power_sum = (
        left_re * left_re + left_im * left_im + right_re * right_re + right_im * right_im + 1.0
    )
    return (edge_weight, 2.0 * cross_im / power_sum)


HIGHEST = lax.Precision.HIGHEST


def group_sum(n, size):
    group = lax.broadcasted_iota(jnp.int32, (n // size, n), 0)
    cell = lax.broadcasted_iota(jnp.int32, (n // size, n), 1)
    return (cell // size == group).astype(jnp.float32)


def pick(n, offset):
    group = lax.broadcasted_iota(jnp.int32, (n // 2, n), 0)
    cell = lax.broadcasted_iota(jnp.int32, (n // 2, n), 1)
    return (cell == 2 * group + offset).astype(jnp.float32)


def sandwich(left, vector, right):
    inner = jnp.dot(left, vector, precision=HIGHEST)
    return jnp.dot(inner, right, precision=HIGHEST)


def restrict_sum(vector):
    rows_now, cols_now = vector.shape
    return sandwich(group_sum(rows_now, 2), vector, group_sum(cols_now, 2).T)


def prolong_copy(vector):
    rows_now, cols_now = vector.shape
    return sandwich(group_sum(2 * rows_now, 2).T, vector, group_sum(2 * cols_now, 2))


def coarsen(east, west, south, north):
    rows_now, cols_now = east.shape
    row_sum = group_sum(rows_now, 2)
    col_sum = group_sum(cols_now, 2).T
    return (
        sandwich(row_sum, east, pick(cols_now, 1).T),
        sandwich(row_sum, west, pick(cols_now, 0).T),
        sandwich(pick(rows_now, 1), south, col_sum),
        sandwich(pick(rows_now, 0), north, col_sum),
    )


def build_levels(east, west, south, north, first_level, last_level):
    levels = {}
    for level in range(first_level, last_level):
        diagonal = east + west + south + north + MU * 4.0**level
        levels[level] = (east, west, south, north, diagonal)
        if level + 1 < LEVELS:
            east, west, south, north = coarsen(east, west, south, north)
    return levels, (east, west, south, north)


def jacobi_sweeps(rhs_vec, operators, apply_fn):
    estimate = OMEGA * rhs_vec / operators[4]
    for sweep_index in range(SWEEPS - 1):
        estimate = estimate + OMEGA * (rhs_vec - apply_fn(estimate, operators)) / operators[4]
    return estimate


def vcycle(rhs_vec, level, levels, apply_fn, stop_fn):
    if level == LEVELS - 1:
        return jacobi_sweeps(rhs_vec, levels[level], apply_fn)
    if stop_fn is not None and level == GATHER_LEVEL:
        return stop_fn(rhs_vec)
    diagonal = levels[level][4]
    estimate = OMEGA * rhs_vec / diagonal
    remain = rhs_vec - apply_fn(estimate, levels[level])
    correction = vcycle(restrict_sum(remain), level + 1, levels, apply_fn, stop_fn)
    estimate = estimate + prolong_copy(correction)
    return estimate + OMEGA * (rhs_vec - apply_fn(estimate, levels[level])) / diagonal


def everyone():
    return lax.axis_size("az") * lax.axis_size("rg")


def gather_strip(blocks, sums=None):
    n_az = lax.axis_size("az")
    n_rg = lax.axis_size("rg")
    count, h, w = blocks.shape
    if sums is not None:
        extra = jnp.zeros((1, h, w), jnp.float32).at[0, 0, :sums.shape[0]].set(sums)
        blocks = jnp.concatenate([blocks, extra])
    sent = jnp.broadcast_to(blocks[None], (n_az,) + blocks.shape)
    got = lax.all_to_all(sent, "az", 0, 0, tiled=True)
    summed = None
    if sums is not None:
        column_sums = jnp.sum(got[:, count, 0, :sums.shape[0]], axis=0)
        rows = lax.all_to_all(jnp.broadcast_to(column_sums[None], (n_rg, sums.shape[0])), "rg", 0, 0, tiled=True)
        summed = jnp.sum(rows, axis=0)
        got = got[:, :count]
    column = got.transpose(1, 0, 2, 3).reshape(count, n_az * h, w)
    left = lax.ppermute(column, "rg", [(i, i + 1) for i in range(n_rg - 1)])
    right = lax.ppermute(column, "rg", [(i + 1, i) for i in range(n_rg - 1)])
    return jnp.concatenate([left, column, right], axis=-1), summed


def shifted(values, axis):
    pad = [(0, 0)] * values.ndim
    pad[axis] = (1, 0)
    return lax.slice_in_dim(jnp.pad(values, pad), 0, values.shape[axis], axis=axis)


def total(values):
    n = everyone()
    sent = jnp.broadcast_to(values[None], (n, values.shape[0]))
    got = lax.all_to_all(sent, ("az", "rg"), 0, 0, tiled=True)
    return jnp.sum(got, axis=0)


def local(master_phasor_raster, slave_phasor_raster, segment_track_trim, segment_slant_trim):
    n_az = lax.axis_size("az")
    n_range = lax.axis_size("rg")
    segment_ordinal = lax.axis_index("az")
    range_index = lax.axis_index("rg")
    track_trim_width = lax.dynamic_index_in_dim(
        segment_track_trim, segment_ordinal, 0, keepdims=False
    )
    slant_trim_width = lax.dynamic_index_in_dim(
        segment_slant_trim, segment_ordinal, 0, keepdims=False
    )
    lines_here = master_phasor_raster.shape[1]
    slant_sample_total = master_phasor_raster.shape[2]
    along_track_position = range_index * lines_here + jnp.arange(lines_here, dtype=jnp.int32)
    column_index = jnp.arange(slant_sample_total, dtype=jnp.int32)
    row_ok = (along_track_position >= track_trim_width[0]) & (
        along_track_position < SEGMENT_HEIGHT - track_trim_width[1]
    )
    col_ok = (column_index >= slant_trim_width[0]) & (
        column_index < slant_sample_total - slant_trim_width[1]
    )
    pixel_totals = mean_multilook(master_phasor_raster, slave_phasor_raster, row_ok, col_ok)
    look_re, look_im, power_one, power_two = (
        pixel_totals[0],
        pixel_totals[1],
        pixel_totals[2],
        pixel_totals[3],
    )
    weight = 0.05 + 4.0 * (look_re * look_re + look_im * look_im) / jnp.maximum(
        power_one * power_two, 1.0
    )
    widest = 2 * ITERS
    border = widest + 1
    fields = jnp.stack([look_re, look_im, weight])
    n_fields, rows_here, cols_all = fields.shape
    cols_here = cols_all // n_range
    fields = jnp.pad(fields, ((0, 0), (0, 0), (border, border)))
    fields = jnp.stack([fields[:, :, c * cols_here:(c + 1) * cols_here + 2 * border] for c in range(n_range)])
    fields = lax.all_to_all(fields, "rg", 0, 0, tiled=True)
    fields = fields.transpose(1, 0, 2, 3).reshape(n_fields, n_range * rows_here, cols_here + 2 * border)
    shard_height_total = n_range * rows_here
    above = lax.ppermute(fields[:, -border:, :], "az", [(i, i + 1) for i in range(n_az - 1)])
    below = lax.ppermute(fields[:, :border, :], "az", [(i + 1, i) for i in range(n_az - 1)])
    fields = jnp.concatenate([above, fields, below], axis=1)
    weight = fields[2, border:-border, border:-border]

    row_global = segment_ordinal * shard_height_total - border + jnp.arange(
        shard_height_total + 2 * border, dtype=jnp.int32)
    col_global = range_index * cols_here - border + jnp.arange(cols_here + 2 * border, dtype=jnp.int32)
    edge_h, grad_h = edge_terms(fields[0, :, :-1], fields[1, :, :-1], fields[2, :, :-1],
                                fields[0, :, 1:], fields[1, :, 1:], fields[2, :, 1:])
    keep_h = ((col_global[:-1] >= 0) & (col_global[:-1] <= cols_here * n_range - 2)).astype(jnp.float32)
    edge_h = edge_h * keep_h[None, :]
    edge_v, grad_v = edge_terms(fields[0, :-1], fields[1, :-1], fields[2, :-1],
                                fields[0, 1:], fields[1, 1:], fields[2, 1:])
    keep_v = ((row_global[:-1] >= 0) & (row_global[:-1] <= shard_height_total * n_az - 2)).astype(jnp.float32)
    edge_v = edge_v * keep_v[:, None]
    flux_h = edge_h * grad_h
    flux_v = edge_v * grad_v
    east_w = edge_h[1:-1, 1:]
    west_w = edge_h[1:-1, :-1]
    south_w = edge_v[1:, 1:-1]
    north_w = edge_v[:-1, 1:-1]
    diag_w = east_w + west_w + south_w + north_w + MU * 4.0**0
    ops_w = (east_w, west_w, south_w, north_w, diag_w)
    rhs_wide = -(flux_h[1:-1, 1:] - flux_h[1:-1, :-1] + flux_v[1:, 1:-1] - flux_v[:-1, 1:-1])

    def crop(values, ring):
        cut = (values.shape[-2] - shard_height_total) // 2 - ring
        if cut == 0:
            return values
        return values[..., cut:-cut, cut:-cut]

    def ops_at(ring):
        return tuple(crop(x, ring) for x in ops_w)

    levels, coarse_edges = build_levels(*ops_at(0)[:4], first_level=0, last_level=GATHER_LEVEL)
    block_h, block_w = coarse_edges[0].shape
    whole = {}

    def coarse_solve(rhs_vec, ring, sums):
        if not whole:
            got, summed = gather_strip(jnp.stack([coarse_edges[0], coarse_edges[2], rhs_vec]), sums)
            east_s, south_s = got[0], got[1]
            whole["levels"] = build_levels(east_s, shifted(east_s, 1), south_s, shifted(south_s, 0),
                                           GATHER_LEVEL, LEVELS)[0]
            strip_rhs = got[2]
        else:
            got, summed = gather_strip(rhs_vec[None], sums)
            strip_rhs = got[0]
        strip_x = vcycle(strip_rhs, GATHER_LEVEL, whole["levels"], apply_padded, None)
        coarse_ring = ring // 2
        strip_x = jnp.pad(strip_x, ((coarse_ring, coarse_ring), (0, 0)))
        return lax.dynamic_slice(strip_x, (segment_ordinal * block_h, block_w - coarse_ring),
                                 (block_h + 2 * coarse_ring, block_w + 2 * coarse_ring)), summed

    def precondition(rhs_wide, sums=None):
        ring = (rhs_wide.shape[0] - shard_height_total) // 2
        diag_here = ops_at(ring)[4]
        estimate = OMEGA * rhs_wide / diag_here
        remain = crop(rhs_wide, 0) - apply_inner(crop(estimate, 1), levels[0])
        patch, summed = coarse_solve(restrict_sum(remain), ring, sums)
        estimate = estimate + prolong_copy(patch)
        inner = ops_at(ring - 1)
        smoothed = crop(estimate, ring - 1) + OMEGA * (crop(rhs_wide, ring - 1) - apply_inner(estimate, inner)) / inner[4]
        return smoothed, apply_inner(smoothed, ops_at(ring - 2)), summed

    def ring_of(values):
        return (values.shape[-2] - shard_height_total) // 2

    def own_sums(*pairs):
        return jnp.stack([jnp.sum(crop(a, 0) * crop(b, 0)) for a, b in pairs])

    residual_wide = rhs_wide
    precond, image_u, _ = precondition(residual_wide)
    sums = own_sums((residual_wide, precond), (image_u, precond))
    if ITERS > 1:
        pre_image, image_pre, sums = precondition(image_u, sums)
    else:
        sums = total(sums)
    norm_now = sums[0]
    curvature = sums[1]
    step_length = norm_now / curvature
    direction, image_vec = precond, image_u
    if ITERS > 1:
        pre_dir, image_pre_dir = pre_image, image_pre
    solution = step_length * crop(direction, 0)
    for step_index in range(1, ITERS):
        residual_wide = crop(residual_wide, ring_of(image_vec)) - step_length * image_vec
        precond = crop(precond, ring_of(pre_dir)) - step_length * pre_dir
        image_u = crop(image_u, ring_of(image_pre_dir)) - step_length * image_pre_dir
        sums = own_sums((residual_wide, precond), (image_u, precond), (precond, image_vec))
        if step_index + 1 < ITERS:
            pre_image, image_pre, sums = precondition(image_u, sums)
        else:
            sums = total(sums)
        norm_next = sums[0]
        ratio = norm_next / norm_now
        curvature = sums[1] + 2.0 * ratio * sums[2] + ratio * ratio * curvature
        step_length = norm_next / curvature
        direction = precond + ratio * crop(direction, ring_of(precond))
        image_vec = image_u + ratio * crop(image_vec, ring_of(image_u))
        if step_index + 1 < ITERS:
            pre_dir = pre_image + ratio * crop(pre_dir, ring_of(pre_image))
            image_pre_dir = image_pre + ratio * crop(image_pre_dir, ring_of(image_pre))
        solution = solution + step_length * crop(direction, 0)
        norm_now = norm_next
    return (solution, weight)


def solution(mesh):
    return jax.shard_map(
        local,
        mesh=mesh,
        in_specs=(P(None, ("az", "rg"), None), P(None, ("az", "rg"), None), P(), P()),
        out_specs=(P("az", "rg"), P("az", "rg")),
        check_vma=False,
    )
```

```python
import jax
import jax.numpy as jnp
from jax import lax
from jax.sharding import PartitionSpec as P
from jax.experimental import pallas as pl

LOOK = 5
LEVELS = 6
ITERS = 3
SWEEPS = 4
SEGMENT_HEIGHT = 160
GATHER_LEVEL = 1


OMEGA = 0.6
MU = 0.01


def neighbours(v):
    n_az = lax.axis_size("az")
    n_rg = lax.axis_size("rg")
    above = lax.ppermute(v[..., -1:, :], "az", [(i, i + 1) for i in range(n_az - 1)])
    below = lax.ppermute(v[..., :1, :], "az", [(i + 1, i) for i in range(n_az - 1)])
    left = lax.ppermute(v[..., :, -1:], "rg", [(i, i + 1) for i in range(n_rg - 1)])
    right = lax.ppermute(v[..., :, :1], "rg", [(i + 1, i) for i in range(n_rg - 1)])
    north = jnp.concatenate([above, v[..., :-1, :]], axis=-2)
    south = jnp.concatenate([v[..., 1:, :], below], axis=-2)
    west = jnp.concatenate([left, v[..., :, :-1]], axis=-1)
    east = jnp.concatenate([v[..., :, 1:], right], axis=-1)
    return north, south, west, east


def apply_halo(vector, operators):
    east, west, south, north, diagonal = operators
    v_n, v_s, v_w, v_e = neighbours(vector)
    return diagonal * vector - east * v_e - west * v_w - south * v_s - north * v_n


def extended(v, width):
    n_az = lax.axis_size("az")
    n_rg = lax.axis_size("rg")
    above = lax.ppermute(v[..., -width:, :], "az", [(i, i + 1) for i in range(n_az - 1)])
    below = lax.ppermute(v[..., :width, :], "az", [(i + 1, i) for i in range(n_az - 1)])
    v = jnp.concatenate([above, v, below], axis=-2)
    left = lax.ppermute(v[..., :, -width:], "rg", [(i, i + 1) for i in range(n_rg - 1)])
    right = lax.ppermute(v[..., :, :width], "rg", [(i + 1, i) for i in range(n_rg - 1)])
    return jnp.concatenate([left, v, right], axis=-1)


def apply_inner(padded, operators):
    east, west, south, north, diagonal = operators
    return (diagonal * padded[1:-1, 1:-1] - east * padded[1:-1, 2:] - west * padded[1:-1, :-2]
            - south * padded[2:, 1:-1] - north * padded[:-2, 1:-1])


def apply_padded(vector, operators):
    east, west, south, north, diagonal = operators
    padded = jnp.pad(vector, 1)
    return (diagonal * vector - east * padded[1:-1, 2:] - west * padded[1:-1, :-2]
            - south * padded[2:, 1:-1] - north * padded[:-2, 1:-1])


def multilook_kernel(lead_ref, trail_ref, row_ref, col_ref, out_ref):
    mask = row_ref[:, 0:1] * col_ref[...]
    first_re = lead_ref[0].astype(jnp.float32) * mask
    first_im = lead_ref[1].astype(jnp.float32) * mask
    second_re = trail_ref[0].astype(jnp.float32) * mask
    second_im = trail_ref[1].astype(jnp.float32) * mask
    products = (
        first_re * second_re + first_im * second_im,
        first_im * second_re - first_re * second_im,
        first_re * first_re + first_im * first_im,
        second_re * second_re + second_im * second_im,
    )
    for part, values in enumerate(products):
        for group in range(out_ref.shape[1]):
            acc = values[group * LOOK:group * LOOK + 1, :]
            for offset in range(1, LOOK):
                acc = acc + values[group * LOOK + offset:group * LOOK + offset + 1, :]
            out_ref[part, group:group + 1, :] = acc


def mean_multilook(leading, trailing, row_ok, col_ok):
    _, height_rows, width_cols = leading.shape
    block = 1024
    rows = pl.pallas_call(
        multilook_kernel,
        grid=(width_cols // block,),
        in_specs=[
            pl.BlockSpec((2, height_rows, block), lambda j: (0, 0, j)),
            pl.BlockSpec((2, height_rows, block), lambda j: (0, 0, j)),
            pl.BlockSpec((height_rows, 128), lambda j: (0, 0)),
            pl.BlockSpec((1, block), lambda j: (0, j)),
        ],
        out_specs=pl.BlockSpec((4, height_rows // LOOK, block), lambda j: (0, 0, j)),
        out_shape=jax.ShapeDtypeStruct((4, height_rows // LOOK, width_cols), jnp.float32),
    )(leading, trailing, jnp.broadcast_to(row_ok.astype(jnp.float32)[:, None], (height_rows, 128)),
      col_ok.astype(jnp.float32)[None, :])
    span = LOOK * 128
    grouped = rows.reshape(4, height_rows // LOOK, width_cols // span, span)
    cols = jnp.einsum("pikc,cd->pikd", grouped, group_sum(span, LOOK).T, precision=HIGHEST)
    return cols.reshape(4, height_rows // LOOK, width_cols // LOOK)


def edge_terms(left_re, left_im, left_weight, right_re, right_im, right_weight):
    edge_weight = 0.5 * (left_weight + right_weight)
    cross_im = right_im * left_re - right_re * left_im
    power_sum = (
        left_re * left_re + left_im * left_im + right_re * right_re + right_im * right_im + 1.0
    )
    return (edge_weight, 2.0 * cross_im / power_sum)


HIGHEST = lax.Precision.HIGHEST


def group_sum(n, size):
    group = lax.broadcasted_iota(jnp.int32, (n // size, n), 0)
    cell = lax.broadcasted_iota(jnp.int32, (n // size, n), 1)
    return (cell // size == group).astype(jnp.float32)


def pick(n, offset):
    group = lax.broadcasted_iota(jnp.int32, (n // 2, n), 0)
    cell = lax.broadcasted_iota(jnp.int32, (n // 2, n), 1)
    return (cell == 2 * group + offset).astype(jnp.float32)


def sandwich(left, vector, right):
    inner = jnp.dot(left, vector, precision=HIGHEST)
    return jnp.dot(inner, right, precision=HIGHEST)


def restrict_sum(vector):
    rows_now, cols_now = vector.shape
    return sandwich(group_sum(rows_now, 2), vector, group_sum(cols_now, 2).T)


def prolong_copy(vector):
    rows_now, cols_now = vector.shape
    return sandwich(group_sum(2 * rows_now, 2).T, vector, group_sum(2 * cols_now, 2))


def coarsen(east, west, south, north):
    rows_now, cols_now = east.shape
    row_sum = group_sum(rows_now, 2)
    col_sum = group_sum(cols_now, 2).T
    return (
        sandwich(row_sum, east, pick(cols_now, 1).T),
        sandwich(row_sum, west, pick(cols_now, 0).T),
        sandwich(pick(rows_now, 1), south, col_sum),
        sandwich(pick(rows_now, 0), north, col_sum),
    )


def build_levels(east, west, south, north, first_level, last_level):
    levels = {}
    for level in range(first_level, last_level):
        diagonal = east + west + south + north + MU * 4.0**level
        levels[level] = (east, west, south, north, diagonal)
        if level + 1 < LEVELS:
            east, west, south, north = coarsen(east, west, south, north)
    return levels, (east, west, south, north)


def jacobi_sweeps(rhs_vec, operators, apply_fn):
    estimate = OMEGA * rhs_vec / operators[4]
    for sweep_index in range(SWEEPS - 1):
        estimate = estimate + OMEGA * (rhs_vec - apply_fn(estimate, operators)) / operators[4]
    return estimate


def vcycle(rhs_vec, level, levels, apply_fn, stop_fn):
    if level == LEVELS - 1:
        return jacobi_sweeps(rhs_vec, levels[level], apply_fn)
    if stop_fn is not None and level == GATHER_LEVEL:
        return stop_fn(rhs_vec)
    diagonal = levels[level][4]
    estimate = OMEGA * rhs_vec / diagonal
    remain = rhs_vec - apply_fn(estimate, levels[level])
    correction = vcycle(restrict_sum(remain), level + 1, levels, apply_fn, stop_fn)
    estimate = estimate + prolong_copy(correction)
    return estimate + OMEGA * (rhs_vec - apply_fn(estimate, levels[level])) / diagonal


def everyone():
    return lax.axis_size("az") * lax.axis_size("rg")


def gather_strip(blocks, sums=None):
    n_az = lax.axis_size("az")
    n_rg = lax.axis_size("rg")
    count, h, w = blocks.shape
    if sums is not None:
        extra = jnp.zeros((1, h, w), jnp.float32).at[0, 0, :sums.shape[0]].set(sums)
        blocks = jnp.concatenate([blocks, extra])
    sent = jnp.broadcast_to(blocks[None], (n_az,) + blocks.shape)
    got = lax.all_to_all(sent, "az", 0, 0, tiled=True)
    summed = None
    if sums is not None:
        column_sums = jnp.sum(got[:, count, 0, :sums.shape[0]], axis=0)
        rows = lax.all_to_all(jnp.broadcast_to(column_sums[None], (n_rg, sums.shape[0])), "rg", 0, 0, tiled=True)
        summed = jnp.sum(rows, axis=0)
        got = got[:, :count]
    column = got.transpose(1, 0, 2, 3).reshape(count, n_az * h, w)
    left = lax.ppermute(column, "rg", [(i, i + 1) for i in range(n_rg - 1)])
    right = lax.ppermute(column, "rg", [(i + 1, i) for i in range(n_rg - 1)])
    return jnp.concatenate([left, column, right], axis=-1), summed


def shifted(values, axis):
    pad = [(0, 0)] * values.ndim
    pad[axis] = (1, 0)
    return lax.slice_in_dim(jnp.pad(values, pad), 0, values.shape[axis], axis=axis)


def total(values):
    n = everyone()
    sent = jnp.broadcast_to(values[None], (n, values.shape[0]))
    got = lax.all_to_all(sent, ("az", "rg"), 0, 0, tiled=True)
    return jnp.sum(got, axis=0)


def local(master_phasor_raster, slave_phasor_raster, segment_track_trim, segment_slant_trim):
    n_az = lax.axis_size("az")
    n_range = lax.axis_size("rg")
    segment_ordinal = lax.axis_index("az")
    range_index = lax.axis_index("rg")
    track_trim_width = lax.dynamic_index_in_dim(
        segment_track_trim, segment_ordinal, 0, keepdims=False
    )
    slant_trim_width = lax.dynamic_index_in_dim(
        segment_slant_trim, segment_ordinal, 0, keepdims=False
    )
    lines_here = master_phasor_raster.shape[1]
    slant_sample_total = master_phasor_raster.shape[2]
    along_track_position = range_index * lines_here + jnp.arange(lines_here, dtype=jnp.int32)
    column_index = jnp.arange(slant_sample_total, dtype=jnp.int32)
    row_ok = (along_track_position >= track_trim_width[0]) & (
        along_track_position < SEGMENT_HEIGHT - track_trim_width[1]
    )
    col_ok = (column_index >= slant_trim_width[0]) & (
        column_index < slant_sample_total - slant_trim_width[1]
    )
    pixel_totals = mean_multilook(master_phasor_raster, slave_phasor_raster, row_ok, col_ok)
    look_re, look_im, power_one, power_two = (
        pixel_totals[0],
        pixel_totals[1],
        pixel_totals[2],
        pixel_totals[3],
    )
    weight = 0.05 + 4.0 * (look_re * look_re + look_im * look_im) / jnp.maximum(
        power_one * power_two, 1.0
    )
    widest = 2 * ITERS
    border = widest + 1
    fields = jnp.stack([look_re, look_im, weight])
    n_fields, rows_here, cols_all = fields.shape
    cols_here = cols_all // n_range
    main = fields.reshape(n_fields, rows_here, n_range, cols_here).transpose(2, 0, 1, 3)
    zero = jnp.zeros((1, n_fields, rows_here, border), jnp.float32)
    before = jnp.concatenate([zero, main[:-1, :, :, -border:]], axis=0)
    after = jnp.concatenate([main[1:, :, :, :border], zero], axis=0)
    fields = jnp.concatenate([before, main, after], axis=-1)
    fields = lax.all_to_all(fields, "rg", 0, 0, tiled=True)
    fields = fields.transpose(1, 0, 2, 3).reshape(n_fields, n_range * rows_here, cols_here + 2 * border)
    shard_height_total = n_range * rows_here
    above = lax.ppermute(fields[:, -border:, :], "az", [(i, i + 1) for i in range(n_az - 1)])
    below = lax.ppermute(fields[:, :border, :], "az", [(i + 1, i) for i in range(n_az - 1)])
    fields = jnp.concatenate([above, fields, below], axis=1)
    weight = fields[2, border:-border, border:-border]

    row_global = segment_ordinal * shard_height_total - border + jnp.arange(
        shard_height_total + 2 * border, dtype=jnp.int32)
    col_global = range_index * cols_here - border + jnp.arange(cols_here + 2 * border, dtype=jnp.int32)
    edge_h, grad_h = edge_terms(fields[0, :, :-1], fields[1, :, :-1], fields[2, :, :-1],
                                fields[0, :, 1:], fields[1, :, 1:], fields[2, :, 1:])
    keep_h = ((col_global[:-1] >= 0) & (col_global[:-1] <= cols_here * n_range - 2)).astype(jnp.float32)
    edge_h = edge_h * keep_h[None, :]
    edge_v, grad_v = edge_terms(fields[0, :-1], fields[1, :-1], fields[2, :-1],
                                fields[0, 1:], fields[1, 1:], fields[2, 1:])
    keep_v = ((row_global[:-1] >= 0) & (row_global[:-1] <= shard_height_total * n_az - 2)).astype(jnp.float32)
    edge_v = edge_v * keep_v[:, None]
    flux_h = edge_h * grad_h
    flux_v = edge_v * grad_v
    east_w = edge_h[1:-1, 1:]
    west_w = edge_h[1:-1, :-1]
    south_w = edge_v[1:, 1:-1]
    north_w = edge_v[:-1, 1:-1]
    diag_w = east_w + west_w + south_w + north_w + MU * 4.0**0
    ops_w = (east_w, west_w, south_w, north_w, diag_w)
    rhs_wide = -(flux_h[1:-1, 1:] - flux_h[1:-1, :-1] + flux_v[1:, 1:-1] - flux_v[:-1, 1:-1])

    def crop(values, ring):
        cut = (values.shape[-2] - shard_height_total) // 2 - ring
        if cut == 0:
            return values
        return values[..., cut:-cut, cut:-cut]

    def ops_at(ring):
        return tuple(crop(x, ring) for x in ops_w)

    levels, coarse_edges = build_levels(*ops_at(0)[:4], first_level=0, last_level=GATHER_LEVEL)
    block_h, block_w = coarse_edges[0].shape
    whole = {}

    def coarse_solve(rhs_vec, ring, sums):
        if not whole:
            got, summed = gather_strip(jnp.stack([coarse_edges[0], coarse_edges[2], rhs_vec]), sums)
            east_s, south_s = got[0], got[1]
            whole["levels"] = build_levels(east_s, shifted(east_s, 1), south_s, shifted(south_s, 0),
                                           GATHER_LEVEL, LEVELS)[0]
            strip_rhs = got[2]
        else:
            got, summed = gather_strip(rhs_vec[None], sums)
            strip_rhs = got[0]
        strip_x = vcycle(strip_rhs, GATHER_LEVEL, whole["levels"], apply_padded, None)
        coarse_ring = ring // 2
        strip_x = jnp.pad(strip_x, ((coarse_ring, coarse_ring), (0, 0)))
        return lax.dynamic_slice(strip_x, (segment_ordinal * block_h, block_w - coarse_ring),
                                 (block_h + 2 * coarse_ring, block_w + 2 * coarse_ring)), summed

    def precondition(rhs_wide, sums=None):
        ring = (rhs_wide.shape[0] - shard_height_total) // 2
        diag_here = ops_at(ring)[4]
        estimate = OMEGA * rhs_wide / diag_here
        remain = crop(rhs_wide, 0) - apply_inner(crop(estimate, 1), levels[0])
        patch, summed = coarse_solve(restrict_sum(remain), ring, sums)
        estimate = estimate + prolong_copy(patch)
        inner = ops_at(ring - 1)
        smoothed = crop(estimate, ring - 1) + OMEGA * (crop(rhs_wide, ring - 1) - apply_inner(estimate, inner)) / inner[4]
        return smoothed, apply_inner(smoothed, ops_at(ring - 2)), summed

    def ring_of(values):
        return (values.shape[-2] - shard_height_total) // 2

    def own_sums(*pairs):
        return jnp.stack([jnp.sum(crop(a, 0) * crop(b, 0)) for a, b in pairs])

    residual_wide = rhs_wide
    precond, image_u, _ = precondition(residual_wide)
    sums = own_sums((residual_wide, precond), (image_u, precond))
    if ITERS > 1:
        pre_image, image_pre, sums = precondition(image_u, sums)
    else:
        sums = total(sums)
    norm_now = sums[0]
    curvature = sums[1]
    step_length = norm_now / curvature
    direction, image_vec = precond, image_u
    if ITERS > 1:
        pre_dir, image_pre_dir = pre_image, image_pre
    solution = step_length * crop(direction, 0)
    for step_index in range(1, ITERS):
        residual_wide = crop(residual_wide, ring_of(image_vec)) - step_length * image_vec
        precond = crop(precond, ring_of(pre_dir)) - step_length * pre_dir
        image_u = crop(image_u, ring_of(image_pre_dir)) - step_length * image_pre_dir
        sums = own_sums((residual_wide, precond), (image_u, precond), (precond, image_vec))
        if step_index + 1 < ITERS:
            pre_image, image_pre, sums = precondition(image_u, sums)
        else:
            sums = total(sums)
        norm_next = sums[0]
        ratio = norm_next / norm_now
        curvature = sums[1] + 2.0 * ratio * sums[2] + ratio * ratio * curvature
        step_length = norm_next / curvature
        direction = precond + ratio * crop(direction, ring_of(precond))
        image_vec = image_u + ratio * crop(image_vec, ring_of(image_u))
        if step_index + 1 < ITERS:
            pre_dir = pre_image + ratio * crop(pre_dir, ring_of(pre_image))
            image_pre_dir = image_pre + ratio * crop(image_pre_dir, ring_of(image_pre))
        solution = solution + step_length * crop(direction, 0)
        norm_now = norm_next
    return (solution, weight)


def solution(mesh):
    return jax.shard_map(
        local,
        mesh=mesh,
        in_specs=(P(None, ("az", "rg"), None), P(None, ("az", "rg"), None), P(), P()),
        out_specs=(P("az", "rg"), P("az", "rg")),
        check_vma=False,
    )
```

```python
import jax
import jax.numpy as jnp
from jax import lax
from jax.sharding import PartitionSpec as P
from jax.experimental import pallas as pl
from jax.experimental.pallas import tpu as pltpu

LOOK = 5
LEVELS = 6
ITERS = 3
SWEEPS = 4
SEGMENT_HEIGHT = 160
GATHER_LEVEL = 1


OMEGA = 0.6
MU = 0.01


def neighbours(v):
    n_az = lax.axis_size("az")
    n_rg = lax.axis_size("rg")
    above = lax.ppermute(v[..., -1:, :], "az", [(i, i + 1) for i in range(n_az - 1)])
    below = lax.ppermute(v[..., :1, :], "az", [(i + 1, i) for i in range(n_az - 1)])
    left = lax.ppermute(v[..., :, -1:], "rg", [(i, i + 1) for i in range(n_rg - 1)])
    right = lax.ppermute(v[..., :, :1], "rg", [(i + 1, i) for i in range(n_rg - 1)])
    north = jnp.concatenate([above, v[..., :-1, :]], axis=-2)
    south = jnp.concatenate([v[..., 1:, :], below], axis=-2)
    west = jnp.concatenate([left, v[..., :, :-1]], axis=-1)
    east = jnp.concatenate([v[..., :, 1:], right], axis=-1)
    return north, south, west, east


def apply_halo(vector, operators):
    east, west, south, north, diagonal = operators
    v_n, v_s, v_w, v_e = neighbours(vector)
    return diagonal * vector - east * v_e - west * v_w - south * v_s - north * v_n


def extended(v, width):
    n_az = lax.axis_size("az")
    n_rg = lax.axis_size("rg")
    above = lax.ppermute(v[..., -width:, :], "az", [(i, i + 1) for i in range(n_az - 1)])
    below = lax.ppermute(v[..., :width, :], "az", [(i + 1, i) for i in range(n_az - 1)])
    v = jnp.concatenate([above, v, below], axis=-2)
    left = lax.ppermute(v[..., :, -width:], "rg", [(i, i + 1) for i in range(n_rg - 1)])
    right = lax.ppermute(v[..., :, :width], "rg", [(i + 1, i) for i in range(n_rg - 1)])
    return jnp.concatenate([left, v, right], axis=-1)


def apply_inner(padded, operators):
    east, west, south, north, diagonal = operators
    return (diagonal * padded[1:-1, 1:-1] - east * padded[1:-1, 2:] - west * padded[1:-1, :-2]
            - south * padded[2:, 1:-1] - north * padded[:-2, 1:-1])


def apply_padded(vector, operators):
    east, west, south, north, diagonal = operators
    padded = jnp.pad(vector, 1)
    return (diagonal * vector - east * padded[1:-1, 2:] - west * padded[1:-1, :-2]
            - south * padded[2:, 1:-1] - north * padded[:-2, 1:-1])


def multilook_kernel(bounds_ref, lead_ref, trail_ref, out_ref):
    shape = lead_ref.shape[1:]
    line = lax.broadcasted_iota(jnp.int32, shape, 0)
    column = pl.program_id(0) * shape[1] + lax.broadcasted_iota(jnp.int32, shape, 1)
    mask = ((line >= bounds_ref[0]) & (line < bounds_ref[1]) & (column >= bounds_ref[2])
            & (column < bounds_ref[3])).astype(jnp.float32)
    first_re = lead_ref[0].astype(jnp.float32) * mask
    first_im = lead_ref[1].astype(jnp.float32) * mask
    second_re = trail_ref[0].astype(jnp.float32) * mask
    second_im = trail_ref[1].astype(jnp.float32) * mask
    products = (
        first_re * second_re + first_im * second_im,
        first_im * second_re - first_re * second_im,
        first_re * first_re + first_im * first_im,
        second_re * second_re + second_im * second_im,
    )
    for part, values in enumerate(products):
        for group in range(out_ref.shape[1]):
            acc = values[group * LOOK:group * LOOK + 1, :]
            for offset in range(1, LOOK):
                acc = acc + values[group * LOOK + offset:group * LOOK + offset + 1, :]
            out_ref[part, group:group + 1, :] = acc


def mean_multilook(leading, trailing, bounds):
    _, height_rows, width_cols = leading.shape
    block = 1024
    rows = pl.pallas_call(
        multilook_kernel,
        grid=(width_cols // block,),
        in_specs=[
            pl.BlockSpec(memory_space=pltpu.SMEM),
            pl.BlockSpec((2, height_rows, block), lambda j: (0, 0, j)),
            pl.BlockSpec((2, height_rows, block), lambda j: (0, 0, j)),
        ],
        out_specs=pl.BlockSpec((4, height_rows // LOOK, block), lambda j: (0, 0, j)),
        out_shape=jax.ShapeDtypeStruct((4, height_rows // LOOK, width_cols), jnp.float32),
    )(bounds, leading, trailing)
    span = LOOK * 128
    grouped = rows.reshape(4, height_rows // LOOK, width_cols // span, span)
    cols = jnp.einsum("pikc,cd->pikd", grouped, group_sum(span, LOOK).T, precision=HIGHEST)
    return cols.reshape(4, height_rows // LOOK, width_cols // LOOK)


def edge_terms(left_re, left_im, left_weight, right_re, right_im, right_weight):
    edge_weight = 0.5 * (left_weight + right_weight)
    cross_im = right_im * left_re - right_re * left_im
    power_sum = (
        left_re * left_re + left_im * left_im + right_re * right_re + right_im * right_im + 1.0
    )
    return (edge_weight, 2.0 * cross_im / power_sum)


HIGHEST = lax.Precision.HIGHEST


def group_sum(n, size):
    group = lax.broadcasted_iota(jnp.int32, (n // size, n), 0)
    cell = lax.broadcasted_iota(jnp.int32, (n // size, n), 1)
    return (cell // size == group).astype(jnp.float32)


def pick(n, offset):
    group = lax.broadcasted_iota(jnp.int32, (n // 2, n), 0)
    cell = lax.broadcasted_iota(jnp.int32, (n // 2, n), 1)
    return (cell == 2 * group + offset).astype(jnp.float32)


def sandwich(left, vector, right):
    inner = jnp.dot(left, vector, precision=HIGHEST)
    return jnp.dot(inner, right, precision=HIGHEST)


def restrict_sum(vector):
    rows_now, cols_now = vector.shape
    return sandwich(group_sum(rows_now, 2), vector, group_sum(cols_now, 2).T)


def prolong_copy(vector):
    rows_now, cols_now = vector.shape
    return sandwich(group_sum(2 * rows_now, 2).T, vector, group_sum(2 * cols_now, 2))


def coarsen(east, west, south, north):
    rows_now, cols_now = east.shape
    row_sum = group_sum(rows_now, 2)
    col_sum = group_sum(cols_now, 2).T
    return (
        sandwich(row_sum, east, pick(cols_now, 1).T),
        sandwich(row_sum, west, pick(cols_now, 0).T),
        sandwich(pick(rows_now, 1), south, col_sum),
        sandwich(pick(rows_now, 0), north, col_sum),
    )


def build_levels(east, west, south, north, first_level, last_level):
    levels = {}
    for level in range(first_level, last_level):
        diagonal = east + west + south + north + MU * 4.0**level
        levels[level] = (east, west, south, north, diagonal)
        if level + 1 < LEVELS:
            east, west, south, north = coarsen(east, west, south, north)
    return levels, (east, west, south, north)


def jacobi_sweeps(rhs_vec, operators, apply_fn):
    estimate = OMEGA * rhs_vec / operators[4]
    for sweep_index in range(SWEEPS - 1):
        estimate = estimate + OMEGA * (rhs_vec - apply_fn(estimate, operators)) / operators[4]
    return estimate


def vcycle(rhs_vec, level, levels, apply_fn, stop_fn):
    if level == LEVELS - 1:
        return jacobi_sweeps(rhs_vec, levels[level], apply_fn)
    if stop_fn is not None and level == GATHER_LEVEL:
        return stop_fn(rhs_vec)
    diagonal = levels[level][4]
    estimate = OMEGA * rhs_vec / diagonal
    remain = rhs_vec - apply_fn(estimate, levels[level])
    correction = vcycle(restrict_sum(remain), level + 1, levels, apply_fn, stop_fn)
    estimate = estimate + prolong_copy(correction)
    return estimate + OMEGA * (rhs_vec - apply_fn(estimate, levels[level])) / diagonal


def everyone():
    return lax.axis_size("az") * lax.axis_size("rg")


def gather_strip(blocks, sums=None):
    n_az = lax.axis_size("az")
    n_rg = lax.axis_size("rg")
    count, h, w = blocks.shape
    if sums is not None:
        extra = jnp.zeros((1, h, w), jnp.float32).at[0, 0, :sums.shape[0]].set(sums)
        blocks = jnp.concatenate([blocks, extra])
    sent = jnp.broadcast_to(blocks[None], (n_az,) + blocks.shape)
    got = lax.all_to_all(sent, "az", 0, 0, tiled=True)
    summed = None
    if sums is not None:
        column_sums = jnp.sum(got[:, count, 0, :sums.shape[0]], axis=0)
        rows = lax.all_to_all(jnp.broadcast_to(column_sums[None], (n_rg, sums.shape[0])), "rg", 0, 0, tiled=True)
        summed = jnp.sum(rows, axis=0)
        got = got[:, :count]
    column = got.transpose(1, 0, 2, 3).reshape(count, n_az * h, w)
    left = lax.ppermute(column, "rg", [(i, i + 1) for i in range(n_rg - 1)])
    right = lax.ppermute(column, "rg", [(i + 1, i) for i in range(n_rg - 1)])
    return jnp.concatenate([left, column, right], axis=-1), summed


def shifted(values, axis):
    pad = [(0, 0)] * values.ndim
    pad[axis] = (1, 0)
    return lax.slice_in_dim(jnp.pad(values, pad), 0, values.shape[axis], axis=axis)


def total(values):
    n = everyone()
    sent = jnp.broadcast_to(values[None], (n, values.shape[0]))
    got = lax.all_to_all(sent, ("az", "rg"), 0, 0, tiled=True)
    return jnp.sum(got, axis=0)


def local(master_phasor_raster, slave_phasor_raster, segment_track_trim, segment_slant_trim):
    n_az = lax.axis_size("az")
    n_range = lax.axis_size("rg")
    segment_ordinal = lax.axis_index("az")
    range_index = lax.axis_index("rg")
    track_trim_width = lax.dynamic_index_in_dim(
        segment_track_trim, segment_ordinal, 0, keepdims=False
    )
    slant_trim_width = lax.dynamic_index_in_dim(
        segment_slant_trim, segment_ordinal, 0, keepdims=False
    )
    lines_here = master_phasor_raster.shape[1]
    slant_sample_total = master_phasor_raster.shape[2]
    first_line = range_index * lines_here
    bounds = jnp.stack([
        track_trim_width[0] - first_line,
        SEGMENT_HEIGHT - track_trim_width[1] - first_line,
        slant_trim_width[0],
        slant_sample_total - slant_trim_width[1],
    ]).astype(jnp.int32)
    pixel_totals = mean_multilook(master_phasor_raster, slave_phasor_raster, bounds)
    look_re, look_im, power_one, power_two = (
        pixel_totals[0],
        pixel_totals[1],
        pixel_totals[2],
        pixel_totals[3],
    )
    weight = 0.05 + 4.0 * (look_re * look_re + look_im * look_im) / jnp.maximum(
        power_one * power_two, 1.0
    )
    widest = 2 * ITERS
    border = widest + 1
    fields = jnp.stack([look_re, look_im, weight])
    n_fields, rows_here, cols_all = fields.shape
    cols_here = cols_all // n_range
    main = fields.reshape(n_fields, rows_here, n_range, cols_here).transpose(2, 0, 1, 3)
    zero = jnp.zeros((1, n_fields, rows_here, border), jnp.float32)
    before = jnp.concatenate([zero, main[:-1, :, :, -border:]], axis=0)
    after = jnp.concatenate([main[1:, :, :, :border], zero], axis=0)
    fields = jnp.concatenate([before, main, after], axis=-1)
    fields = lax.all_to_all(fields, "rg", 0, 0, tiled=True)
    fields = fields.transpose(1, 0, 2, 3).reshape(n_fields, n_range * rows_here, cols_here + 2 * border)
    shard_height_total = n_range * rows_here
    above = lax.ppermute(fields[:, -border:, :], "az", [(i, i + 1) for i in range(n_az - 1)])
    below = lax.ppermute(fields[:, :border, :], "az", [(i + 1, i) for i in range(n_az - 1)])
    fields = jnp.concatenate([above, fields, below], axis=1)
    weight = fields[2, border:-border, border:-border]

    row_global = segment_ordinal * shard_height_total - border + jnp.arange(
        shard_height_total + 2 * border, dtype=jnp.int32)
    col_global = range_index * cols_here - border + jnp.arange(cols_here + 2 * border, dtype=jnp.int32)
    edge_h, grad_h = edge_terms(fields[0, :, :-1], fields[1, :, :-1], fields[2, :, :-1],
                                fields[0, :, 1:], fields[1, :, 1:], fields[2, :, 1:])
    keep_h = ((col_global[:-1] >= 0) & (col_global[:-1] <= cols_here * n_range - 2)).astype(jnp.float32)
    edge_h = edge_h * keep_h[None, :]
    edge_v, grad_v = edge_terms(fields[0, :-1], fields[1, :-1], fields[2, :-1],
                                fields[0, 1:], fields[1, 1:], fields[2, 1:])
    keep_v = ((row_global[:-1] >= 0) & (row_global[:-1] <= shard_height_total * n_az - 2)).astype(jnp.float32)
    edge_v = edge_v * keep_v[:, None]
    flux_h = edge_h * grad_h
    flux_v = edge_v * grad_v
    east_w = edge_h[1:-1, 1:]
    west_w = edge_h[1:-1, :-1]
    south_w = edge_v[1:, 1:-1]
    north_w = edge_v[:-1, 1:-1]
    diag_w = east_w + west_w + south_w + north_w + MU * 4.0**0
    ops_w = (east_w, west_w, south_w, north_w, diag_w)
    rhs_wide = -(flux_h[1:-1, 1:] - flux_h[1:-1, :-1] + flux_v[1:, 1:-1] - flux_v[:-1, 1:-1])

    def crop(values, ring):
        cut = (values.shape[-2] - shard_height_total) // 2 - ring
        if cut == 0:
            return values
        return values[..., cut:-cut, cut:-cut]

    def ops_at(ring):
        return tuple(crop(x, ring) for x in ops_w)

    levels, coarse_edges = build_levels(*ops_at(0)[:4], first_level=0, last_level=GATHER_LEVEL)
    block_h, block_w = coarse_edges[0].shape
    whole = {}

    def coarse_solve(rhs_vec, ring, sums):
        if not whole:
            got, summed = gather_strip(jnp.stack([coarse_edges[0], coarse_edges[2], rhs_vec]), sums)
            east_s, south_s = got[0], got[1]
            whole["levels"] = build_levels(east_s, shifted(east_s, 1), south_s, shifted(south_s, 0),
                                           GATHER_LEVEL, LEVELS)[0]
            strip_rhs = got[2]
        else:
            got, summed = gather_strip(rhs_vec[None], sums)
            strip_rhs = got[0]
        strip_x = vcycle(strip_rhs, GATHER_LEVEL, whole["levels"], apply_padded, None)
        coarse_ring = ring // 2
        strip_x = jnp.pad(strip_x, ((coarse_ring, coarse_ring), (0, 0)))
        return lax.dynamic_slice(strip_x, (segment_ordinal * block_h, block_w - coarse_ring),
                                 (block_h + 2 * coarse_ring, block_w + 2 * coarse_ring)), summed

    def precondition(rhs_wide, sums=None):
        ring = (rhs_wide.shape[0] - shard_height_total) // 2
        diag_here = ops_at(ring)[4]
        estimate = OMEGA * rhs_wide / diag_here
        remain = crop(rhs_wide, 0) - apply_inner(crop(estimate, 1), levels[0])
        patch, summed = coarse_solve(restrict_sum(remain), ring, sums)
        estimate = estimate + prolong_copy(patch)
        inner = ops_at(ring - 1)
        smoothed = crop(estimate, ring - 1) + OMEGA * (crop(rhs_wide, ring - 1) - apply_inner(estimate, inner)) / inner[4]
        return smoothed, apply_inner(smoothed, ops_at(ring - 2)), summed

    def ring_of(values):
        return (values.shape[-2] - shard_height_total) // 2

    def own_sums(*pairs):
        return jnp.stack([jnp.sum(crop(a, 0) * crop(b, 0)) for a, b in pairs])

    residual_wide = rhs_wide
    precond, image_u, _ = precondition(residual_wide)
    sums = own_sums((residual_wide, precond), (image_u, precond))
    if ITERS > 1:
        pre_image, image_pre, sums = precondition(image_u, sums)
    else:
        sums = total(sums)
    norm_now = sums[0]
    curvature = sums[1]
    step_length = norm_now / curvature
    direction, image_vec = precond, image_u
    if ITERS > 1:
        pre_dir, image_pre_dir = pre_image, image_pre
    solution = step_length * crop(direction, 0)
    for step_index in range(1, ITERS):
        residual_wide = crop(residual_wide, ring_of(image_vec)) - step_length * image_vec
        precond = crop(precond, ring_of(pre_dir)) - step_length * pre_dir
        image_u = crop(image_u, ring_of(image_pre_dir)) - step_length * image_pre_dir
        sums = own_sums((residual_wide, precond), (image_u, precond), (precond, image_vec))
        if step_index + 1 < ITERS:
            pre_image, image_pre, sums = precondition(image_u, sums)
        else:
            sums = total(sums)
        norm_next = sums[0]
        ratio = norm_next / norm_now
        curvature = sums[1] + 2.0 * ratio * sums[2] + ratio * ratio * curvature
        step_length = norm_next / curvature
        direction = precond + ratio * crop(direction, ring_of(precond))
        image_vec = image_u + ratio * crop(image_vec, ring_of(image_u))
        if step_index + 1 < ITERS:
            pre_dir = pre_image + ratio * crop(pre_dir, ring_of(pre_image))
            image_pre_dir = image_pre + ratio * crop(image_pre_dir, ring_of(image_pre))
        solution = solution + step_length * crop(direction, 0)
        norm_now = norm_next
    return (solution, weight)


def solution(mesh):
    return jax.shard_map(
        local,
        mesh=mesh,
        in_specs=(P(None, ("az", "rg"), None), P(None, ("az", "rg"), None), P(), P()),
        out_specs=(P("az", "rg"), P("az", "rg")),
        check_vma=False,
    )
```

```python
import jax
import jax.numpy as jnp
from jax import lax
from jax.sharding import PartitionSpec as P
from jax.experimental import pallas as pl
from jax.experimental.pallas import tpu as pltpu

LOOK = 5
LEVELS = 6
ITERS = 3
SWEEPS = 4
SEGMENT_HEIGHT = 160
GATHER_LEVEL = 1


OMEGA = 0.6
MU = 0.01


def neighbours(v):
    n_az = lax.axis_size("az")
    n_rg = lax.axis_size("rg")
    above = lax.ppermute(v[..., -1:, :], "az", [(i, i + 1) for i in range(n_az - 1)])
    below = lax.ppermute(v[..., :1, :], "az", [(i + 1, i) for i in range(n_az - 1)])
    left = lax.ppermute(v[..., :, -1:], "rg", [(i, i + 1) for i in range(n_rg - 1)])
    right = lax.ppermute(v[..., :, :1], "rg", [(i + 1, i) for i in range(n_rg - 1)])
    north = jnp.concatenate([above, v[..., :-1, :]], axis=-2)
    south = jnp.concatenate([v[..., 1:, :], below], axis=-2)
    west = jnp.concatenate([left, v[..., :, :-1]], axis=-1)
    east = jnp.concatenate([v[..., :, 1:], right], axis=-1)
    return north, south, west, east


def apply_halo(vector, operators):
    east, west, south, north, diagonal = operators
    v_n, v_s, v_w, v_e = neighbours(vector)
    return diagonal * vector - east * v_e - west * v_w - south * v_s - north * v_n


def extended(v, width):
    n_az = lax.axis_size("az")
    n_rg = lax.axis_size("rg")
    above = lax.ppermute(v[..., -width:, :], "az", [(i, i + 1) for i in range(n_az - 1)])
    below = lax.ppermute(v[..., :width, :], "az", [(i + 1, i) for i in range(n_az - 1)])
    v = jnp.concatenate([above, v, below], axis=-2)
    left = lax.ppermute(v[..., :, -width:], "rg", [(i, i + 1) for i in range(n_rg - 1)])
    right = lax.ppermute(v[..., :, :width], "rg", [(i + 1, i) for i in range(n_rg - 1)])
    return jnp.concatenate([left, v, right], axis=-1)


def apply_inner(padded, operators):
    east, west, south, north, diagonal = operators
    return (diagonal * padded[1:-1, 1:-1] - east * padded[1:-1, 2:] - west * padded[1:-1, :-2]
            - south * padded[2:, 1:-1] - north * padded[:-2, 1:-1])


def apply_padded(vector, operators):
    east, west, south, north, diagonal = operators
    padded = jnp.pad(vector, 1)
    return (diagonal * vector - east * padded[1:-1, 2:] - west * padded[1:-1, :-2]
            - south * padded[2:, 1:-1] - north * padded[:-2, 1:-1])


def multilook_kernel(bounds_ref, lead_ref, trail_ref, out_ref):
    shape = lead_ref.shape[1:]
    line = lax.broadcasted_iota(jnp.int32, shape, 0)
    column = pl.program_id(0) * shape[1] + lax.broadcasted_iota(jnp.int32, shape, 1)
    mask = ((line >= bounds_ref[0]) & (line < bounds_ref[1]) & (column >= bounds_ref[2])
            & (column < bounds_ref[3])).astype(jnp.float32)
    first_re = lead_ref[0].astype(jnp.float32) * mask
    first_im = lead_ref[1].astype(jnp.float32) * mask
    second_re = trail_ref[0].astype(jnp.float32) * mask
    second_im = trail_ref[1].astype(jnp.float32) * mask
    products = (
        first_re * second_re + first_im * second_im,
        first_im * second_re - first_re * second_im,
        first_re * first_re + first_im * first_im,
        second_re * second_re + second_im * second_im,
    )
    for part, values in enumerate(products):
        for group in range(out_ref.shape[1]):
            acc = values[group * LOOK:group * LOOK + 1, :]
            for offset in range(1, LOOK):
                acc = acc + values[group * LOOK + offset:group * LOOK + offset + 1, :]
            out_ref[part, group:group + 1, :] = acc


def mean_multilook(leading, trailing, bounds):
    _, height_rows, width_cols = leading.shape
    block = 2560
    rows = pl.pallas_call(
        multilook_kernel,
        grid=(width_cols // block,),
        in_specs=[
            pl.BlockSpec(memory_space=pltpu.SMEM),
            pl.BlockSpec((2, height_rows, block), lambda j: (0, 0, j)),
            pl.BlockSpec((2, height_rows, block), lambda j: (0, 0, j)),
        ],
        out_specs=pl.BlockSpec((4, height_rows // LOOK, block), lambda j: (0, 0, j)),
        out_shape=jax.ShapeDtypeStruct((4, height_rows // LOOK, width_cols), jnp.float32),
    )(bounds, leading, trailing)
    span = LOOK * 128
    grouped = rows.reshape(4, height_rows // LOOK, width_cols // span, span)
    cols = jnp.einsum("pikc,cd->pikd", grouped, group_sum(span, LOOK).T, precision=HIGHEST)
    return cols.reshape(4, height_rows // LOOK, width_cols // LOOK)


def edge_terms(left_re, left_im, left_weight, right_re, right_im, right_weight):
    edge_weight = 0.5 * (left_weight + right_weight)
    cross_im = right_im * left_re - right_re * left_im
    power_sum = (
        left_re * left_re + left_im * left_im + right_re * right_re + right_im * right_im + 1.0
    )
    return (edge_weight, 2.0 * cross_im / power_sum)


HIGHEST = lax.Precision.HIGHEST


def group_sum(n, size):
    group = lax.broadcasted_iota(jnp.int32, (n // size, n), 0)
    cell = lax.broadcasted_iota(jnp.int32, (n // size, n), 1)
    return (cell // size == group).astype(jnp.float32)


def pick(n, offset):
    group = lax.broadcasted_iota(jnp.int32, (n // 2, n), 0)
    cell = lax.broadcasted_iota(jnp.int32, (n // 2, n), 1)
    return (cell == 2 * group + offset).astype(jnp.float32)


def sandwich(left, vector, right):
    inner = jnp.dot(left, vector, precision=HIGHEST)
    return jnp.dot(inner, right, precision=HIGHEST)


def restrict_sum(vector):
    rows_now, cols_now = vector.shape
    return sandwich(group_sum(rows_now, 2), vector, group_sum(cols_now, 2).T)


def prolong_copy(vector):
    rows_now, cols_now = vector.shape
    return sandwich(group_sum(2 * rows_now, 2).T, vector, group_sum(2 * cols_now, 2))


def coarsen(east, west, south, north):
    rows_now, cols_now = east.shape
    row_sum = group_sum(rows_now, 2)
    col_sum = group_sum(cols_now, 2).T
    return (
        sandwich(row_sum, east, pick(cols_now, 1).T),
        sandwich(row_sum, west, pick(cols_now, 0).T),
        sandwich(pick(rows_now, 1), south, col_sum),
        sandwich(pick(rows_now, 0), north, col_sum),
    )


def build_levels(east, west, south, north, first_level, last_level):
    levels = {}
    for level in range(first_level, last_level):
        diagonal = east + west + south + north + MU * 4.0**level
        levels[level] = (east, west, south, north, diagonal)
        if level + 1 < LEVELS:
            east, west, south, north = coarsen(east, west, south, north)
    return levels, (east, west, south, north)


def jacobi_sweeps(rhs_vec, operators, apply_fn):
    estimate = OMEGA * rhs_vec / operators[4]
    for sweep_index in range(SWEEPS - 1):
        estimate = estimate + OMEGA * (rhs_vec - apply_fn(estimate, operators)) / operators[4]
    return estimate


def vcycle(rhs_vec, level, levels, apply_fn, stop_fn):
    if level == LEVELS - 1:
        return jacobi_sweeps(rhs_vec, levels[level], apply_fn)
    if stop_fn is not None and level == GATHER_LEVEL:
        return stop_fn(rhs_vec)
    diagonal = levels[level][4]
    estimate = OMEGA * rhs_vec / diagonal
    remain = rhs_vec - apply_fn(estimate, levels[level])
    correction = vcycle(restrict_sum(remain), level + 1, levels, apply_fn, stop_fn)
    estimate = estimate + prolong_copy(correction)
    return estimate + OMEGA * (rhs_vec - apply_fn(estimate, levels[level])) / diagonal


def everyone():
    return lax.axis_size("az") * lax.axis_size("rg")


def gather_strip(blocks, sums=None):
    n_az = lax.axis_size("az")
    n_rg = lax.axis_size("rg")
    count, h, w = blocks.shape
    if sums is not None:
        extra = jnp.zeros((1, h, w), jnp.float32).at[0, 0, :sums.shape[0]].set(sums)
        blocks = jnp.concatenate([blocks, extra])
    sent = jnp.broadcast_to(blocks[None], (n_az,) + blocks.shape)
    got = lax.all_to_all(sent, "az", 0, 0, tiled=True)
    summed = None
    if sums is not None:
        column_sums = jnp.sum(got[:, count, 0, :sums.shape[0]], axis=0)
        rows = lax.all_to_all(jnp.broadcast_to(column_sums[None], (n_rg, sums.shape[0])), "rg", 0, 0, tiled=True)
        summed = jnp.sum(rows, axis=0)
        got = got[:, :count]
    column = got.transpose(1, 0, 2, 3).reshape(count, n_az * h, w)
    left = lax.ppermute(column, "rg", [(i, i + 1) for i in range(n_rg - 1)])
    right = lax.ppermute(column, "rg", [(i + 1, i) for i in range(n_rg - 1)])
    return jnp.concatenate([left, column, right], axis=-1), summed


def shifted(values, axis):
    pad = [(0, 0)] * values.ndim
    pad[axis] = (1, 0)
    return lax.slice_in_dim(jnp.pad(values, pad), 0, values.shape[axis], axis=axis)


def total(values):
    n = everyone()
    sent = jnp.broadcast_to(values[None], (n, values.shape[0]))
    got = lax.all_to_all(sent, ("az", "rg"), 0, 0, tiled=True)
    return jnp.sum(got, axis=0)


def local(master_phasor_raster, slave_phasor_raster, segment_track_trim, segment_slant_trim):
    n_az = lax.axis_size("az")
    n_range = lax.axis_size("rg")
    segment_ordinal = lax.axis_index("az")
    range_index = lax.axis_index("rg")
    track_trim_width = lax.dynamic_index_in_dim(
        segment_track_trim, segment_ordinal, 0, keepdims=False
    )
    slant_trim_width = lax.dynamic_index_in_dim(
        segment_slant_trim, segment_ordinal, 0, keepdims=False
    )
    lines_here = master_phasor_raster.shape[1]
    slant_sample_total = master_phasor_raster.shape[2]
    first_line = range_index * lines_here
    bounds = jnp.stack([
        track_trim_width[0] - first_line,
        SEGMENT_HEIGHT - track_trim_width[1] - first_line,
        slant_trim_width[0],
        slant_sample_total - slant_trim_width[1],
    ]).astype(jnp.int32)
    pixel_totals = mean_multilook(master_phasor_raster, slave_phasor_raster, bounds)
    look_re, look_im, power_one, power_two = (
        pixel_totals[0],
        pixel_totals[1],
        pixel_totals[2],
        pixel_totals[3],
    )
    weight = 0.05 + 4.0 * (look_re * look_re + look_im * look_im) / jnp.maximum(
        power_one * power_two, 1.0
    )
    widest = 2 * ITERS
    border = widest + 1
    fields = jnp.stack([look_re, look_im, weight])
    n_fields, rows_here, cols_all = fields.shape
    cols_here = cols_all // n_range
    main = fields.reshape(n_fields, rows_here, n_range, cols_here).transpose(2, 0, 1, 3)
    zero = jnp.zeros((1, n_fields, rows_here, border), jnp.float32)
    before = jnp.concatenate([zero, main[:-1, :, :, -border:]], axis=0)
    after = jnp.concatenate([main[1:, :, :, :border], zero], axis=0)
    fields = jnp.concatenate([before, main, after], axis=-1)
    fields = lax.all_to_all(fields, "rg", 0, 0, tiled=True)
    fields = fields.transpose(1, 0, 2, 3).reshape(n_fields, n_range * rows_here, cols_here + 2 * border)
    shard_height_total = n_range * rows_here
    above = lax.ppermute(fields[:, -border:, :], "az", [(i, i + 1) for i in range(n_az - 1)])
    below = lax.ppermute(fields[:, :border, :], "az", [(i + 1, i) for i in range(n_az - 1)])
    fields = jnp.concatenate([above, fields, below], axis=1)
    weight = fields[2, border:-border, border:-border]

    row_global = segment_ordinal * shard_height_total - border + jnp.arange(
        shard_height_total + 2 * border, dtype=jnp.int32)
    col_global = range_index * cols_here - border + jnp.arange(cols_here + 2 * border, dtype=jnp.int32)
    edge_h, grad_h = edge_terms(fields[0, :, :-1], fields[1, :, :-1], fields[2, :, :-1],
                                fields[0, :, 1:], fields[1, :, 1:], fields[2, :, 1:])
    keep_h = ((col_global[:-1] >= 0) & (col_global[:-1] <= cols_here * n_range - 2)).astype(jnp.float32)
    edge_h = edge_h * keep_h[None, :]
    edge_v, grad_v = edge_terms(fields[0, :-1], fields[1, :-1], fields[2, :-1],
                                fields[0, 1:], fields[1, 1:], fields[2, 1:])
    keep_v = ((row_global[:-1] >= 0) & (row_global[:-1] <= shard_height_total * n_az - 2)).astype(jnp.float32)
    edge_v = edge_v * keep_v[:, None]
    flux_h = edge_h * grad_h
    flux_v = edge_v * grad_v
    east_w = edge_h[1:-1, 1:]
    west_w = edge_h[1:-1, :-1]
    south_w = edge_v[1:, 1:-1]
    north_w = edge_v[:-1, 1:-1]
    diag_w = east_w + west_w + south_w + north_w + MU * 4.0**0
    ops_w = (east_w, west_w, south_w, north_w, diag_w)
    rhs_wide = -(flux_h[1:-1, 1:] - flux_h[1:-1, :-1] + flux_v[1:, 1:-1] - flux_v[:-1, 1:-1])

    def crop(values, ring):
        cut = (values.shape[-2] - shard_height_total) // 2 - ring
        if cut == 0:
            return values
        return values[..., cut:-cut, cut:-cut]

    def ops_at(ring):
        return tuple(crop(x, ring) for x in ops_w)

    levels, coarse_edges = build_levels(*ops_at(0)[:4], first_level=0, last_level=GATHER_LEVEL)
    block_h, block_w = coarse_edges[0].shape
    whole = {}

    def coarse_solve(rhs_vec, ring, sums):
        if not whole:
            got, summed = gather_strip(jnp.stack([coarse_edges[0], coarse_edges[2], rhs_vec]), sums)
            east_s, south_s = got[0], got[1]
            whole["levels"] = build_levels(east_s, shifted(east_s, 1), south_s, shifted(south_s, 0),
                                           GATHER_LEVEL, LEVELS)[0]
            strip_rhs = got[2]
        else:
            got, summed = gather_strip(rhs_vec[None], sums)
            strip_rhs = got[0]
        strip_x = vcycle(strip_rhs, GATHER_LEVEL, whole["levels"], apply_padded, None)
        coarse_ring = ring // 2
        strip_x = jnp.pad(strip_x, ((coarse_ring, coarse_ring), (0, 0)))
        return lax.dynamic_slice(strip_x, (segment_ordinal * block_h, block_w - coarse_ring),
                                 (block_h + 2 * coarse_ring, block_w + 2 * coarse_ring)), summed

    def precondition(rhs_wide, sums=None):
        ring = (rhs_wide.shape[0] - shard_height_total) // 2
        diag_here = ops_at(ring)[4]
        estimate = OMEGA * rhs_wide / diag_here
        remain = crop(rhs_wide, 0) - apply_inner(crop(estimate, 1), levels[0])
        patch, summed = coarse_solve(restrict_sum(remain), ring, sums)
        estimate = estimate + prolong_copy(patch)
        inner = ops_at(ring - 1)
        smoothed = crop(estimate, ring - 1) + OMEGA * (crop(rhs_wide, ring - 1) - apply_inner(estimate, inner)) / inner[4]
        return smoothed, apply_inner(smoothed, ops_at(ring - 2)), summed

    def ring_of(values):
        return (values.shape[-2] - shard_height_total) // 2

    def own_sums(*pairs):
        return jnp.stack([jnp.sum(crop(a, 0) * crop(b, 0)) for a, b in pairs])

    residual_wide = rhs_wide
    precond, image_u, _ = precondition(residual_wide)
    sums = own_sums((residual_wide, precond), (image_u, precond))
    if ITERS > 1:
        pre_image, image_pre, sums = precondition(image_u, sums)
    else:
        sums = total(sums)
    norm_now = sums[0]
    curvature = sums[1]
    step_length = norm_now / curvature
    direction, image_vec = precond, image_u
    if ITERS > 1:
        pre_dir, image_pre_dir = pre_image, image_pre
    solution = step_length * crop(direction, 0)
    for step_index in range(1, ITERS):
        residual_wide = crop(residual_wide, ring_of(image_vec)) - step_length * image_vec
        precond = crop(precond, ring_of(pre_dir)) - step_length * pre_dir
        image_u = crop(image_u, ring_of(image_pre_dir)) - step_length * image_pre_dir
        sums = own_sums((residual_wide, precond), (image_u, precond), (precond, image_vec))
        if step_index + 1 < ITERS:
            pre_image, image_pre, sums = precondition(image_u, sums)
        else:
            sums = total(sums)
        norm_next = sums[0]
        ratio = norm_next / norm_now
        curvature = sums[1] + 2.0 * ratio * sums[2] + ratio * ratio * curvature
        step_length = norm_next / curvature
        direction = precond + ratio * crop(direction, ring_of(precond))
        image_vec = image_u + ratio * crop(image_vec, ring_of(image_u))
        if step_index + 1 < ITERS:
            pre_dir = pre_image + ratio * crop(pre_dir, ring_of(pre_image))
            image_pre_dir = image_pre + ratio * crop(image_pre_dir, ring_of(image_pre))
        solution = solution + step_length * crop(direction, 0)
        norm_now = norm_next
    return (solution, weight)


def solution(mesh):
    return jax.shard_map(
        local,
        mesh=mesh,
        in_specs=(P(None, ("az", "rg"), None), P(None, ("az", "rg"), None), P(), P()),
        out_specs=(P("az", "rg"), P("az", "rg")),
        check_vma=False,
    )
```

```python
import jax
import jax.numpy as jnp
from jax import lax
from jax.sharding import PartitionSpec as P
from jax.experimental import pallas as pl
from jax.experimental.pallas import tpu as pltpu

LOOK = 5
LEVELS = 6
ITERS = 3
SWEEPS = 4
SEGMENT_HEIGHT = 160
GATHER_LEVEL = 1


OMEGA = 0.6
MU = 0.01


def neighbours(v):
    n_az = lax.axis_size("az")
    n_rg = lax.axis_size("rg")
    above = lax.ppermute(v[..., -1:, :], "az", [(i, i + 1) for i in range(n_az - 1)])
    below = lax.ppermute(v[..., :1, :], "az", [(i + 1, i) for i in range(n_az - 1)])
    left = lax.ppermute(v[..., :, -1:], "rg", [(i, i + 1) for i in range(n_rg - 1)])
    right = lax.ppermute(v[..., :, :1], "rg", [(i + 1, i) for i in range(n_rg - 1)])
    north = jnp.concatenate([above, v[..., :-1, :]], axis=-2)
    south = jnp.concatenate([v[..., 1:, :], below], axis=-2)
    west = jnp.concatenate([left, v[..., :, :-1]], axis=-1)
    east = jnp.concatenate([v[..., :, 1:], right], axis=-1)
    return north, south, west, east


def apply_halo(vector, operators):
    east, west, south, north, diagonal = operators
    v_n, v_s, v_w, v_e = neighbours(vector)
    return diagonal * vector - east * v_e - west * v_w - south * v_s - north * v_n


def extended(v, width):
    n_az = lax.axis_size("az")
    n_rg = lax.axis_size("rg")
    above = lax.ppermute(v[..., -width:, :], "az", [(i, i + 1) for i in range(n_az - 1)])
    below = lax.ppermute(v[..., :width, :], "az", [(i + 1, i) for i in range(n_az - 1)])
    v = jnp.concatenate([above, v, below], axis=-2)
    left = lax.ppermute(v[..., :, -width:], "rg", [(i, i + 1) for i in range(n_rg - 1)])
    right = lax.ppermute(v[..., :, :width], "rg", [(i + 1, i) for i in range(n_rg - 1)])
    return jnp.concatenate([left, v, right], axis=-1)


def apply_inner(padded, operators):
    east, west, south, north, diagonal = operators
    return (diagonal * padded[1:-1, 1:-1] - east * padded[1:-1, 2:] - west * padded[1:-1, :-2]
            - south * padded[2:, 1:-1] - north * padded[:-2, 1:-1])


def apply_padded(vector, operators):
    east, west, south, north, diagonal = operators
    padded = jnp.pad(vector, 1)
    return (diagonal * vector - east * padded[1:-1, 2:] - west * padded[1:-1, :-2]
            - south * padded[2:, 1:-1] - north * padded[:-2, 1:-1])


def multilook_kernel(bounds_ref, lead_ref, trail_ref, out_ref):
    shape = lead_ref.shape[1:]
    line = lax.broadcasted_iota(jnp.int32, shape, 0)
    column = pl.program_id(0) * shape[1] + lax.broadcasted_iota(jnp.int32, shape, 1)
    mask = ((line >= bounds_ref[0]) & (line < bounds_ref[1]) & (column >= bounds_ref[2])
            & (column < bounds_ref[3])).astype(jnp.float32)
    first_re = lead_ref[0].astype(jnp.float32) * mask
    first_im = lead_ref[1].astype(jnp.float32) * mask
    second_re = trail_ref[0].astype(jnp.float32) * mask
    second_im = trail_ref[1].astype(jnp.float32) * mask
    products = (
        first_re * second_re + first_im * second_im,
        first_im * second_re - first_re * second_im,
        first_re * first_re + first_im * first_im,
        second_re * second_re + second_im * second_im,
    )
    for part, values in enumerate(products):
        for group in range(out_ref.shape[1]):
            acc = values[group * LOOK:group * LOOK + 1, :]
            for offset in range(1, LOOK):
                acc = acc + values[group * LOOK + offset:group * LOOK + offset + 1, :]
            out_ref[part, group:group + 1, :] = acc


def mean_multilook(leading, trailing, bounds):
    _, height_rows, width_cols = leading.shape
    block = 5120
    rows = pl.pallas_call(
        multilook_kernel,
        grid=(width_cols // block,),
        in_specs=[
            pl.BlockSpec(memory_space=pltpu.SMEM),
            pl.BlockSpec((2, height_rows, block), lambda j: (0, 0, j)),
            pl.BlockSpec((2, height_rows, block), lambda j: (0, 0, j)),
        ],
        out_specs=pl.BlockSpec((4, height_rows // LOOK, block), lambda j: (0, 0, j)),
        out_shape=jax.ShapeDtypeStruct((4, height_rows // LOOK, width_cols), jnp.float32),
    )(bounds, leading, trailing)
    span = LOOK * 128
    grouped = rows.reshape(4, height_rows // LOOK, width_cols // span, span)
    cols = jnp.einsum("pikc,cd->pikd", grouped, group_sum(span, LOOK).T, precision=HIGHEST)
    return cols.reshape(4, height_rows // LOOK, width_cols // LOOK)


def edge_terms(left_re, left_im, left_weight, right_re, right_im, right_weight):
    edge_weight = 0.5 * (left_weight + right_weight)
    cross_im = right_im * left_re - right_re * left_im
    power_sum = (
        left_re * left_re + left_im * left_im + right_re * right_re + right_im * right_im + 1.0
    )
    return (edge_weight, 2.0 * cross_im / power_sum)


HIGHEST = lax.Precision.HIGHEST


def group_sum(n, size):
    group = lax.broadcasted_iota(jnp.int32, (n // size, n), 0)
    cell = lax.broadcasted_iota(jnp.int32, (n // size, n), 1)
    return (cell // size == group).astype(jnp.float32)


def pick(n, offset):
    group = lax.broadcasted_iota(jnp.int32, (n // 2, n), 0)
    cell = lax.broadcasted_iota(jnp.int32, (n // 2, n), 1)
    return (cell == 2 * group + offset).astype(jnp.float32)


def sandwich(left, vector, right):
    inner = jnp.dot(left, vector, precision=HIGHEST)
    return jnp.dot(inner, right, precision=HIGHEST)


def restrict_sum(vector):
    rows_now, cols_now = vector.shape
    return sandwich(group_sum(rows_now, 2), vector, group_sum(cols_now, 2).T)


def prolong_copy(vector):
    rows_now, cols_now = vector.shape
    return sandwich(group_sum(2 * rows_now, 2).T, vector, group_sum(2 * cols_now, 2))


def coarsen(east, west, south, north):
    rows_now, cols_now = east.shape
    row_sum = group_sum(rows_now, 2)
    col_sum = group_sum(cols_now, 2).T
    return (
        sandwich(row_sum, east, pick(cols_now, 1).T),
        sandwich(row_sum, west, pick(cols_now, 0).T),
        sandwich(pick(rows_now, 1), south, col_sum),
        sandwich(pick(rows_now, 0), north, col_sum),
    )


def build_levels(east, west, south, north, first_level, last_level):
    levels = {}
    for level in range(first_level, last_level):
        diagonal = east + west + south + north + MU * 4.0**level
        levels[level] = (east, west, south, north, diagonal)
        if level + 1 < LEVELS:
            east, west, south, north = coarsen(east, west, south, north)
    return levels, (east, west, south, north)


def jacobi_sweeps(rhs_vec, operators, apply_fn):
    estimate = OMEGA * rhs_vec / operators[4]
    for sweep_index in range(SWEEPS - 1):
        estimate = estimate + OMEGA * (rhs_vec - apply_fn(estimate, operators)) / operators[4]
    return estimate


def vcycle(rhs_vec, level, levels, apply_fn, stop_fn):
    if level == LEVELS - 1:
        return jacobi_sweeps(rhs_vec, levels[level], apply_fn)
    if stop_fn is not None and level == GATHER_LEVEL:
        return stop_fn(rhs_vec)
    diagonal = levels[level][4]
    estimate = OMEGA * rhs_vec / diagonal
    remain = rhs_vec - apply_fn(estimate, levels[level])
    correction = vcycle(restrict_sum(remain), level + 1, levels, apply_fn, stop_fn)
    estimate = estimate + prolong_copy(correction)
    return estimate + OMEGA * (rhs_vec - apply_fn(estimate, levels[level])) / diagonal


def everyone():
    return lax.axis_size("az") * lax.axis_size("rg")


def gather_strip(blocks, sums=None):
    n_az = lax.axis_size("az")
    n_rg = lax.axis_size("rg")
    count, h, w = blocks.shape
    if sums is not None:
        extra = jnp.zeros((1, h, w), jnp.float32).at[0, 0, :sums.shape[0]].set(sums)
        blocks = jnp.concatenate([blocks, extra])
    sent = jnp.broadcast_to(blocks[None], (n_az,) + blocks.shape)
    got = lax.all_to_all(sent, "az", 0, 0, tiled=True)
    summed = None
    if sums is not None:
        column_sums = jnp.sum(got[:, count, 0, :sums.shape[0]], axis=0)
        rows = lax.all_to_all(jnp.broadcast_to(column_sums[None], (n_rg, sums.shape[0])), "rg", 0, 0, tiled=True)
        summed = jnp.sum(rows, axis=0)
        got = got[:, :count]
    column = got.transpose(1, 0, 2, 3).reshape(count, n_az * h, w)
    left = lax.ppermute(column, "rg", [(i, i + 1) for i in range(n_rg - 1)])
    right = lax.ppermute(column, "rg", [(i + 1, i) for i in range(n_rg - 1)])
    return jnp.concatenate([left, column, right], axis=-1), summed


def shifted(values, axis):
    pad = [(0, 0)] * values.ndim
    pad[axis] = (1, 0)
    return lax.slice_in_dim(jnp.pad(values, pad), 0, values.shape[axis], axis=axis)


def total(values):
    n = everyone()
    sent = jnp.broadcast_to(values[None], (n, values.shape[0]))
    got = lax.all_to_all(sent, ("az", "rg"), 0, 0, tiled=True)
    return jnp.sum(got, axis=0)


def local(master_phasor_raster, slave_phasor_raster, segment_track_trim, segment_slant_trim):
    n_az = lax.axis_size("az")
    n_range = lax.axis_size("rg")
    segment_ordinal = lax.axis_index("az")
    range_index = lax.axis_index("rg")
    track_trim_width = lax.dynamic_index_in_dim(
        segment_track_trim, segment_ordinal, 0, keepdims=False
    )
    slant_trim_width = lax.dynamic_index_in_dim(
        segment_slant_trim, segment_ordinal, 0, keepdims=False
    )
    lines_here = master_phasor_raster.shape[1]
    slant_sample_total = master_phasor_raster.shape[2]
    first_line = range_index * lines_here
    bounds = jnp.stack([
        track_trim_width[0] - first_line,
        SEGMENT_HEIGHT - track_trim_width[1] - first_line,
        slant_trim_width[0],
        slant_sample_total - slant_trim_width[1],
    ]).astype(jnp.int32)
    pixel_totals = mean_multilook(master_phasor_raster, slave_phasor_raster, bounds)
    look_re, look_im, power_one, power_two = (
        pixel_totals[0],
        pixel_totals[1],
        pixel_totals[2],
        pixel_totals[3],
    )
    weight = 0.05 + 4.0 * (look_re * look_re + look_im * look_im) / jnp.maximum(
        power_one * power_two, 1.0
    )
    widest = 2 * ITERS
    border = widest + 1
    fields = jnp.stack([look_re, look_im, weight])
    n_fields, rows_here, cols_all = fields.shape
    cols_here = cols_all // n_range
    main = fields.reshape(n_fields, rows_here, n_range, cols_here).transpose(2, 0, 1, 3)
    zero = jnp.zeros((1, n_fields, rows_here, border), jnp.float32)
    before = jnp.concatenate([zero, main[:-1, :, :, -border:]], axis=0)
    after = jnp.concatenate([main[1:, :, :, :border], zero], axis=0)
    fields = jnp.concatenate([before, main, after], axis=-1)
    fields = lax.all_to_all(fields, "rg", 0, 0, tiled=True)
    fields = fields.transpose(1, 0, 2, 3).reshape(n_fields, n_range * rows_here, cols_here + 2 * border)
    shard_height_total = n_range * rows_here
    above = lax.ppermute(fields[:, -border:, :], "az", [(i, i + 1) for i in range(n_az - 1)])
    below = lax.ppermute(fields[:, :border, :], "az", [(i + 1, i) for i in range(n_az - 1)])
    fields = jnp.concatenate([above, fields, below], axis=1)
    weight = fields[2, border:-border, border:-border]

    row_global = segment_ordinal * shard_height_total - border + jnp.arange(
        shard_height_total + 2 * border, dtype=jnp.int32)
    col_global = range_index * cols_here - border + jnp.arange(cols_here + 2 * border, dtype=jnp.int32)
    edge_h, grad_h = edge_terms(fields[0, :, :-1], fields[1, :, :-1], fields[2, :, :-1],
                                fields[0, :, 1:], fields[1, :, 1:], fields[2, :, 1:])
    keep_h = ((col_global[:-1] >= 0) & (col_global[:-1] <= cols_here * n_range - 2)).astype(jnp.float32)
    edge_h = edge_h * keep_h[None, :]
    edge_v, grad_v = edge_terms(fields[0, :-1], fields[1, :-1], fields[2, :-1],
                                fields[0, 1:], fields[1, 1:], fields[2, 1:])
    keep_v = ((row_global[:-1] >= 0) & (row_global[:-1] <= shard_height_total * n_az - 2)).astype(jnp.float32)
    edge_v = edge_v * keep_v[:, None]
    flux_h = edge_h * grad_h
    flux_v = edge_v * grad_v
    east_w = edge_h[1:-1, 1:]
    west_w = edge_h[1:-1, :-1]
    south_w = edge_v[1:, 1:-1]
    north_w = edge_v[:-1, 1:-1]
    diag_w = east_w + west_w + south_w + north_w + MU * 4.0**0
    ops_w = (east_w, west_w, south_w, north_w, diag_w)
    rhs_wide = -(flux_h[1:-1, 1:] - flux_h[1:-1, :-1] + flux_v[1:, 1:-1] - flux_v[:-1, 1:-1])

    def crop(values, ring):
        cut = (values.shape[-2] - shard_height_total) // 2 - ring
        if cut == 0:
            return values
        return values[..., cut:-cut, cut:-cut]

    def ops_at(ring):
        return tuple(crop(x, ring) for x in ops_w)

    levels, coarse_edges = build_levels(*ops_at(0)[:4], first_level=0, last_level=GATHER_LEVEL)
    block_h, block_w = coarse_edges[0].shape
    whole = {}

    def coarse_solve(rhs_vec, ring, sums):
        if not whole:
            got, summed = gather_strip(jnp.stack([coarse_edges[0], coarse_edges[2], rhs_vec]), sums)
            east_s, south_s = got[0], got[1]
            whole["levels"] = build_levels(east_s, shifted(east_s, 1), south_s, shifted(south_s, 0),
                                           GATHER_LEVEL, LEVELS)[0]
            strip_rhs = got[2]
        else:
            got, summed = gather_strip(rhs_vec[None], sums)
            strip_rhs = got[0]
        strip_x = vcycle(strip_rhs, GATHER_LEVEL, whole["levels"], apply_padded, None)
        coarse_ring = ring // 2
        strip_x = jnp.pad(strip_x, ((coarse_ring, coarse_ring), (0, 0)))
        return lax.dynamic_slice(strip_x, (segment_ordinal * block_h, block_w - coarse_ring),
                                 (block_h + 2 * coarse_ring, block_w + 2 * coarse_ring)), summed

    def precondition(rhs_wide, sums=None):
        ring = (rhs_wide.shape[0] - shard_height_total) // 2
        diag_here = ops_at(ring)[4]
        estimate = OMEGA * rhs_wide / diag_here
        remain = crop(rhs_wide, 0) - apply_inner(crop(estimate, 1), levels[0])
        patch, summed = coarse_solve(restrict_sum(remain), ring, sums)
        estimate = estimate + prolong_copy(patch)
        inner = ops_at(ring - 1)
        smoothed = crop(estimate, ring - 1) + OMEGA * (crop(rhs_wide, ring - 1) - apply_inner(estimate, inner)) / inner[4]
        return smoothed, apply_inner(smoothed, ops_at(ring - 2)), summed

    def ring_of(values):
        return (values.shape[-2] - shard_height_total) // 2

    def own_sums(*pairs):
        return jnp.stack([jnp.sum(crop(a, 0) * crop(b, 0)) for a, b in pairs])

    residual_wide = rhs_wide
    precond, image_u, _ = precondition(residual_wide)
    sums = own_sums((residual_wide, precond), (image_u, precond))
    if ITERS > 1:
        pre_image, image_pre, sums = precondition(image_u, sums)
    else:
        sums = total(sums)
    norm_now = sums[0]
    curvature = sums[1]
    step_length = norm_now / curvature
    direction, image_vec = precond, image_u
    if ITERS > 1:
        pre_dir, image_pre_dir = pre_image, image_pre
    solution = step_length * crop(direction, 0)
    for step_index in range(1, ITERS):
        residual_wide = crop(residual_wide, ring_of(image_vec)) - step_length * image_vec
        precond = crop(precond, ring_of(pre_dir)) - step_length * pre_dir
        image_u = crop(image_u, ring_of(image_pre_dir)) - step_length * image_pre_dir
        sums = own_sums((residual_wide, precond), (image_u, precond), (precond, image_vec))
        if step_index + 1 < ITERS:
            pre_image, image_pre, sums = precondition(image_u, sums)
        else:
            sums = total(sums)
        norm_next = sums[0]
        ratio = norm_next / norm_now
        curvature = sums[1] + 2.0 * ratio * sums[2] + ratio * ratio * curvature
        step_length = norm_next / curvature
        direction = precond + ratio * crop(direction, ring_of(precond))
        image_vec = image_u + ratio * crop(image_vec, ring_of(image_u))
        if step_index + 1 < ITERS:
            pre_dir = pre_image + ratio * crop(pre_dir, ring_of(pre_image))
            image_pre_dir = image_pre + ratio * crop(image_pre_dir, ring_of(image_pre))
        solution = solution + step_length * crop(direction, 0)
        norm_now = norm_next
    return (solution, weight)


def solution(mesh):
    return jax.shard_map(
        local,
        mesh=mesh,
        in_specs=(P(None, ("az", "rg"), None), P(None, ("az", "rg"), None), P(), P()),
        out_specs=(P("az", "rg"), P("az", "rg")),
        check_vma=False,
    )
```

```python
import jax
import jax.numpy as jnp
from jax import lax
from jax.sharding import PartitionSpec as P
from jax.experimental import pallas as pl
from jax.experimental.pallas import tpu as pltpu

LOOK = 5
LEVELS = 6
ITERS = 3
SWEEPS = 4
SEGMENT_HEIGHT = 160
GATHER_LEVEL = 1


OMEGA = 0.6
MU = 0.01


def neighbours(v):
    n_az = lax.axis_size("az")
    n_rg = lax.axis_size("rg")
    above = lax.ppermute(v[..., -1:, :], "az", [(i, i + 1) for i in range(n_az - 1)])
    below = lax.ppermute(v[..., :1, :], "az", [(i + 1, i) for i in range(n_az - 1)])
    left = lax.ppermute(v[..., :, -1:], "rg", [(i, i + 1) for i in range(n_rg - 1)])
    right = lax.ppermute(v[..., :, :1], "rg", [(i + 1, i) for i in range(n_rg - 1)])
    north = jnp.concatenate([above, v[..., :-1, :]], axis=-2)
    south = jnp.concatenate([v[..., 1:, :], below], axis=-2)
    west = jnp.concatenate([left, v[..., :, :-1]], axis=-1)
    east = jnp.concatenate([v[..., :, 1:], right], axis=-1)
    return north, south, west, east


def apply_halo(vector, operators):
    east, west, south, north, diagonal = operators
    v_n, v_s, v_w, v_e = neighbours(vector)
    return diagonal * vector - east * v_e - west * v_w - south * v_s - north * v_n


def extended(v, width):
    n_az = lax.axis_size("az")
    n_rg = lax.axis_size("rg")
    above = lax.ppermute(v[..., -width:, :], "az", [(i, i + 1) for i in range(n_az - 1)])
    below = lax.ppermute(v[..., :width, :], "az", [(i + 1, i) for i in range(n_az - 1)])
    v = jnp.concatenate([above, v, below], axis=-2)
    left = lax.ppermute(v[..., :, -width:], "rg", [(i, i + 1) for i in range(n_rg - 1)])
    right = lax.ppermute(v[..., :, :width], "rg", [(i + 1, i) for i in range(n_rg - 1)])
    return jnp.concatenate([left, v, right], axis=-1)


def apply_inner(padded, operators):
    east, west, south, north, diagonal = operators
    return (diagonal * padded[1:-1, 1:-1] - east * padded[1:-1, 2:] - west * padded[1:-1, :-2]
            - south * padded[2:, 1:-1] - north * padded[:-2, 1:-1])


def apply_padded(vector, operators):
    east, west, south, north, diagonal = operators
    padded = jnp.pad(vector, 1)
    return (diagonal * vector - east * padded[1:-1, 2:] - west * padded[1:-1, :-2]
            - south * padded[2:, 1:-1] - north * padded[:-2, 1:-1])


def multilook_kernel(bounds_ref, lead_ref, trail_ref, out_ref):
    shape = lead_ref.shape[1:]
    line = lax.broadcasted_iota(jnp.int32, shape, 0)
    column = pl.program_id(0) * shape[1] + lax.broadcasted_iota(jnp.int32, shape, 1)
    mask = ((line >= bounds_ref[0]) & (line < bounds_ref[1]) & (column >= bounds_ref[2])
            & (column < bounds_ref[3])).astype(jnp.float32)
    first_re = lead_ref[0].astype(jnp.float32) * mask
    first_im = lead_ref[1].astype(jnp.float32) * mask
    second_re = trail_ref[0].astype(jnp.float32) * mask
    second_im = trail_ref[1].astype(jnp.float32) * mask
    products = (
        first_re * second_re + first_im * second_im,
        first_im * second_re - first_re * second_im,
        first_re * first_re + first_im * first_im,
        second_re * second_re + second_im * second_im,
    )
    chunks, span = out_ref.shape[2:]
    for part, values in enumerate(products):
        for group in range(out_ref.shape[1]):
            acc = values[group * LOOK:group * LOOK + 1, :]
            for offset in range(1, LOOK):
                acc = acc + values[group * LOOK + offset:group * LOOK + offset + 1, :]
            for chunk in range(chunks):
                out_ref[part, group, chunk:chunk + 1, :] = acc[:, chunk * span:(chunk + 1) * span]


def mean_multilook(leading, trailing, bounds):
    _, height_rows, width_cols = leading.shape
    block = 5120
    span = LOOK * 128
    rows = pl.pallas_call(
        multilook_kernel,
        grid=(width_cols // block,),
        in_specs=[
            pl.BlockSpec(memory_space=pltpu.SMEM),
            pl.BlockSpec((2, height_rows, block), lambda j: (0, 0, j)),
            pl.BlockSpec((2, height_rows, block), lambda j: (0, 0, j)),
        ],
        out_specs=pl.BlockSpec((4, height_rows // LOOK, block // span, span), lambda j: (0, 0, j, 0)),
        out_shape=jax.ShapeDtypeStruct((4, height_rows // LOOK, width_cols // span, span), jnp.float32),
    )(bounds, leading, trailing)
    grouped = rows
    cols = jnp.einsum("pikc,cd->pikd", grouped, group_sum(span, LOOK).T, precision=HIGHEST)
    return cols.reshape(4, height_rows // LOOK, width_cols // LOOK)


def edge_terms(left_re, left_im, left_weight, right_re, right_im, right_weight):
    edge_weight = 0.5 * (left_weight + right_weight)
    cross_im = right_im * left_re - right_re * left_im
    power_sum = (
        left_re * left_re + left_im * left_im + right_re * right_re + right_im * right_im + 1.0
    )
    return (edge_weight, 2.0 * cross_im / power_sum)


HIGHEST = lax.Precision.HIGHEST


def group_sum(n, size):
    group = lax.broadcasted_iota(jnp.int32, (n // size, n), 0)
    cell = lax.broadcasted_iota(jnp.int32, (n // size, n), 1)
    return (cell // size == group).astype(jnp.float32)


def pick(n, offset):
    group = lax.broadcasted_iota(jnp.int32, (n // 2, n), 0)
    cell = lax.broadcasted_iota(jnp.int32, (n // 2, n), 1)
    return (cell == 2 * group + offset).astype(jnp.float32)


def sandwich(left, vector, right):
    inner = jnp.dot(left, vector, precision=HIGHEST)
    return jnp.dot(inner, right, precision=HIGHEST)


def restrict_sum(vector):
    rows_now, cols_now = vector.shape
    return sandwich(group_sum(rows_now, 2), vector, group_sum(cols_now, 2).T)


def prolong_copy(vector):
    rows_now, cols_now = vector.shape
    return sandwich(group_sum(2 * rows_now, 2).T, vector, group_sum(2 * cols_now, 2))


def coarsen(east, west, south, north):
    rows_now, cols_now = east.shape
    row_sum = group_sum(rows_now, 2)
    col_sum = group_sum(cols_now, 2).T
    return (
        sandwich(row_sum, east, pick(cols_now, 1).T),
        sandwich(row_sum, west, pick(cols_now, 0).T),
        sandwich(pick(rows_now, 1), south, col_sum),
        sandwich(pick(rows_now, 0), north, col_sum),
    )


def build_levels(east, west, south, north, first_level, last_level):
    levels = {}
    for level in range(first_level, last_level):
        diagonal = east + west + south + north + MU * 4.0**level
        levels[level] = (east, west, south, north, diagonal)
        if level + 1 < LEVELS:
            east, west, south, north = coarsen(east, west, south, north)
    return levels, (east, west, south, north)


def jacobi_sweeps(rhs_vec, operators, apply_fn):
    estimate = OMEGA * rhs_vec / operators[4]
    for sweep_index in range(SWEEPS - 1):
        estimate = estimate + OMEGA * (rhs_vec - apply_fn(estimate, operators)) / operators[4]
    return estimate


def vcycle(rhs_vec, level, levels, apply_fn, stop_fn):
    if level == LEVELS - 1:
        return jacobi_sweeps(rhs_vec, levels[level], apply_fn)
    if stop_fn is not None and level == GATHER_LEVEL:
        return stop_fn(rhs_vec)
    diagonal = levels[level][4]
    estimate = OMEGA * rhs_vec / diagonal
    remain = rhs_vec - apply_fn(estimate, levels[level])
    correction = vcycle(restrict_sum(remain), level + 1, levels, apply_fn, stop_fn)
    estimate = estimate + prolong_copy(correction)
    return estimate + OMEGA * (rhs_vec - apply_fn(estimate, levels[level])) / diagonal


def everyone():
    return lax.axis_size("az") * lax.axis_size("rg")


def gather_strip(blocks, sums=None):
    n_az = lax.axis_size("az")
    n_rg = lax.axis_size("rg")
    count, h, w = blocks.shape
    if sums is not None:
        extra = jnp.zeros((1, h, w), jnp.float32).at[0, 0, :sums.shape[0]].set(sums)
        blocks = jnp.concatenate([blocks, extra])
    sent = jnp.broadcast_to(blocks[None], (n_az,) + blocks.shape)
    got = lax.all_to_all(sent, "az", 0, 0, tiled=True)
    summed = None
    if sums is not None:
        column_sums = jnp.sum(got[:, count, 0, :sums.shape[0]], axis=0)
        rows = lax.all_to_all(jnp.broadcast_to(column_sums[None], (n_rg, sums.shape[0])), "rg", 0, 0, tiled=True)
        summed = jnp.sum(rows, axis=0)
        got = got[:, :count]
    column = got.transpose(1, 0, 2, 3).reshape(count, n_az * h, w)
    left = lax.ppermute(column, "rg", [(i, i + 1) for i in range(n_rg - 1)])
    right = lax.ppermute(column, "rg", [(i + 1, i) for i in range(n_rg - 1)])
    return jnp.concatenate([left, column, right], axis=-1), summed


def shifted(values, axis):
    pad = [(0, 0)] * values.ndim
    pad[axis] = (1, 0)
    return lax.slice_in_dim(jnp.pad(values, pad), 0, values.shape[axis], axis=axis)


def total(values):
    n = everyone()
    sent = jnp.broadcast_to(values[None], (n, values.shape[0]))
    got = lax.all_to_all(sent, ("az", "rg"), 0, 0, tiled=True)
    return jnp.sum(got, axis=0)


def local(master_phasor_raster, slave_phasor_raster, segment_track_trim, segment_slant_trim):
    n_az = lax.axis_size("az")
    n_range = lax.axis_size("rg")
    segment_ordinal = lax.axis_index("az")
    range_index = lax.axis_index("rg")
    track_trim_width = lax.dynamic_index_in_dim(
        segment_track_trim, segment_ordinal, 0, keepdims=False
    )
    slant_trim_width = lax.dynamic_index_in_dim(
        segment_slant_trim, segment_ordinal, 0, keepdims=False
    )
    lines_here = master_phasor_raster.shape[1]
    slant_sample_total = master_phasor_raster.shape[2]
    first_line = range_index * lines_here
    bounds = jnp.stack([
        track_trim_width[0] - first_line,
        SEGMENT_HEIGHT - track_trim_width[1] - first_line,
        slant_trim_width[0],
        slant_sample_total - slant_trim_width[1],
    ]).astype(jnp.int32)
    pixel_totals = mean_multilook(master_phasor_raster, slave_phasor_raster, bounds)
    look_re, look_im, power_one, power_two = (
        pixel_totals[0],
        pixel_totals[1],
        pixel_totals[2],
        pixel_totals[3],
    )
    weight = 0.05 + 4.0 * (look_re * look_re + look_im * look_im) / jnp.maximum(
        power_one * power_two, 1.0
    )
    widest = 2 * ITERS
    border = widest + 1
    fields = jnp.stack([look_re, look_im, weight])
    n_fields, rows_here, cols_all = fields.shape
    cols_here = cols_all // n_range
    main = fields.reshape(n_fields, rows_here, n_range, cols_here).transpose(2, 0, 1, 3)
    zero = jnp.zeros((1, n_fields, rows_here, border), jnp.float32)
    before = jnp.concatenate([zero, main[:-1, :, :, -border:]], axis=0)
    after = jnp.concatenate([main[1:, :, :, :border], zero], axis=0)
    fields = jnp.concatenate([before, main, after], axis=-1)
    fields = lax.all_to_all(fields, "rg", 0, 0, tiled=True)
    fields = fields.transpose(1, 0, 2, 3).reshape(n_fields, n_range * rows_here, cols_here + 2 * border)
    shard_height_total = n_range * rows_here
    above = lax.ppermute(fields[:, -border:, :], "az", [(i, i + 1) for i in range(n_az - 1)])
    below = lax.ppermute(fields[:, :border, :], "az", [(i + 1, i) for i in range(n_az - 1)])
    fields = jnp.concatenate([above, fields, below], axis=1)
    weight = fields[2, border:-border, border:-border]

    row_global = segment_ordinal * shard_height_total - border + jnp.arange(
        shard_height_total + 2 * border, dtype=jnp.int32)
    col_global = range_index * cols_here - border + jnp.arange(cols_here + 2 * border, dtype=jnp.int32)
    edge_h, grad_h = edge_terms(fields[0, :, :-1], fields[1, :, :-1], fields[2, :, :-1],
                                fields[0, :, 1:], fields[1, :, 1:], fields[2, :, 1:])
    keep_h = ((col_global[:-1] >= 0) & (col_global[:-1] <= cols_here * n_range - 2)).astype(jnp.float32)
    edge_h = edge_h * keep_h[None, :]
    edge_v, grad_v = edge_terms(fields[0, :-1], fields[1, :-1], fields[2, :-1],
                                fields[0, 1:], fields[1, 1:], fields[2, 1:])
    keep_v = ((row_global[:-1] >= 0) & (row_global[:-1] <= shard_height_total * n_az - 2)).astype(jnp.float32)
    edge_v = edge_v * keep_v[:, None]
    flux_h = edge_h * grad_h
    flux_v = edge_v * grad_v
    east_w = edge_h[1:-1, 1:]
    west_w = edge_h[1:-1, :-1]
    south_w = edge_v[1:, 1:-1]
    north_w = edge_v[:-1, 1:-1]
    diag_w = east_w + west_w + south_w + north_w + MU * 4.0**0
    ops_w = (east_w, west_w, south_w, north_w, diag_w)
    rhs_wide = -(flux_h[1:-1, 1:] - flux_h[1:-1, :-1] + flux_v[1:, 1:-1] - flux_v[:-1, 1:-1])

    def crop(values, ring):
        cut = (values.shape[-2] - shard_height_total) // 2 - ring
        if cut == 0:
            return values
        return values[..., cut:-cut, cut:-cut]

    def ops_at(ring):
        return tuple(crop(x, ring) for x in ops_w)

    levels, coarse_edges = build_levels(*ops_at(0)[:4], first_level=0, last_level=GATHER_LEVEL)
    block_h, block_w = coarse_edges[0].shape
    whole = {}

    def coarse_solve(rhs_vec, ring, sums):
        if not whole:
            got, summed = gather_strip(jnp.stack([coarse_edges[0], coarse_edges[2], rhs_vec]), sums)
            east_s, south_s = got[0], got[1]
            whole["levels"] = build_levels(east_s, shifted(east_s, 1), south_s, shifted(south_s, 0),
                                           GATHER_LEVEL, LEVELS)[0]
            strip_rhs = got[2]
        else:
            got, summed = gather_strip(rhs_vec[None], sums)
            strip_rhs = got[0]
        strip_x = vcycle(strip_rhs, GATHER_LEVEL, whole["levels"], apply_padded, None)
        coarse_ring = ring // 2
        strip_x = jnp.pad(strip_x, ((coarse_ring, coarse_ring), (0, 0)))
        return lax.dynamic_slice(strip_x, (segment_ordinal * block_h, block_w - coarse_ring),
                                 (block_h + 2 * coarse_ring, block_w + 2 * coarse_ring)), summed

    def precondition(rhs_wide, sums=None):
        ring = (rhs_wide.shape[0] - shard_height_total) // 2
        diag_here = ops_at(ring)[4]
        estimate = OMEGA * rhs_wide / diag_here
        remain = crop(rhs_wide, 0) - apply_inner(crop(estimate, 1), levels[0])
        patch, summed = coarse_solve(restrict_sum(remain), ring, sums)
        estimate = estimate + prolong_copy(patch)
        inner = ops_at(ring - 1)
        smoothed = crop(estimate, ring - 1) + OMEGA * (crop(rhs_wide, ring - 1) - apply_inner(estimate, inner)) / inner[4]
        return smoothed, apply_inner(smoothed, ops_at(ring - 2)), summed

    def ring_of(values):
        return (values.shape[-2] - shard_height_total) // 2

    def own_sums(*pairs):
        return jnp.stack([jnp.sum(crop(a, 0) * crop(b, 0)) for a, b in pairs])

    residual_wide = rhs_wide
    precond, image_u, _ = precondition(residual_wide)
    sums = own_sums((residual_wide, precond), (image_u, precond))
    if ITERS > 1:
        pre_image, image_pre, sums = precondition(image_u, sums)
    else:
        sums = total(sums)
    norm_now = sums[0]
    curvature = sums[1]
    step_length = norm_now / curvature
    direction, image_vec = precond, image_u
    if ITERS > 1:
        pre_dir, image_pre_dir = pre_image, image_pre
    solution = step_length * crop(direction, 0)
    for step_index in range(1, ITERS):
        residual_wide = crop(residual_wide, ring_of(image_vec)) - step_length * image_vec
        precond = crop(precond, ring_of(pre_dir)) - step_length * pre_dir
        image_u = crop(image_u, ring_of(image_pre_dir)) - step_length * image_pre_dir
        sums = own_sums((residual_wide, precond), (image_u, precond), (precond, image_vec))
        if step_index + 1 < ITERS:
            pre_image, image_pre, sums = precondition(image_u, sums)
        else:
            sums = total(sums)
        norm_next = sums[0]
        ratio = norm_next / norm_now
        curvature = sums[1] + 2.0 * ratio * sums[2] + ratio * ratio * curvature
        step_length = norm_next / curvature
        direction = precond + ratio * crop(direction, ring_of(precond))
        image_vec = image_u + ratio * crop(image_vec, ring_of(image_u))
        if step_index + 1 < ITERS:
            pre_dir = pre_image + ratio * crop(pre_dir, ring_of(pre_image))
            image_pre_dir = image_pre + ratio * crop(image_pre_dir, ring_of(image_pre))
        solution = solution + step_length * crop(direction, 0)
        norm_now = norm_next
    return (solution, weight)


def solution(mesh):
    return jax.shard_map(
        local,
        mesh=mesh,
        in_specs=(P(None, ("az", "rg"), None), P(None, ("az", "rg"), None), P(), P()),
        out_specs=(P("az", "rg"), P("az", "rg")),
        check_vma=False,
    )
```

```python
import jax
import jax.numpy as jnp
from jax import lax
from jax.sharding import PartitionSpec as P
from jax.experimental import pallas as pl
from jax.experimental.pallas import tpu as pltpu

LOOK = 5
LEVELS = 6
ITERS = 3
SWEEPS = 4
SEGMENT_HEIGHT = 160
GATHER_LEVEL = 1


OMEGA = 0.6
MU = 0.01


def neighbours(v):
    n_az = lax.axis_size("az")
    n_rg = lax.axis_size("rg")
    above = lax.ppermute(v[..., -1:, :], "az", [(i, i + 1) for i in range(n_az - 1)])
    below = lax.ppermute(v[..., :1, :], "az", [(i + 1, i) for i in range(n_az - 1)])
    left = lax.ppermute(v[..., :, -1:], "rg", [(i, i + 1) for i in range(n_rg - 1)])
    right = lax.ppermute(v[..., :, :1], "rg", [(i + 1, i) for i in range(n_rg - 1)])
    north = jnp.concatenate([above, v[..., :-1, :]], axis=-2)
    south = jnp.concatenate([v[..., 1:, :], below], axis=-2)
    west = jnp.concatenate([left, v[..., :, :-1]], axis=-1)
    east = jnp.concatenate([v[..., :, 1:], right], axis=-1)
    return north, south, west, east


def apply_halo(vector, operators):
    east, west, south, north, diagonal = operators
    v_n, v_s, v_w, v_e = neighbours(vector)
    return diagonal * vector - east * v_e - west * v_w - south * v_s - north * v_n


def extended(v, width):
    n_az = lax.axis_size("az")
    n_rg = lax.axis_size("rg")
    above = lax.ppermute(v[..., -width:, :], "az", [(i, i + 1) for i in range(n_az - 1)])
    below = lax.ppermute(v[..., :width, :], "az", [(i + 1, i) for i in range(n_az - 1)])
    v = jnp.concatenate([above, v, below], axis=-2)
    left = lax.ppermute(v[..., :, -width:], "rg", [(i, i + 1) for i in range(n_rg - 1)])
    right = lax.ppermute(v[..., :, :width], "rg", [(i + 1, i) for i in range(n_rg - 1)])
    return jnp.concatenate([left, v, right], axis=-1)


def apply_inner(padded, operators):
    east, west, south, north, diagonal = operators
    return (diagonal * padded[1:-1, 1:-1] - east * padded[1:-1, 2:] - west * padded[1:-1, :-2]
            - south * padded[2:, 1:-1] - north * padded[:-2, 1:-1])


def apply_padded(vector, operators):
    east, west, south, north, diagonal = operators
    padded = jnp.pad(vector, 1)
    return (diagonal * vector - east * padded[1:-1, 2:] - west * padded[1:-1, :-2]
            - south * padded[2:, 1:-1] - north * padded[:-2, 1:-1])


def multilook_kernel(bounds_ref, lead_ref, trail_ref, out_ref):
    shape = lead_ref.shape[1:]
    line = lax.broadcasted_iota(jnp.int32, shape, 0)
    column = pl.program_id(0) * shape[1] + lax.broadcasted_iota(jnp.int32, shape, 1)
    mask = ((line >= bounds_ref[0]) & (line < bounds_ref[1]) & (column >= bounds_ref[2])
            & (column < bounds_ref[3])).astype(jnp.float32)
    first_re = lead_ref[0].astype(jnp.float32) * mask
    first_im = lead_ref[1].astype(jnp.float32) * mask
    second_re = trail_ref[0].astype(jnp.float32) * mask
    second_im = trail_ref[1].astype(jnp.float32) * mask
    products = (
        first_re * second_re + first_im * second_im,
        first_im * second_re - first_re * second_im,
        first_re * first_re + first_im * first_im,
        second_re * second_re + second_im * second_im,
    )
    chunks, span = out_ref.shape[2:]
    for part, values in enumerate(products):
        for group in range(out_ref.shape[1]):
            acc = values[group * LOOK:group * LOOK + 1, :]
            for offset in range(1, LOOK):
                acc = acc + values[group * LOOK + offset:group * LOOK + offset + 1, :]
            for chunk in range(chunks):
                out_ref[part, group, chunk:chunk + 1, :] = acc[:, chunk * span:(chunk + 1) * span]


def mean_multilook(leading, trailing, bounds):
    _, height_rows, width_cols = leading.shape
    block = 5120
    span = LOOK * 128
    rows = pl.pallas_call(
        multilook_kernel,
        grid=(width_cols // block,),
        in_specs=[
            pl.BlockSpec(memory_space=pltpu.SMEM),
            pl.BlockSpec((2, height_rows, block), lambda j: (0, 0, j)),
            pl.BlockSpec((2, height_rows, block), lambda j: (0, 0, j)),
        ],
        out_specs=pl.BlockSpec((4, height_rows // LOOK, block // span, span), lambda j: (0, 0, j, 0)),
        out_shape=jax.ShapeDtypeStruct((4, height_rows // LOOK, width_cols // span, span), jnp.float32),
    )(bounds, leading, trailing)
    grouped = rows
    cols = jnp.einsum("pikc,cd->pikd", grouped, group_sum(span, LOOK).T, precision=HIGHEST)
    return cols.reshape(4, height_rows // LOOK, width_cols // LOOK)


def edge_terms(left_re, left_im, left_weight, right_re, right_im, right_weight):
    edge_weight = 0.5 * (left_weight + right_weight)
    cross_im = right_im * left_re - right_re * left_im
    power_sum = (
        left_re * left_re + left_im * left_im + right_re * right_re + right_im * right_im + 1.0
    )
    return (edge_weight, 2.0 * cross_im / power_sum)


HIGHEST = lax.Precision.HIGHEST


def group_sum(n, size):
    group = lax.broadcasted_iota(jnp.int32, (n // size, n), 0)
    cell = lax.broadcasted_iota(jnp.int32, (n // size, n), 1)
    return (cell // size == group).astype(jnp.float32)


def pick(n, offset):
    group = lax.broadcasted_iota(jnp.int32, (n // 2, n), 0)
    cell = lax.broadcasted_iota(jnp.int32, (n // 2, n), 1)
    return (cell == 2 * group + offset).astype(jnp.float32)


def sandwich(left, vector, right):
    inner = jnp.dot(left, vector, precision=HIGHEST)
    return jnp.dot(inner, right, precision=HIGHEST)


def restrict_sum(vector):
    rows_now, cols_now = vector.shape
    return sandwich(group_sum(rows_now, 2), vector, group_sum(cols_now, 2).T)


def prolong_copy(vector):
    rows_now, cols_now = vector.shape
    return sandwich(group_sum(2 * rows_now, 2).T, vector, group_sum(2 * cols_now, 2))


def coarsen(east, west, south, north):
    rows_now, cols_now = east.shape
    row_sum = group_sum(rows_now, 2)
    col_sum = group_sum(cols_now, 2).T
    return (
        sandwich(row_sum, east, pick(cols_now, 1).T),
        sandwich(row_sum, west, pick(cols_now, 0).T),
        sandwich(pick(rows_now, 1), south, col_sum),
        sandwich(pick(rows_now, 0), north, col_sum),
    )


def build_levels(east, west, south, north, first_level, last_level):
    levels = {}
    for level in range(first_level, last_level):
        diagonal = east + west + south + north + MU * 4.0**level
        levels[level] = (east, west, south, north, diagonal)
        if level + 1 < LEVELS:
            east, west, south, north = coarsen(east, west, south, north)
    return levels, (east, west, south, north)


def jacobi_sweeps(rhs_vec, operators, apply_fn):
    estimate = OMEGA * rhs_vec / operators[4]
    for sweep_index in range(SWEEPS - 1):
        estimate = estimate + OMEGA * (rhs_vec - apply_fn(estimate, operators)) / operators[4]
    return estimate


def vcycle(rhs_vec, level, levels, apply_fn, stop_fn):
    if level == LEVELS - 1:
        return jacobi_sweeps(rhs_vec, levels[level], apply_fn)
    if stop_fn is not None and level == GATHER_LEVEL:
        return stop_fn(rhs_vec)
    diagonal = levels[level][4]
    estimate = OMEGA * rhs_vec / diagonal
    remain = rhs_vec - apply_fn(estimate, levels[level])
    correction = vcycle(restrict_sum(remain), level + 1, levels, apply_fn, stop_fn)
    estimate = estimate + prolong_copy(correction)
    return estimate + OMEGA * (rhs_vec - apply_fn(estimate, levels[level])) / diagonal


def everyone():
    return lax.axis_size("az") * lax.axis_size("rg")


def gather_strip(blocks, sums=None):
    n_az = lax.axis_size("az")
    n_rg = lax.axis_size("rg")
    count, h, w = blocks.shape
    if sums is not None:
        extra = jnp.zeros((1, h, w), jnp.float32).at[0, 0, :sums.shape[0]].set(sums)
        blocks = jnp.concatenate([blocks, extra])
    sent = jnp.broadcast_to(blocks[None], (n_az,) + blocks.shape)
    got = lax.all_to_all(sent, "az", 0, 0, tiled=True)
    summed = None
    if sums is not None:
        column_sums = jnp.sum(got[:, count, 0, :sums.shape[0]], axis=0)
        got = got[:, :count]
    column = got.transpose(1, 0, 2, 3).reshape(count, n_az * h, w)
    left = lax.ppermute(column, "rg", [(i, i + 1) for i in range(n_rg - 1)])
    right = lax.ppermute(column, "rg", [(i + 1, i) for i in range(n_rg - 1)])
    if sums is not None:
        column_sums, left, right = lax.optimization_barrier((column_sums, left, right))
        rows = lax.all_to_all(jnp.broadcast_to(column_sums[None], (n_rg, sums.shape[0])), "rg", 0, 0, tiled=True)
        summed = jnp.sum(rows, axis=0)
    return jnp.concatenate([left, column, right], axis=-1), summed


def shifted(values, axis):
    pad = [(0, 0)] * values.ndim
    pad[axis] = (1, 0)
    return lax.slice_in_dim(jnp.pad(values, pad), 0, values.shape[axis], axis=axis)


def total(values):
    n = everyone()
    sent = jnp.broadcast_to(values[None], (n, values.shape[0]))
    got = lax.all_to_all(sent, ("az", "rg"), 0, 0, tiled=True)
    return jnp.sum(got, axis=0)


def local(master_phasor_raster, slave_phasor_raster, segment_track_trim, segment_slant_trim):
    n_az = lax.axis_size("az")
    n_range = lax.axis_size("rg")
    segment_ordinal = lax.axis_index("az")
    range_index = lax.axis_index("rg")
    track_trim_width = lax.dynamic_index_in_dim(
        segment_track_trim, segment_ordinal, 0, keepdims=False
    )
    slant_trim_width = lax.dynamic_index_in_dim(
        segment_slant_trim, segment_ordinal, 0, keepdims=False
    )
    lines_here = master_phasor_raster.shape[1]
    slant_sample_total = master_phasor_raster.shape[2]
    first_line = range_index * lines_here
    bounds = jnp.stack([
        track_trim_width[0] - first_line,
        SEGMENT_HEIGHT - track_trim_width[1] - first_line,
        slant_trim_width[0],
        slant_sample_total - slant_trim_width[1],
    ]).astype(jnp.int32)
    pixel_totals = mean_multilook(master_phasor_raster, slave_phasor_raster, bounds)
    look_re, look_im, power_one, power_two = (
        pixel_totals[0],
        pixel_totals[1],
        pixel_totals[2],
        pixel_totals[3],
    )
    weight = 0.05 + 4.0 * (look_re * look_re + look_im * look_im) / jnp.maximum(
        power_one * power_two, 1.0
    )
    widest = 2 * ITERS
    border = widest + 1
    fields = jnp.stack([look_re, look_im, weight])
    n_fields, rows_here, cols_all = fields.shape
    cols_here = cols_all // n_range
    main = fields.reshape(n_fields, rows_here, n_range, cols_here).transpose(2, 0, 1, 3)
    zero = jnp.zeros((1, n_fields, rows_here, border), jnp.float32)
    before = jnp.concatenate([zero, main[:-1, :, :, -border:]], axis=0)
    after = jnp.concatenate([main[1:, :, :, :border], zero], axis=0)
    fields = jnp.concatenate([before, main, after], axis=-1)
    fields = lax.all_to_all(fields, "rg", 0, 0, tiled=True)
    fields = fields.transpose(1, 0, 2, 3).reshape(n_fields, n_range * rows_here, cols_here + 2 * border)
    shard_height_total = n_range * rows_here
    above = lax.ppermute(fields[:, -border:, :], "az", [(i, i + 1) for i in range(n_az - 1)])
    below = lax.ppermute(fields[:, :border, :], "az", [(i + 1, i) for i in range(n_az - 1)])
    fields = jnp.concatenate([above, fields, below], axis=1)
    weight = fields[2, border:-border, border:-border]

    row_global = segment_ordinal * shard_height_total - border + jnp.arange(
        shard_height_total + 2 * border, dtype=jnp.int32)
    col_global = range_index * cols_here - border + jnp.arange(cols_here + 2 * border, dtype=jnp.int32)
    edge_h, grad_h = edge_terms(fields[0, :, :-1], fields[1, :, :-1], fields[2, :, :-1],
                                fields[0, :, 1:], fields[1, :, 1:], fields[2, :, 1:])
    keep_h = ((col_global[:-1] >= 0) & (col_global[:-1] <= cols_here * n_range - 2)).astype(jnp.float32)
    edge_h = edge_h * keep_h[None, :]
    edge_v, grad_v = edge_terms(fields[0, :-1], fields[1, :-1], fields[2, :-1],
                                fields[0, 1:], fields[1, 1:], fields[2, 1:])
    keep_v = ((row_global[:-1] >= 0) & (row_global[:-1] <= shard_height_total * n_az - 2)).astype(jnp.float32)
    edge_v = edge_v * keep_v[:, None]
    flux_h = edge_h * grad_h
    flux_v = edge_v * grad_v
    east_w = edge_h[1:-1, 1:]
    west_w = edge_h[1:-1, :-1]
    south_w = edge_v[1:, 1:-1]
    north_w = edge_v[:-1, 1:-1]
    diag_w = east_w + west_w + south_w + north_w + MU * 4.0**0
    ops_w = (east_w, west_w, south_w, north_w, diag_w)
    rhs_wide = -(flux_h[1:-1, 1:] - flux_h[1:-1, :-1] + flux_v[1:, 1:-1] - flux_v[:-1, 1:-1])

    def crop(values, ring):
        cut = (values.shape[-2] - shard_height_total) // 2 - ring
        if cut == 0:
            return values
        return values[..., cut:-cut, cut:-cut]

    def ops_at(ring):
        return tuple(crop(x, ring) for x in ops_w)

    levels, coarse_edges = build_levels(*ops_at(0)[:4], first_level=0, last_level=GATHER_LEVEL)
    block_h, block_w = coarse_edges[0].shape
    whole = {}

    def coarse_solve(rhs_vec, ring, sums):
        if not whole:
            got, summed = gather_strip(jnp.stack([coarse_edges[0], coarse_edges[2], rhs_vec]), sums)
            east_s, south_s = got[0], got[1]
            whole["levels"] = build_levels(east_s, shifted(east_s, 1), south_s, shifted(south_s, 0),
                                           GATHER_LEVEL, LEVELS)[0]
            strip_rhs = got[2]
        else:
            got, summed = gather_strip(rhs_vec[None], sums)
            strip_rhs = got[0]
        strip_x = vcycle(strip_rhs, GATHER_LEVEL, whole["levels"], apply_padded, None)
        coarse_ring = ring // 2
        strip_x = jnp.pad(strip_x, ((coarse_ring, coarse_ring), (0, 0)))
        return lax.dynamic_slice(strip_x, (segment_ordinal * block_h, block_w - coarse_ring),
                                 (block_h + 2 * coarse_ring, block_w + 2 * coarse_ring)), summed

    def precondition(rhs_wide, sums=None):
        ring = (rhs_wide.shape[0] - shard_height_total) // 2
        diag_here = ops_at(ring)[4]
        estimate = OMEGA * rhs_wide / diag_here
        remain = crop(rhs_wide, 0) - apply_inner(crop(estimate, 1), levels[0])
        patch, summed = coarse_solve(restrict_sum(remain), ring, sums)
        estimate = estimate + prolong_copy(patch)
        inner = ops_at(ring - 1)
        smoothed = crop(estimate, ring - 1) + OMEGA * (crop(rhs_wide, ring - 1) - apply_inner(estimate, inner)) / inner[4]
        return smoothed, apply_inner(smoothed, ops_at(ring - 2)), summed

    def ring_of(values):
        return (values.shape[-2] - shard_height_total) // 2

    def own_sums(*pairs):
        return jnp.stack([jnp.sum(crop(a, 0) * crop(b, 0)) for a, b in pairs])

    residual_wide = rhs_wide
    precond, image_u, _ = precondition(residual_wide)
    sums = own_sums((residual_wide, precond), (image_u, precond))
    if ITERS > 1:
        pre_image, image_pre, sums = precondition(image_u, sums)
    else:
        sums = total(sums)
    norm_now = sums[0]
    curvature = sums[1]
    step_length = norm_now / curvature
    direction, image_vec = precond, image_u
    if ITERS > 1:
        pre_dir, image_pre_dir = pre_image, image_pre
    solution = step_length * crop(direction, 0)
    for step_index in range(1, ITERS):
        residual_wide = crop(residual_wide, ring_of(image_vec)) - step_length * image_vec
        precond = crop(precond, ring_of(pre_dir)) - step_length * pre_dir
        image_u = crop(image_u, ring_of(image_pre_dir)) - step_length * image_pre_dir
        sums = own_sums((residual_wide, precond), (image_u, precond), (precond, image_vec))
        if step_index + 1 < ITERS:
            pre_image, image_pre, sums = precondition(image_u, sums)
        else:
            sums = total(sums)
        norm_next = sums[0]
        ratio = norm_next / norm_now
        curvature = sums[1] + 2.0 * ratio * sums[2] + ratio * ratio * curvature
        step_length = norm_next / curvature
        direction = precond + ratio * crop(direction, ring_of(precond))
        image_vec = image_u + ratio * crop(image_vec, ring_of(image_u))
        if step_index + 1 < ITERS:
            pre_dir = pre_image + ratio * crop(pre_dir, ring_of(pre_image))
            image_pre_dir = image_pre + ratio * crop(image_pre_dir, ring_of(image_pre))
        solution = solution + step_length * crop(direction, 0)
        norm_now = norm_next
    return (solution, weight)


def solution(mesh):
    return jax.shard_map(
        local,
        mesh=mesh,
        in_specs=(P(None, ("az", "rg"), None), P(None, ("az", "rg"), None), P(), P()),
        out_specs=(P("az", "rg"), P("az", "rg")),
        check_vma=False,
    )
```

```python
import jax
import jax.numpy as jnp
from jax import lax
from jax.sharding import PartitionSpec as P
from jax.experimental import pallas as pl
from jax.experimental.pallas import tpu as pltpu

LOOK = 5
LEVELS = 6
ITERS = 3
SWEEPS = 4
SEGMENT_HEIGHT = 160
GATHER_LEVEL = 1


OMEGA = 0.6
MU = 0.01


def neighbours(v):
    n_az = lax.axis_size("az")
    n_rg = lax.axis_size("rg")
    above = lax.ppermute(v[..., -1:, :], "az", [(i, i + 1) for i in range(n_az - 1)])
    below = lax.ppermute(v[..., :1, :], "az", [(i + 1, i) for i in range(n_az - 1)])
    left = lax.ppermute(v[..., :, -1:], "rg", [(i, i + 1) for i in range(n_rg - 1)])
    right = lax.ppermute(v[..., :, :1], "rg", [(i + 1, i) for i in range(n_rg - 1)])
    north = jnp.concatenate([above, v[..., :-1, :]], axis=-2)
    south = jnp.concatenate([v[..., 1:, :], below], axis=-2)
    west = jnp.concatenate([left, v[..., :, :-1]], axis=-1)
    east = jnp.concatenate([v[..., :, 1:], right], axis=-1)
    return north, south, west, east


def apply_halo(vector, operators):
    east, west, south, north, diagonal = operators
    v_n, v_s, v_w, v_e = neighbours(vector)
    return diagonal * vector - east * v_e - west * v_w - south * v_s - north * v_n


def extended(v, width):
    n_az = lax.axis_size("az")
    n_rg = lax.axis_size("rg")
    above = lax.ppermute(v[..., -width:, :], "az", [(i, i + 1) for i in range(n_az - 1)])
    below = lax.ppermute(v[..., :width, :], "az", [(i + 1, i) for i in range(n_az - 1)])
    v = jnp.concatenate([above, v, below], axis=-2)
    left = lax.ppermute(v[..., :, -width:], "rg", [(i, i + 1) for i in range(n_rg - 1)])
    right = lax.ppermute(v[..., :, :width], "rg", [(i + 1, i) for i in range(n_rg - 1)])
    return jnp.concatenate([left, v, right], axis=-1)


def apply_inner(padded, operators):
    east, west, south, north, diagonal = operators
    return (diagonal * padded[1:-1, 1:-1] - east * padded[1:-1, 2:] - west * padded[1:-1, :-2]
            - south * padded[2:, 1:-1] - north * padded[:-2, 1:-1])


def apply_padded(vector, operators):
    east, west, south, north, diagonal = operators
    padded = jnp.pad(vector, 1)
    return (diagonal * vector - east * padded[1:-1, 2:] - west * padded[1:-1, :-2]
            - south * padded[2:, 1:-1] - north * padded[:-2, 1:-1])


def multilook_kernel(bounds_ref, lead_ref, trail_ref, out_ref):
    shape = (lead_ref.shape[0], lead_ref.shape[2])
    line = lax.broadcasted_iota(jnp.int32, shape, 0)
    column = pl.program_id(0) * shape[1] + lax.broadcasted_iota(jnp.int32, shape, 1)
    mask = ((line >= bounds_ref[0]) & (line < bounds_ref[1]) & (column >= bounds_ref[2])
            & (column < bounds_ref[3])).astype(jnp.float32)
    first_re = lead_ref[:, 0, :].astype(jnp.float32) * mask
    first_im = lead_ref[:, 1, :].astype(jnp.float32) * mask
    second_re = trail_ref[:, 0, :].astype(jnp.float32) * mask
    second_im = trail_ref[:, 1, :].astype(jnp.float32) * mask
    products = (
        first_re * second_re + first_im * second_im,
        first_im * second_re - first_re * second_im,
        first_re * first_re + first_im * first_im,
        second_re * second_re + second_im * second_im,
    )
    chunks, span = out_ref.shape[2:]
    for part, values in enumerate(products):
        for group in range(out_ref.shape[1]):
            acc = values[group * LOOK:group * LOOK + 1, :]
            for offset in range(1, LOOK):
                acc = acc + values[group * LOOK + offset:group * LOOK + offset + 1, :]
            for chunk in range(chunks):
                out_ref[part, group, chunk:chunk + 1, :] = acc[:, chunk * span:(chunk + 1) * span]


def mean_multilook(leading, trailing, bounds):
    _, height_rows, width_cols = leading.shape
    block = 5120
    span = LOOK * 128
    rows = pl.pallas_call(
        multilook_kernel,
        grid=(width_cols // block,),
        in_specs=[
            pl.BlockSpec(memory_space=pltpu.SMEM),
            pl.BlockSpec((height_rows, 2, block), lambda j: (0, 0, j)),
            pl.BlockSpec((height_rows, 2, block), lambda j: (0, 0, j)),
        ],
        out_specs=pl.BlockSpec((4, height_rows // LOOK, block // span, span), lambda j: (0, 0, j, 0)),
        out_shape=jax.ShapeDtypeStruct((4, height_rows // LOOK, width_cols // span, span), jnp.float32),
    )(bounds, jnp.transpose(leading, (1, 0, 2)), jnp.transpose(trailing, (1, 0, 2)))
    grouped = rows
    cols = jnp.einsum("pikc,cd->pikd", grouped, group_sum(span, LOOK).T, precision=HIGHEST)
    return cols.reshape(4, height_rows // LOOK, width_cols // LOOK)


def edge_terms(left_re, left_im, left_weight, right_re, right_im, right_weight):
    edge_weight = 0.5 * (left_weight + right_weight)
    cross_im = right_im * left_re - right_re * left_im
    power_sum = (
        left_re * left_re + left_im * left_im + right_re * right_re + right_im * right_im + 1.0
    )
    return (edge_weight, 2.0 * cross_im / power_sum)


HIGHEST = lax.Precision.HIGHEST


def group_sum(n, size):
    group = lax.broadcasted_iota(jnp.int32, (n // size, n), 0)
    cell = lax.broadcasted_iota(jnp.int32, (n // size, n), 1)
    return (cell // size == group).astype(jnp.float32)


def pick(n, offset):
    group = lax.broadcasted_iota(jnp.int32, (n // 2, n), 0)
    cell = lax.broadcasted_iota(jnp.int32, (n // 2, n), 1)
    return (cell == 2 * group + offset).astype(jnp.float32)


def sandwich(left, vector, right):
    inner = jnp.dot(left, vector, precision=HIGHEST)
    return jnp.dot(inner, right, precision=HIGHEST)


def restrict_sum(vector):
    rows_now, cols_now = vector.shape
    return sandwich(group_sum(rows_now, 2), vector, group_sum(cols_now, 2).T)


def prolong_copy(vector):
    rows_now, cols_now = vector.shape
    return sandwich(group_sum(2 * rows_now, 2).T, vector, group_sum(2 * cols_now, 2))


def coarsen(east, west, south, north):
    rows_now, cols_now = east.shape
    row_sum = group_sum(rows_now, 2)
    col_sum = group_sum(cols_now, 2).T
    return (
        sandwich(row_sum, east, pick(cols_now, 1).T),
        sandwich(row_sum, west, pick(cols_now, 0).T),
        sandwich(pick(rows_now, 1), south, col_sum),
        sandwich(pick(rows_now, 0), north, col_sum),
    )


def build_levels(east, west, south, north, first_level, last_level):
    levels = {}
    for level in range(first_level, last_level):
        diagonal = east + west + south + north + MU * 4.0**level
        levels[level] = (east, west, south, north, diagonal)
        if level + 1 < LEVELS:
            east, west, south, north = coarsen(east, west, south, north)
    return levels, (east, west, south, north)


def jacobi_sweeps(rhs_vec, operators, apply_fn):
    estimate = OMEGA * rhs_vec / operators[4]
    for sweep_index in range(SWEEPS - 1):
        estimate = estimate + OMEGA * (rhs_vec - apply_fn(estimate, operators)) / operators[4]
    return estimate


def vcycle(rhs_vec, level, levels, apply_fn, stop_fn):
    if level == LEVELS - 1:
        return jacobi_sweeps(rhs_vec, levels[level], apply_fn)
    if stop_fn is not None and level == GATHER_LEVEL:
        return stop_fn(rhs_vec)
    diagonal = levels[level][4]
    estimate = OMEGA * rhs_vec / diagonal
    remain = rhs_vec - apply_fn(estimate, levels[level])
    correction = vcycle(restrict_sum(remain), level + 1, levels, apply_fn, stop_fn)
    estimate = estimate + prolong_copy(correction)
    return estimate + OMEGA * (rhs_vec - apply_fn(estimate, levels[level])) / diagonal


def everyone():
    return lax.axis_size("az") * lax.axis_size("rg")


def gather_strip(blocks, sums=None):
    n_az = lax.axis_size("az")
    n_rg = lax.axis_size("rg")
    count, h, w = blocks.shape
    if sums is not None:
        extra = jnp.zeros((1, h, w), jnp.float32).at[0, 0, :sums.shape[0]].set(sums)
        blocks = jnp.concatenate([blocks, extra])
    sent = jnp.broadcast_to(blocks[None], (n_az,) + blocks.shape)
    got = lax.all_to_all(sent, "az", 0, 0, tiled=True)
    summed = None
    if sums is not None:
        column_sums = jnp.sum(got[:, count, 0, :sums.shape[0]], axis=0)
        rows = lax.all_to_all(jnp.broadcast_to(column_sums[None], (n_rg, sums.shape[0])), "rg", 0, 0, tiled=True)
        summed = jnp.sum(rows, axis=0)
        got = got[:, :count]
    column = got.transpose(1, 0, 2, 3).reshape(count, n_az * h, w)
    left = lax.ppermute(column, "rg", [(i, i + 1) for i in range(n_rg - 1)])
    right = lax.ppermute(column, "rg", [(i + 1, i) for i in range(n_rg - 1)])
    return jnp.concatenate([left, column, right], axis=-1), summed


def shifted(values, axis):
    pad = [(0, 0)] * values.ndim
    pad[axis] = (1, 0)
    return lax.slice_in_dim(jnp.pad(values, pad), 0, values.shape[axis], axis=axis)


def total(values):
    n = everyone()
    sent = jnp.broadcast_to(values[None], (n, values.shape[0]))
    got = lax.all_to_all(sent, ("az", "rg"), 0, 0, tiled=True)
    return jnp.sum(got, axis=0)


def local(master_phasor_raster, slave_phasor_raster, segment_track_trim, segment_slant_trim):
    n_az = lax.axis_size("az")
    n_range = lax.axis_size("rg")
    segment_ordinal = lax.axis_index("az")
    range_index = lax.axis_index("rg")
    track_trim_width = lax.dynamic_index_in_dim(
        segment_track_trim, segment_ordinal, 0, keepdims=False
    )
    slant_trim_width = lax.dynamic_index_in_dim(
        segment_slant_trim, segment_ordinal, 0, keepdims=False
    )
    lines_here = master_phasor_raster.shape[1]
    slant_sample_total = master_phasor_raster.shape[2]
    first_line = range_index * lines_here
    bounds = jnp.stack([
        track_trim_width[0] - first_line,
        SEGMENT_HEIGHT - track_trim_width[1] - first_line,
        slant_trim_width[0],
        slant_sample_total - slant_trim_width[1],
    ]).astype(jnp.int32)
    pixel_totals = mean_multilook(master_phasor_raster, slave_phasor_raster, bounds)
    look_re, look_im, power_one, power_two = (
        pixel_totals[0],
        pixel_totals[1],
        pixel_totals[2],
        pixel_totals[3],
    )
    weight = 0.05 + 4.0 * (look_re * look_re + look_im * look_im) / jnp.maximum(
        power_one * power_two, 1.0
    )
    widest = 2 * ITERS
    border = widest + 1
    fields = jnp.stack([look_re, look_im, weight])
    n_fields, rows_here, cols_all = fields.shape
    cols_here = cols_all // n_range
    main = fields.reshape(n_fields, rows_here, n_range, cols_here).transpose(2, 0, 1, 3)
    zero = jnp.zeros((1, n_fields, rows_here, border), jnp.float32)
    before = jnp.concatenate([zero, main[:-1, :, :, -border:]], axis=0)
    after = jnp.concatenate([main[1:, :, :, :border], zero], axis=0)
    fields = jnp.concatenate([before, main, after], axis=-1)
    fields = lax.all_to_all(fields, "rg", 0, 0, tiled=True)
    fields = fields.transpose(1, 0, 2, 3).reshape(n_fields, n_range * rows_here, cols_here + 2 * border)
    shard_height_total = n_range * rows_here
    above = lax.ppermute(fields[:, -border:, :], "az", [(i, i + 1) for i in range(n_az - 1)])
    below = lax.ppermute(fields[:, :border, :], "az", [(i + 1, i) for i in range(n_az - 1)])
    fields = jnp.concatenate([above, fields, below], axis=1)
    weight = fields[2, border:-border, border:-border]

    row_global = segment_ordinal * shard_height_total - border + jnp.arange(
        shard_height_total + 2 * border, dtype=jnp.int32)
    col_global = range_index * cols_here - border + jnp.arange(cols_here + 2 * border, dtype=jnp.int32)
    edge_h, grad_h = edge_terms(fields[0, :, :-1], fields[1, :, :-1], fields[2, :, :-1],
                                fields[0, :, 1:], fields[1, :, 1:], fields[2, :, 1:])
    keep_h = ((col_global[:-1] >= 0) & (col_global[:-1] <= cols_here * n_range - 2)).astype(jnp.float32)
    edge_h = edge_h * keep_h[None, :]
    edge_v, grad_v = edge_terms(fields[0, :-1], fields[1, :-1], fields[2, :-1],
                                fields[0, 1:], fields[1, 1:], fields[2, 1:])
    keep_v = ((row_global[:-1] >= 0) & (row_global[:-1] <= shard_height_total * n_az - 2)).astype(jnp.float32)
    edge_v = edge_v * keep_v[:, None]
    flux_h = edge_h * grad_h
    flux_v = edge_v * grad_v
    east_w = edge_h[1:-1, 1:]
    west_w = edge_h[1:-1, :-1]
    south_w = edge_v[1:, 1:-1]
    north_w = edge_v[:-1, 1:-1]
    diag_w = east_w + west_w + south_w + north_w + MU * 4.0**0
    ops_w = (east_w, west_w, south_w, north_w, diag_w)
    rhs_wide = -(flux_h[1:-1, 1:] - flux_h[1:-1, :-1] + flux_v[1:, 1:-1] - flux_v[:-1, 1:-1])

    def crop(values, ring):
        cut = (values.shape[-2] - shard_height_total) // 2 - ring
        if cut == 0:
            return values
        return values[..., cut:-cut, cut:-cut]

    def ops_at(ring):
        return tuple(crop(x, ring) for x in ops_w)

    levels, coarse_edges = build_levels(*ops_at(0)[:4], first_level=0, last_level=GATHER_LEVEL)
    block_h, block_w = coarse_edges[0].shape
    whole = {}

    def coarse_solve(rhs_vec, ring, sums):
        if not whole:
            got, summed = gather_strip(jnp.stack([coarse_edges[0], coarse_edges[2], rhs_vec]), sums)
            east_s, south_s = got[0], got[1]
            whole["levels"] = build_levels(east_s, shifted(east_s, 1), south_s, shifted(south_s, 0),
                                           GATHER_LEVEL, LEVELS)[0]
            strip_rhs = got[2]
        else:
            got, summed = gather_strip(rhs_vec[None], sums)
            strip_rhs = got[0]
        strip_x = vcycle(strip_rhs, GATHER_LEVEL, whole["levels"], apply_padded, None)
        coarse_ring = ring // 2
        strip_x = jnp.pad(strip_x, ((coarse_ring, coarse_ring), (0, 0)))
        return lax.dynamic_slice(strip_x, (segment_ordinal * block_h, block_w - coarse_ring),
                                 (block_h + 2 * coarse_ring, block_w + 2 * coarse_ring)), summed

    def precondition(rhs_wide, sums=None):
        ring = (rhs_wide.shape[0] - shard_height_total) // 2
        diag_here = ops_at(ring)[4]
        estimate = OMEGA * rhs_wide / diag_here
        remain = crop(rhs_wide, 0) - apply_inner(crop(estimate, 1), levels[0])
        patch, summed = coarse_solve(restrict_sum(remain), ring, sums)
        estimate = estimate + prolong_copy(patch)
        inner = ops_at(ring - 1)
        smoothed = crop(estimate, ring - 1) + OMEGA * (crop(rhs_wide, ring - 1) - apply_inner(estimate, inner)) / inner[4]
        return smoothed, apply_inner(smoothed, ops_at(ring - 2)), summed

    def ring_of(values):
        return (values.shape[-2] - shard_height_total) // 2

    def own_sums(*pairs):
        return jnp.stack([jnp.sum(crop(a, 0) * crop(b, 0)) for a, b in pairs])

    residual_wide = rhs_wide
    precond, image_u, _ = precondition(residual_wide)
    sums = own_sums((residual_wide, precond), (image_u, precond))
    if ITERS > 1:
        pre_image, image_pre, sums = precondition(image_u, sums)
    else:
        sums = total(sums)
    norm_now = sums[0]
    curvature = sums[1]
    step_length = norm_now / curvature
    direction, image_vec = precond, image_u
    if ITERS > 1:
        pre_dir, image_pre_dir = pre_image, image_pre
    solution = step_length * crop(direction, 0)
    for step_index in range(1, ITERS):
        residual_wide = crop(residual_wide, ring_of(image_vec)) - step_length * image_vec
        precond = crop(precond, ring_of(pre_dir)) - step_length * pre_dir
        image_u = crop(image_u, ring_of(image_pre_dir)) - step_length * image_pre_dir
        sums = own_sums((residual_wide, precond), (image_u, precond), (precond, image_vec))
        if step_index + 1 < ITERS:
            pre_image, image_pre, sums = precondition(image_u, sums)
        else:
            sums = total(sums)
        norm_next = sums[0]
        ratio = norm_next / norm_now
        curvature = sums[1] + 2.0 * ratio * sums[2] + ratio * ratio * curvature
        step_length = norm_next / curvature
        direction = precond + ratio * crop(direction, ring_of(precond))
        image_vec = image_u + ratio * crop(image_vec, ring_of(image_u))
        if step_index + 1 < ITERS:
            pre_dir = pre_image + ratio * crop(pre_dir, ring_of(pre_image))
            image_pre_dir = image_pre + ratio * crop(image_pre_dir, ring_of(image_pre))
        solution = solution + step_length * crop(direction, 0)
        norm_now = norm_next
    return (solution, weight)


def solution(mesh):
    return jax.shard_map(
        local,
        mesh=mesh,
        in_specs=(P(None, ("az", "rg"), None), P(None, ("az", "rg"), None), P(), P()),
        out_specs=(P("az", "rg"), P("az", "rg")),
        check_vma=False,
    )
```

```python
import jax
import jax.numpy as jnp
from jax import lax
from jax.sharding import PartitionSpec as P
from jax.experimental import pallas as pl
from jax.experimental.pallas import tpu as pltpu

LOOK = 5
LEVELS = 6
ITERS = 3
SWEEPS = 4
SEGMENT_HEIGHT = 160
GATHER_LEVEL = 1


OMEGA = 0.6
MU = 0.01


def neighbours(v):
    n_az = lax.axis_size("az")
    n_rg = lax.axis_size("rg")
    above = lax.ppermute(v[..., -1:, :], "az", [(i, i + 1) for i in range(n_az - 1)])
    below = lax.ppermute(v[..., :1, :], "az", [(i + 1, i) for i in range(n_az - 1)])
    left = lax.ppermute(v[..., :, -1:], "rg", [(i, i + 1) for i in range(n_rg - 1)])
    right = lax.ppermute(v[..., :, :1], "rg", [(i + 1, i) for i in range(n_rg - 1)])
    north = jnp.concatenate([above, v[..., :-1, :]], axis=-2)
    south = jnp.concatenate([v[..., 1:, :], below], axis=-2)
    west = jnp.concatenate([left, v[..., :, :-1]], axis=-1)
    east = jnp.concatenate([v[..., :, 1:], right], axis=-1)
    return north, south, west, east


def apply_halo(vector, operators):
    east, west, south, north, diagonal = operators
    v_n, v_s, v_w, v_e = neighbours(vector)
    return diagonal * vector - east * v_e - west * v_w - south * v_s - north * v_n


def extended(v, width):
    n_az = lax.axis_size("az")
    n_rg = lax.axis_size("rg")
    above = lax.ppermute(v[..., -width:, :], "az", [(i, i + 1) for i in range(n_az - 1)])
    below = lax.ppermute(v[..., :width, :], "az", [(i + 1, i) for i in range(n_az - 1)])
    v = jnp.concatenate([above, v, below], axis=-2)
    left = lax.ppermute(v[..., :, -width:], "rg", [(i, i + 1) for i in range(n_rg - 1)])
    right = lax.ppermute(v[..., :, :width], "rg", [(i + 1, i) for i in range(n_rg - 1)])
    return jnp.concatenate([left, v, right], axis=-1)


def apply_inner(padded, operators):
    east, west, south, north, diagonal = operators
    return (diagonal * padded[1:-1, 1:-1] - east * padded[1:-1, 2:] - west * padded[1:-1, :-2]
            - south * padded[2:, 1:-1] - north * padded[:-2, 1:-1])


def apply_padded(vector, operators):
    east, west, south, north, diagonal = operators
    padded = jnp.pad(vector, 1)
    return (diagonal * vector - east * padded[1:-1, 2:] - west * padded[1:-1, :-2]
            - south * padded[2:, 1:-1] - north * padded[:-2, 1:-1])


def multilook_kernel(track_ref, slant_ref, lead_ref, trail_ref, out_ref):
    shape = (lead_ref.shape[0], lead_ref.shape[2])
    burst = lax.axis_index("az")
    first_line = lax.axis_index("rg") * shape[0]
    line = first_line + lax.broadcasted_iota(jnp.int32, shape, 0)
    column = pl.program_id(0) * shape[1] + lax.broadcasted_iota(jnp.int32, shape, 1)
    mask = ((line >= track_ref[burst, 0]) & (line < SEGMENT_HEIGHT - track_ref[burst, 1])
            & (column >= slant_ref[burst, 0])
            & (column < pl.num_programs(0) * shape[1] - slant_ref[burst, 1])).astype(jnp.float32)
    first_re = lead_ref[:, 0, :].astype(jnp.float32) * mask
    first_im = lead_ref[:, 1, :].astype(jnp.float32) * mask
    second_re = trail_ref[:, 0, :].astype(jnp.float32) * mask
    second_im = trail_ref[:, 1, :].astype(jnp.float32) * mask
    products = (
        first_re * second_re + first_im * second_im,
        first_im * second_re - first_re * second_im,
        first_re * first_re + first_im * first_im,
        second_re * second_re + second_im * second_im,
    )
    chunks, span = out_ref.shape[2:]
    for part, values in enumerate(products):
        for group in range(out_ref.shape[1]):
            acc = values[group * LOOK:group * LOOK + 1, :]
            for offset in range(1, LOOK):
                acc = acc + values[group * LOOK + offset:group * LOOK + offset + 1, :]
            for chunk in range(chunks):
                out_ref[part, group, chunk:chunk + 1, :] = acc[:, chunk * span:(chunk + 1) * span]


def mean_multilook(leading, trailing, track_trim, slant_trim):
    _, height_rows, width_cols = leading.shape
    block = 5120
    span = LOOK * 128
    rows = pl.pallas_call(
        multilook_kernel,
        grid=(width_cols // block,),
        in_specs=[
            pl.BlockSpec(memory_space=pltpu.SMEM),
            pl.BlockSpec(memory_space=pltpu.SMEM),
            pl.BlockSpec((height_rows, 2, block), lambda j: (0, 0, j)),
            pl.BlockSpec((height_rows, 2, block), lambda j: (0, 0, j)),
        ],
        out_specs=pl.BlockSpec((4, height_rows // LOOK, block // span, span), lambda j: (0, 0, j, 0)),
        out_shape=jax.ShapeDtypeStruct((4, height_rows // LOOK, width_cols // span, span), jnp.float32),
    )(track_trim, slant_trim, jnp.transpose(leading, (1, 0, 2)), jnp.transpose(trailing, (1, 0, 2)))
    grouped = rows
    cols = jnp.einsum("pikc,cd->pikd", grouped, group_sum(span, LOOK).T, precision=HIGHEST)
    return cols.reshape(4, height_rows // LOOK, width_cols // LOOK)


def edge_terms(left_re, left_im, left_weight, right_re, right_im, right_weight):
    edge_weight = 0.5 * (left_weight + right_weight)
    cross_im = right_im * left_re - right_re * left_im
    power_sum = (
        left_re * left_re + left_im * left_im + right_re * right_re + right_im * right_im + 1.0
    )
    return (edge_weight, 2.0 * cross_im / power_sum)


HIGHEST = lax.Precision.HIGHEST


def group_sum(n, size):
    group = lax.broadcasted_iota(jnp.int32, (n // size, n), 0)
    cell = lax.broadcasted_iota(jnp.int32, (n // size, n), 1)
    return (cell // size == group).astype(jnp.float32)


def pick(n, offset):
    group = lax.broadcasted_iota(jnp.int32, (n // 2, n), 0)
    cell = lax.broadcasted_iota(jnp.int32, (n // 2, n), 1)
    return (cell == 2 * group + offset).astype(jnp.float32)


def sandwich(left, vector, right):
    inner = jnp.dot(left, vector, precision=HIGHEST)
    return jnp.dot(inner, right, precision=HIGHEST)


def restrict_sum(vector):
    rows_now, cols_now = vector.shape
    return sandwich(group_sum(rows_now, 2), vector, group_sum(cols_now, 2).T)


def prolong_copy(vector):
    rows_now, cols_now = vector.shape
    return sandwich(group_sum(2 * rows_now, 2).T, vector, group_sum(2 * cols_now, 2))


def coarsen(east, west, south, north):
    rows_now, cols_now = east.shape
    row_sum = group_sum(rows_now, 2)
    col_sum = group_sum(cols_now, 2).T
    return (
        sandwich(row_sum, east, pick(cols_now, 1).T),
        sandwich(row_sum, west, pick(cols_now, 0).T),
        sandwich(pick(rows_now, 1), south, col_sum),
        sandwich(pick(rows_now, 0), north, col_sum),
    )


def build_levels(east, west, south, north, first_level, last_level):
    levels = {}
    for level in range(first_level, last_level):
        diagonal = east + west + south + north + MU * 4.0**level
        levels[level] = (east, west, south, north, diagonal)
        if level + 1 < LEVELS:
            east, west, south, north = coarsen(east, west, south, north)
    return levels, (east, west, south, north)


def jacobi_sweeps(rhs_vec, operators, apply_fn):
    estimate = OMEGA * rhs_vec / operators[4]
    for sweep_index in range(SWEEPS - 1):
        estimate = estimate + OMEGA * (rhs_vec - apply_fn(estimate, operators)) / operators[4]
    return estimate


def vcycle(rhs_vec, level, levels, apply_fn, stop_fn):
    if level == LEVELS - 1:
        return jacobi_sweeps(rhs_vec, levels[level], apply_fn)
    if stop_fn is not None and level == GATHER_LEVEL:
        return stop_fn(rhs_vec)
    diagonal = levels[level][4]
    estimate = OMEGA * rhs_vec / diagonal
    remain = rhs_vec - apply_fn(estimate, levels[level])
    correction = vcycle(restrict_sum(remain), level + 1, levels, apply_fn, stop_fn)
    estimate = estimate + prolong_copy(correction)
    return estimate + OMEGA * (rhs_vec - apply_fn(estimate, levels[level])) / diagonal


def everyone():
    return lax.axis_size("az") * lax.axis_size("rg")


def gather_strip(blocks, sums=None):
    n_az = lax.axis_size("az")
    n_rg = lax.axis_size("rg")
    count, h, w = blocks.shape
    if sums is not None:
        extra = jnp.zeros((1, h, w), jnp.float32).at[0, 0, :sums.shape[0]].set(sums)
        blocks = jnp.concatenate([blocks, extra])
    sent = jnp.broadcast_to(blocks[None], (n_az,) + blocks.shape)
    got = lax.all_to_all(sent, "az", 0, 0, tiled=True)
    summed = None
    if sums is not None:
        column_sums = jnp.sum(got[:, count, 0, :sums.shape[0]], axis=0)
        rows = lax.all_to_all(jnp.broadcast_to(column_sums[None], (n_rg, sums.shape[0])), "rg", 0, 0, tiled=True)
        summed = jnp.sum(rows, axis=0)
        got = got[:, :count]
    column = got.transpose(1, 0, 2, 3).reshape(count, n_az * h, w)
    left = lax.ppermute(column, "rg", [(i, i + 1) for i in range(n_rg - 1)])
    right = lax.ppermute(column, "rg", [(i + 1, i) for i in range(n_rg - 1)])
    return jnp.concatenate([left, column, right], axis=-1), summed


def shifted(values, axis):
    pad = [(0, 0)] * values.ndim
    pad[axis] = (1, 0)
    return lax.slice_in_dim(jnp.pad(values, pad), 0, values.shape[axis], axis=axis)


def total(values):
    n = everyone()
    sent = jnp.broadcast_to(values[None], (n, values.shape[0]))
    got = lax.all_to_all(sent, ("az", "rg"), 0, 0, tiled=True)
    return jnp.sum(got, axis=0)


def local(master_phasor_raster, slave_phasor_raster, segment_track_trim, segment_slant_trim):
    n_az = lax.axis_size("az")
    n_range = lax.axis_size("rg")
    segment_ordinal = lax.axis_index("az")
    range_index = lax.axis_index("rg")
    track_trim_width = lax.dynamic_index_in_dim(
        segment_track_trim, segment_ordinal, 0, keepdims=False
    )
    slant_trim_width = lax.dynamic_index_in_dim(
        segment_slant_trim, segment_ordinal, 0, keepdims=False
    )
    lines_here = master_phasor_raster.shape[1]
    slant_sample_total = master_phasor_raster.shape[2]
    pixel_totals = mean_multilook(master_phasor_raster, slave_phasor_raster, segment_track_trim, segment_slant_trim)
    look_re, look_im, power_one, power_two = (
        pixel_totals[0],
        pixel_totals[1],
        pixel_totals[2],
        pixel_totals[3],
    )
    weight = 0.05 + 4.0 * (look_re * look_re + look_im * look_im) / jnp.maximum(
        power_one * power_two, 1.0
    )
    widest = 2 * ITERS
    border = widest + 1
    fields = jnp.stack([look_re, look_im, weight])
    n_fields, rows_here, cols_all = fields.shape
    cols_here = cols_all // n_range
    main = fields.reshape(n_fields, rows_here, n_range, cols_here).transpose(2, 0, 1, 3)
    zero = jnp.zeros((1, n_fields, rows_here, border), jnp.float32)
    before = jnp.concatenate([zero, main[:-1, :, :, -border:]], axis=0)
    after = jnp.concatenate([main[1:, :, :, :border], zero], axis=0)
    fields = jnp.concatenate([before, main, after], axis=-1)
    fields = lax.all_to_all(fields, "rg", 0, 0, tiled=True)
    fields = fields.transpose(1, 0, 2, 3).reshape(n_fields, n_range * rows_here, cols_here + 2 * border)
    shard_height_total = n_range * rows_here
    above = lax.ppermute(fields[:, -border:, :], "az", [(i, i + 1) for i in range(n_az - 1)])
    below = lax.ppermute(fields[:, :border, :], "az", [(i + 1, i) for i in range(n_az - 1)])
    fields = jnp.concatenate([above, fields, below], axis=1)
    weight = fields[2, border:-border, border:-border]

    row_global = segment_ordinal * shard_height_total - border + jnp.arange(
        shard_height_total + 2 * border, dtype=jnp.int32)
    col_global = range_index * cols_here - border + jnp.arange(cols_here + 2 * border, dtype=jnp.int32)
    edge_h, grad_h = edge_terms(fields[0, :, :-1], fields[1, :, :-1], fields[2, :, :-1],
                                fields[0, :, 1:], fields[1, :, 1:], fields[2, :, 1:])
    keep_h = ((col_global[:-1] >= 0) & (col_global[:-1] <= cols_here * n_range - 2)).astype(jnp.float32)
    edge_h = edge_h * keep_h[None, :]
    edge_v, grad_v = edge_terms(fields[0, :-1], fields[1, :-1], fields[2, :-1],
                                fields[0, 1:], fields[1, 1:], fields[2, 1:])
    keep_v = ((row_global[:-1] >= 0) & (row_global[:-1] <= shard_height_total * n_az - 2)).astype(jnp.float32)
    edge_v = edge_v * keep_v[:, None]
    flux_h = edge_h * grad_h
    flux_v = edge_v * grad_v
    east_w = edge_h[1:-1, 1:]
    west_w = edge_h[1:-1, :-1]
    south_w = edge_v[1:, 1:-1]
    north_w = edge_v[:-1, 1:-1]
    diag_w = east_w + west_w + south_w + north_w + MU * 4.0**0
    ops_w = (east_w, west_w, south_w, north_w, diag_w)
    rhs_wide = -(flux_h[1:-1, 1:] - flux_h[1:-1, :-1] + flux_v[1:, 1:-1] - flux_v[:-1, 1:-1])

    def crop(values, ring):
        cut = (values.shape[-2] - shard_height_total) // 2 - ring
        if cut == 0:
            return values
        return values[..., cut:-cut, cut:-cut]

    def ops_at(ring):
        return tuple(crop(x, ring) for x in ops_w)

    levels, coarse_edges = build_levels(*ops_at(0)[:4], first_level=0, last_level=GATHER_LEVEL)
    block_h, block_w = coarse_edges[0].shape
    whole = {}

    def coarse_solve(rhs_vec, ring, sums):
        if not whole:
            got, summed = gather_strip(jnp.stack([coarse_edges[0], coarse_edges[2], rhs_vec]), sums)
            east_s, south_s = got[0], got[1]
            whole["levels"] = build_levels(east_s, shifted(east_s, 1), south_s, shifted(south_s, 0),
                                           GATHER_LEVEL, LEVELS)[0]
            strip_rhs = got[2]
        else:
            got, summed = gather_strip(rhs_vec[None], sums)
            strip_rhs = got[0]
        strip_x = vcycle(strip_rhs, GATHER_LEVEL, whole["levels"], apply_padded, None)
        coarse_ring = ring // 2
        strip_x = jnp.pad(strip_x, ((coarse_ring, coarse_ring), (0, 0)))
        return lax.dynamic_slice(strip_x, (segment_ordinal * block_h, block_w - coarse_ring),
                                 (block_h + 2 * coarse_ring, block_w + 2 * coarse_ring)), summed

    def precondition(rhs_wide, sums=None):
        ring = (rhs_wide.shape[0] - shard_height_total) // 2
        diag_here = ops_at(ring)[4]
        estimate = OMEGA * rhs_wide / diag_here
        remain = crop(rhs_wide, 0) - apply_inner(crop(estimate, 1), levels[0])
        patch, summed = coarse_solve(restrict_sum(remain), ring, sums)
        estimate = estimate + prolong_copy(patch)
        inner = ops_at(ring - 1)
        smoothed = crop(estimate, ring - 1) + OMEGA * (crop(rhs_wide, ring - 1) - apply_inner(estimate, inner)) / inner[4]
        return smoothed, apply_inner(smoothed, ops_at(ring - 2)), summed

    def ring_of(values):
        return (values.shape[-2] - shard_height_total) // 2

    def own_sums(*pairs):
        return jnp.stack([jnp.sum(crop(a, 0) * crop(b, 0)) for a, b in pairs])

    residual_wide = rhs_wide
    precond, image_u, _ = precondition(residual_wide)
    sums = own_sums((residual_wide, precond), (image_u, precond))
    if ITERS > 1:
        pre_image, image_pre, sums = precondition(image_u, sums)
    else:
        sums = total(sums)
    norm_now = sums[0]
    curvature = sums[1]
    step_length = norm_now / curvature
    direction, image_vec = precond, image_u
    if ITERS > 1:
        pre_dir, image_pre_dir = pre_image, image_pre
    solution = step_length * crop(direction, 0)
    for step_index in range(1, ITERS):
        residual_wide = crop(residual_wide, ring_of(image_vec)) - step_length * image_vec
        precond = crop(precond, ring_of(pre_dir)) - step_length * pre_dir
        image_u = crop(image_u, ring_of(image_pre_dir)) - step_length * image_pre_dir
        sums = own_sums((residual_wide, precond), (image_u, precond), (precond, image_vec))
        if step_index + 1 < ITERS:
            pre_image, image_pre, sums = precondition(image_u, sums)
        else:
            sums = total(sums)
        norm_next = sums[0]
        ratio = norm_next / norm_now
        curvature = sums[1] + 2.0 * ratio * sums[2] + ratio * ratio * curvature
        step_length = norm_next / curvature
        direction = precond + ratio * crop(direction, ring_of(precond))
        image_vec = image_u + ratio * crop(image_vec, ring_of(image_u))
        if step_index + 1 < ITERS:
            pre_dir = pre_image + ratio * crop(pre_dir, ring_of(pre_image))
            image_pre_dir = image_pre + ratio * crop(image_pre_dir, ring_of(image_pre))
        solution = solution + step_length * crop(direction, 0)
        norm_now = norm_next
    return (solution, weight)


def solution(mesh):
    return jax.shard_map(
        local,
        mesh=mesh,
        in_specs=(P(None, ("az", "rg"), None), P(None, ("az", "rg"), None), P(), P()),
        out_specs=(P("az", "rg"), P("az", "rg")),
        check_vma=False,
    )
```
